256 devices in a mesh: row: 8 (over z), gx: 2 (over y_hi), gy: 16 (over y_lo, x, core).
Axes of the slice: x: 4, y: 4 (y_hi: 2, y_lo: 2; y = y_hi * 2 + y_lo), z: 8, core: 2. Of those that a mesh axis runs over, the one named last changes fastest.
Arguments:
- flow_pops: float32 [19, 64, 48, 256], P(None, 'gy', 'row', 'gx'), may hold values from 0 to 0.5, as said below
- concentration: float32 [64, 64, 48, 256], P('row', 'gy', None, 'gx'), may hold values from 0.2 to 2
- solid_mask: int32 [64, 48, 256], P('gy', None, 'gx'), may hold values from 0 to 1
- source_cell: int32 [96], replicated, may hold values from 0 to 786431
- source_scalar: int32 [96], replicated, may hold values from 0 to 63
- source_rate: float32 [96], replicated, may hold values from 0.5 to 2
Outputs:
- final_flow: float32 [19, 64, 48, 256], P(None, 'gy', 'row', 'gx')
- final_concentration: float32 [64, 64, 48, 256], P('row', 'gy', None, 'gx')
The draws below stay inside these ranges and needn't reach their ends.
Inputs may be any that keep to these rules, and one draw needn't show every extreme that they name: `flow_pops`: populations are positive, near the equilibrium of a light wind.
All inputs are finite; a program needn't handle non-finite values.
Results may differ from the reference program's by a relative error of at most 0.0003.
Values sent between devices are 32-bit elements; how exact they have to be, the bound alone decides.
No kernel may reach another device: no remote copies, remote signals or barrier semaphores. Data moves between devices by JAX's collectives and lax.ppermute only.
A program may use at most 64 MiB of HBM per device.

```python
import math
import jax
import jax.numpy as jnp
from jax import lax

NZ = 48
SC_ROW = 8
SOURCES = 96
STEPS = 3
NX = 256
NY = 64
SCALARS = 64
N_ROW = 8


def draw_flow_pops(key, part):
    weights = jnp.array([1.0 / 3.0] + [1.0 / 18.0] * 6 + [1.0 / 36.0] * 12, jnp.float32)
    along = jnp.array([0, 1, -1, 0, 0, 0, 0, 1, -1, 1, -1, 1, -1, 1, -1, 0, 0, 0, 0], jnp.float32) * 0.08
    far_state = weights * (1.0 + 3.0 * along + 4.5 * along * along - 1.5 * 0.0064)
    base_state = far_state.reshape(19, 1, 1, 1)
    rough = jax.random.normal(jax.random.fold_in(key, 3), (19, NY, NZ, NX), jnp.float32)
    return base_state * (1.0 + 0.05 * jnp.clip(rough, -2.5, 2.5))


def draw_solid_mask(key, part):
    heights = jax.random.randint(key, (NY // 8 + 1, NX // 16 + 1), 0, NZ // 2 + 1)
    across = lax.broadcasted_iota(jnp.int32, (NY, NZ, NX), 0)
    upward = lax.broadcasted_iota(jnp.int32, (NY, NZ, NX), 1)
    along_wind = lax.broadcasted_iota(jnp.int32, (NY, NZ, NX), 2)
    height_here = heights[across // 8, along_wind // 16]
    footprint = (across % 8 >= 2) & (across % 8 < 6) & (along_wind % 16 >= 4) & (along_wind % 16 < 12)
    return jnp.where(footprint & (upward < height_here), 1, 0).astype(jnp.int32)


def plant(values, key, low, top_value):
    spot = [jax.random.randint(jax.random.fold_in(key, axis), (), 0, length) for axis, length in enumerate(values.shape)]
    main_axis = values.shape.index(max(values.shape))
    next_to = spot[:main_axis] + [(spot[main_axis] + 1) % values.shape[main_axis]] + spot[main_axis + 1:]
    return values.at[tuple(spot)].set(low).at[tuple(next_to)].set(top_value)


def steps_of(key, extent, split, low, largest):
    def one(axis_at, shards_of):
        steps = jax.random.uniform(jax.random.fold_in(jax.random.fold_in(key, 6), axis_at), (shards_of,), jnp.float32, low / len(split), largest / len(split))
        return jnp.repeat(jnp.exp(steps), extent[axis_at] // shards_of).reshape((-1,) + (1,) * (len(extent) - axis_at - 1))

    factor_of = one(*split[0])
    for cut in split[1:]:
        factor_of = factor_of * one(*cut)
    return factor_of


def setup_inputs(seed: int = 0) -> dict:
    splits = jax.random.split(jax.random.key(seed), 7)
    return {
        "flow_pops": draw_flow_pops(jax.random.fold_in(splits[6], 71), 0),
        "concentration": jnp.clip(jnp.exp(math.log(2.0) - 2.3025851 * jax.random.uniform(splits[1], (SCALARS, NY, NZ, NX), jnp.float32) ** steps_of(splits[1], (SCALARS, NY, NZ, NX), ((0, 8), (1, 16), (3, 2)), -0.2, 0.2)), 0.2, 2.0),
        "solid_mask": draw_solid_mask(jax.random.fold_in(splits[6], 71), 0),
        "source_cell": plant(jax.random.randint(splits[3], (SOURCES,), 0, NY * NZ * NX), jax.random.fold_in(splits[3], 1), 0, (NY * NZ * NX) - 1).astype(jnp.int32),
        "source_scalar": plant(jax.random.randint(splits[4], (SOURCES,), 0, SCALARS), jax.random.fold_in(splits[4], 1), 0, SCALARS - 1).astype(jnp.int32),
        "source_rate": jnp.clip(jnp.exp(jax.random.uniform(splits[5], (SOURCES,), jnp.float32, math.log(0.5), math.log(2.0))), 0.5, 2.0),
    }


flow_vectors = ((0, 0, 0), (1, 0, 0), (-1, 0, 0), (0, 1, 0), (0, -1, 0), (0, 0, 1), (0, 0, -1), (1, 1, 0), (-1, -1, 0), (1, -1, 0), (-1, 1, 0), (1, 0, 1), (-1, 0, -1), (1, 0, -1), (-1, 0, 1), (0, 1, 1), (0, -1, -1), (0, 1, -1), (0, -1, 1))
flow_weights = (1.0 / 3.0,) + (1.0 / 18.0,) * 6 + (1.0 / 36.0,) * 12
flow_mirror = (0, 2, 1, 4, 3, 6, 5, 8, 7, 10, 9, 12, 11, 14, 13, 16, 15, 18, 17)
scalar_weights = (0.25,) + (0.125,) * 6
tau_base = 0.52
smag_const = 0.17
tau_scalar_base = 0.55
schmidt_turb = 0.7
inflow_speed = 0.08

def far_field(member):
    along = flow_vectors[member][0] * inflow_speed
    return flow_weights[member] * (1.0 + 3.0 * along + 4.5 * along * along - 1.5 * inflow_speed * inflow_speed)

def flow_collide(populations, solid):
    density = populations[0]
    for member in range(1, 19):
        density = density + populations[member]
    speeds = []
    for component in range(3):
        moment = jnp.zeros_like(density)
        for member in range(19):
            factor = flow_vectors[member][component]
            if factor != 0:
                moment = moment + factor * populations[member]
        speeds.append(moment / density)
    square = speeds[0] * speeds[0] + speeds[1] * speeds[1] + speeds[2] * speeds[2]
    equilibria = []
    for member in range(19):
        vector = flow_vectors[member]
        project = vector[0] * speeds[0] + vector[1] * speeds[1] + vector[2] * speeds[2]
        equilibria.append(flow_weights[member] * density * (1.0 + 3.0 * project + 4.5 * project * project - 1.5 * square))
    stress = jnp.zeros_like(density)
    for first_axis in range(3):
        for second_axis in range(3):
            tensor = jnp.zeros_like(density)
            for member in range(19):
                factor = flow_vectors[member][first_axis] * flow_vectors[member][second_axis]
                if factor != 0:
                    tensor = tensor + factor * (populations[member] - equilibria[member])
            stress = stress + tensor * tensor
    relaxation = 0.5 * (tau_base + jnp.sqrt(tau_base * tau_base + 18.0 * math.sqrt(2.0) * smag_const * smag_const * jnp.sqrt(stress) / density))
    eddy = (relaxation - tau_base) / 3.0
    fluid_part = jnp.where(solid, jnp.zeros_like(density), jnp.ones_like(density))
    updated = []
    for member in range(19):
        relaxed = populations[member] - (populations[member] - equilibria[member]) / relaxation
        updated.append(jnp.where(solid, populations[flow_mirror[member]], relaxed))
    motion = [speeds[0] * fluid_part, speeds[1] * fluid_part, speeds[2] * fluid_part, eddy * fluid_part]
    return (updated, motion)

def scalar_collide(scalar, motion, solid, source):
    amount = scalar[0]
    for member in range(1, 7):
        amount = amount + scalar[member]
    relaxation = tau_scalar_base + 4.0 * motion[3] / schmidt_turb
    updated = []
    for member in range(7):
        vector = flow_vectors[member]
        project = vector[0] * motion[0] + vector[1] * motion[1] + vector[2] * motion[2]
        equilibrium = scalar_weights[member] * amount * (1.0 + 4.0 * project)
        relaxed = scalar[member] - (scalar[member] - equilibrium) / relaxation + scalar_weights[member] * source
        updated.append(jnp.where(solid, scalar[flow_mirror[member]], relaxed))
    return updated

def shift_in(grid_values, offset, dimension, outside):
    if offset == 0:
        return grid_values
    length = grid_values.shape[dimension]
    plane_shape = list(grid_values.shape)
    plane_shape[dimension] = 1
    edge_plane = jnp.full(plane_shape, outside, grid_values.dtype)
    if offset == 1:
        return jnp.concatenate([edge_plane, lax.slice_in_dim(grid_values, 0, length - 1, axis=dimension)], dimension)
    return jnp.concatenate([lax.slice_in_dim(grid_values, 1, length, axis=dimension), edge_plane], dimension)

def reference(flow_pops, concentration, solid_mask, source_cell, source_scalar, source_rate):
    extent_y, extent_z, extent_x = solid_mask.shape
    height = lax.broadcasted_iota(jnp.int32, solid_mask.shape, 1)
    solid = (solid_mask == 1) | (height == 0) | (height == extent_z - 1)
    populations = [flow_pops[member] for member in range(19)]
    history = []
    for time_step in range(STEPS):
        populations, motion = flow_collide(populations, solid)
        history.append(jnp.stack(motion))
        read = []
        for member in range(19):
            vector = flow_vectors[member]
            moved = shift_in(populations[member], vector[2], 1, 0.0)
            moved = jnp.roll(moved, vector[1], axis=0)
            moved = shift_in(moved, vector[0], 2, far_field(member))
            read.append(moved)
        populations = read
    history = jnp.stack(history)
    blocks = concentration.reshape(N_ROW, SC_ROW, extent_y, extent_z, extent_x)
    cells = extent_y * extent_z * extent_x

    def advance_block(pair):
        block_index, block = pair
        local_scalar = source_scalar - block_index * SC_ROW
        valid = (local_scalar >= 0) & (local_scalar < SC_ROW)
        target = jnp.where(valid, local_scalar, SC_ROW).astype(jnp.int32)
        source = jnp.zeros((SC_ROW, cells), jnp.float32).at[target, source_cell].add(source_rate, mode='drop')
        source = source.reshape(SC_ROW, extent_y, extent_z, extent_x)
        scalar = [scalar_weights[member] * block for member in range(7)]
        for time_step in range(STEPS):
            motion = [history[time_step, component] for component in range(4)]
            scalar = scalar_collide(scalar, motion, solid, source)
            read = []
            for member in range(7):
                vector = flow_vectors[member]
                moved = shift_in(scalar[member], vector[2], 2, 0.0)
                moved = jnp.roll(moved, vector[1], axis=1)
                moved = shift_in(moved, vector[0], 3, 0.0)
                read.append(moved)
            scalar = read
        amount = scalar[0]
        for member in range(1, 7):
            amount = amount + scalar[member]
        return amount
    result = lax.map(advance_block, (jnp.arange(N_ROW, dtype=jnp.int32), blocks))
    final_concentration = result.reshape(concentration.shape)
    return (jnp.stack(populations), final_concentration)
```

```python
import math

import jax
import jax.numpy as jnp
from jax import lax
from jax.sharding import PartitionSpec as P

STEPS = 3


flow_vectors = (
    (0, 0, 0),
    (1, 0, 0),
    (-1, 0, 0),
    (0, 1, 0),
    (0, -1, 0),
    (0, 0, 1),
    (0, 0, -1),
    (1, 1, 0),
    (-1, -1, 0),
    (1, -1, 0),
    (-1, 1, 0),
    (1, 0, 1),
    (-1, 0, -1),
    (1, 0, -1),
    (-1, 0, 1),
    (0, 1, 1),
    (0, -1, -1),
    (0, 1, -1),
    (0, -1, 1),
)
scalar_vectors = flow_vectors[:7]
flow_weights = (1.0 / 3.0,) + (1.0 / 18.0,) * 6 + (1.0 / 36.0,) * 12
flow_mirror = (0, 2, 1, 4, 3, 6, 5, 8, 7, 10, 9, 12, 11, 14, 13, 16, 15, 18, 17)
scalar_weights = (0.25,) + (0.125,) * 6
tau_base = 0.52
smag_const = 0.17
tau_scalar_base = 0.55
schmidt_turb = 0.7
inflow_speed = 0.08


def passed_along(block, axis, distance):
    devices = range(lax.axis_size(axis))
    route = [(i - distance, i) for i in devices if i - distance in devices]
    return lax.ppermute(block, axis, route)


def from_behind(value, axis, steps):
    count = lax.axis_size(axis)
    pairs = [(source, (source + steps) % count) for source in range(count)]
    return lax.ppermute(value, axis, pairs)


def in_order(tiles, dim):
    tiles = jnp.moveaxis(tiles, 0, dim)
    shape = tiles.shape
    return tiles.reshape(*shape[:dim], shape[dim] * shape[dim + 1], *shape[dim + 2 :])


def copy_for_each(x, axis):
    copies = jnp.broadcast_to(x, (lax.axis_size(axis), *x.shape))
    return lax.all_to_all(copies, axis, split_axis=0, concat_axis=0, tiled=True)


def gathered_copies(x, axis, dim):
    return in_order(copy_for_each(x, axis), dim)


def far_field(member):
    along = flow_vectors[member][0] * inflow_speed
    return flow_weights[member] * (
        1.0 + 3.0 * along + 4.5 * along * along - 1.5 * inflow_speed * inflow_speed
    )


def flow_collide(populations, solid):
    density = populations[0]
    for member in range(1, 19):
        density = density + populations[member]
    speeds = []
    for component in range(3):
        moment = jnp.zeros_like(density)
        for member in range(19):
            factor = flow_vectors[member][component]
            if factor != 0:
                moment = moment + factor * populations[member]
        speeds.append(moment / density)
    square = speeds[0] * speeds[0] + speeds[1] * speeds[1] + speeds[2] * speeds[2]
    equilibria = []
    for member in range(19):
        vector = flow_vectors[member]
        project = vector[0] * speeds[0] + vector[1] * speeds[1] + vector[2] * speeds[2]
        equilibria.append(
            flow_weights[member]
            * density
            * (1.0 + 3.0 * project + 4.5 * project * project - 1.5 * square)
        )
    stress = jnp.zeros_like(density)
    for first_axis in range(3):
        for second_axis in range(3):
            tensor = jnp.zeros_like(density)
            for member in range(19):
                factor = flow_vectors[member][first_axis] * flow_vectors[member][second_axis]
                if factor != 0:
                    tensor = tensor + factor * (populations[member] - equilibria[member])
            stress = stress + tensor * tensor
    relaxation = 0.5 * (
        tau_base
        + jnp.sqrt(
            tau_base * tau_base
            + 18.0 * math.sqrt(2.0) * smag_const * smag_const * jnp.sqrt(stress) / density
        )
    )
    eddy = (relaxation - tau_base) / 3.0
    fluid_part = jnp.where(solid, jnp.zeros_like(density), jnp.ones_like(density))
    updated = []
    for member in range(19):
        relaxed = populations[member] - (populations[member] - equilibria[member]) / relaxation
        updated.append(jnp.where(solid, populations[flow_mirror[member]], relaxed))
    motion = jnp.stack(
        [speeds[0] * fluid_part, speeds[1] * fluid_part, speeds[2] * fluid_part, eddy * fluid_part]
    )
    return (updated, motion)


def scalar_collide(scalar, motion, solid, source):
    amount = scalar[0]
    for member in range(1, 7):
        amount = amount + scalar[member]
    relaxation = tau_scalar_base + 4.0 * motion[3] / schmidt_turb
    updated = []
    for member in range(7):
        vector = flow_vectors[member]
        project = vector[0] * motion[0] + vector[1] * motion[1] + vector[2] * motion[2]
        equilibrium = scalar_weights[member] * amount * (1.0 + 4.0 * project)
        relaxed = (
            scalar[member]
            - (scalar[member] - equilibrium) / relaxation
            + scalar_weights[member] * source
        )
        updated.append(jnp.where(solid, scalar[flow_mirror[member]], relaxed))
    return updated


def edge_planes(pieces, vectors, component, dimension, heading):
    planes = []
    for member in range(len(pieces)):
        if vectors[member][component] == heading:
            length = pieces[member].shape[dimension]
            position = length - 1 if heading == 1 else 0
            planes.append(lax.index_in_dim(pieces[member], position, dimension, keepdims=False))
    return jnp.stack(planes)


def displace(pieces, vectors, component, dimension, from_low, from_high):
    result = []
    low_count = 0
    high_count = 0
    for member in range(len(pieces)):
        piece = pieces[member]
        length = piece.shape[dimension]
        heading = vectors[member][component]
        if heading == 1:
            entering = jnp.expand_dims(from_low[low_count], dimension)
            low_count = low_count + 1
            result.append(
                jnp.concatenate(
                    [entering, lax.slice_in_dim(piece, 0, length - 1, axis=dimension)], dimension
                )
            )
        elif heading == -1:
            entering = jnp.expand_dims(from_high[high_count], dimension)
            high_count = high_count + 1
            result.append(
                jnp.concatenate(
                    [lax.slice_in_dim(piece, 1, length, axis=dimension), entering], dimension
                )
            )
        else:
            result.append(piece)
    return result


def local_vertical(pieces, vectors, dimension):
    from_low = jnp.zeros_like(edge_planes(pieces, vectors, 2, dimension, 1))
    from_high = jnp.zeros_like(edge_planes(pieces, vectors, 2, dimension, -1))
    return displace(pieces, vectors, 2, dimension, from_low, from_high)


def send_vertical(planes, offset):
    return passed_along(planes, "row", offset)


def send_spanwise(packed, offset):
    return from_behind(packed, "gy", offset)


def send_streamwise(packed, offset):
    return passed_along(packed, "gx", offset)


def keep_spanwise(flow_in, heading):
    return flow_in


def inflow_fill(flow_in, heading):
    boundary = 0 if heading == 1 else lax.axis_size("gx") - 1
    members = [member for member in range(19) if flow_vectors[member][0] == heading]
    values = jnp.array([far_field(member) for member in members], jnp.float32).reshape(-1, 1, 1)
    return jnp.where(lax.axis_index("gx") == boundary, values + jnp.zeros_like(flow_in), flow_in)


def cross_section(flow, scalar, component, flow_dim, sender, edge_fill, keep_rows):
    arrived_flow = {}
    arrived_scalar = {}
    for heading in (1, -1):
        flow_planes = edge_planes(flow, flow_vectors, component, flow_dim, heading)
        scalar_planes = edge_planes(scalar, scalar_vectors, component, flow_dim + 1, heading)
        if keep_rows:
            width = flow_planes.shape[-1]
            packed = jnp.concatenate(
                [flow_planes.reshape(-1, width), scalar_planes.reshape(-1, width)], 0
            )
            split_at = flow_planes.size // width
        else:
            packed = jnp.concatenate([flow_planes.reshape(-1), scalar_planes.reshape(-1)], 0)
            split_at = flow_planes.size
        arrived = sender(packed, heading)
        arrived_flow[heading] = edge_fill(arrived[:split_at].reshape(flow_planes.shape), heading)
        arrived_scalar[heading] = arrived[split_at:].reshape(scalar_planes.shape)
    flow = displace(flow, flow_vectors, component, flow_dim, arrived_flow[1], arrived_flow[-1])
    scalar = displace(
        scalar, scalar_vectors, component, flow_dim + 1, arrived_scalar[1], arrived_scalar[-1]
    )
    return (flow, scalar)


def on_device(flow_pops, concentration, solid_mask, source_cell, source_scalar, source_rate):
    row_index = lax.axis_index("row")
    slab_depth = flow_pops.shape[2]
    scalars_here, span_y, depth, span_x = concentration.shape
    height = lax.broadcasted_iota(jnp.int32, solid_mask.shape, 1)
    solid = (solid_mask == 1) | (height == 0) | (height == depth - 1)
    total_x = span_x * lax.axis_size("gx")
    cell_y = source_cell // (depth * total_x)
    cell_z = source_cell // total_x % depth
    cell_x = source_cell % total_x
    local_y = cell_y - lax.axis_index("gy") * span_y
    local_x = cell_x - lax.axis_index("gx") * span_x
    local_scalar = source_scalar - row_index * scalars_here
    count = source_cell.shape[0]
    plane_shape = (scalars_here, span_y, depth, count)
    hit = (
        (lax.broadcasted_iota(jnp.int32, plane_shape, 0) == local_scalar)
        & (lax.broadcasted_iota(jnp.int32, plane_shape, 1) == local_y)
        & (lax.broadcasted_iota(jnp.int32, plane_shape, 2) == cell_z)
    )
    weights = jnp.where(hit, source_rate, 0.0).reshape(-1, count)
    columns = (
        lax.broadcasted_iota(jnp.int32, (count, span_x), 1) == local_x[:, None]
    ).astype(jnp.float32)
    source = jnp.dot(
        weights, columns, precision=lax.Precision.HIGHEST, preferred_element_type=jnp.float32
    ).reshape(concentration.shape)
    whole = lax.all_gather(flow_pops, "row", axis=2, tiled=True)
    flow = [whole[member] for member in range(19)]
    scalar = [scalar_weights[member] * concentration for member in range(7)]
    def one_step(time_step, state):
        flow, scalar = state
        flow, motion = flow_collide(list(flow), solid)
        scalar = scalar_collide(list(scalar), [motion[component] for component in range(4)], solid, source)
        flow = local_vertical(flow, flow_vectors, 1)
        scalar = local_vertical(scalar, scalar_vectors, 2)
        flow, scalar = cross_section(flow, scalar, 1, 0, send_spanwise, keep_spanwise, True)
        flow, scalar = cross_section(flow, scalar, 0, 2, send_streamwise, inflow_fill, False)
        return (tuple(flow), tuple(scalar))

    flow, scalar = lax.fori_loop(0, STEPS, one_step, (tuple(flow), tuple(scalar)))
    amount = scalar[0]
    for member in range(1, 7):
        amount = amount + scalar[member]
    stacked = lax.dynamic_slice_in_dim(jnp.stack(flow), row_index * slab_depth, slab_depth, 2)
    return (stacked, amount)


def solution(mesh):
    in_specs = (
        P(None, "gy", "row", "gx"),
        P("row", "gy", None, "gx"),
        P("gy", None, "gx"),
        P(),
        P(),
        P(),
    )
    out_specs = (P(None, "gy", "row", "gx"), P("row", "gy", None, "gx"))
    return jax.shard_map(
        on_device, mesh=mesh, in_specs=in_specs, out_specs=out_specs, check_vma=False
    )
```

```python
import math

import jax
import jax.numpy as jnp
from jax import lax
from jax.sharding import PartitionSpec as P
from jax.experimental import pallas as pl
from jax.experimental.pallas import tpu as pltpu

STEPS = 3


flow_vectors = (
    (0, 0, 0),
    (1, 0, 0),
    (-1, 0, 0),
    (0, 1, 0),
    (0, -1, 0),
    (0, 0, 1),
    (0, 0, -1),
    (1, 1, 0),
    (-1, -1, 0),
    (1, -1, 0),
    (-1, 1, 0),
    (1, 0, 1),
    (-1, 0, -1),
    (1, 0, -1),
    (-1, 0, 1),
    (0, 1, 1),
    (0, -1, -1),
    (0, 1, -1),
    (0, -1, 1),
)
scalar_vectors = flow_vectors[:7]
flow_weights = (1.0 / 3.0,) + (1.0 / 18.0,) * 6 + (1.0 / 36.0,) * 12
flow_mirror = (0, 2, 1, 4, 3, 6, 5, 8, 7, 10, 9, 12, 11, 14, 13, 16, 15, 18, 17)
scalar_weights = (0.25,) + (0.125,) * 6
tau_base = 0.52
smag_const = 0.17
tau_scalar_base = 0.55
schmidt_turb = 0.7
inflow_speed = 0.08


def passed_along(block, axis, distance):
    devices = range(lax.axis_size(axis))
    route = [(i - distance, i) for i in devices if i - distance in devices]
    return lax.ppermute(block, axis, route)


def from_behind(value, axis, steps):
    count = lax.axis_size(axis)
    pairs = [(source, (source + steps) % count) for source in range(count)]
    return lax.ppermute(value, axis, pairs)


def in_order(tiles, dim):
    tiles = jnp.moveaxis(tiles, 0, dim)
    shape = tiles.shape
    return tiles.reshape(*shape[:dim], shape[dim] * shape[dim + 1], *shape[dim + 2 :])


def copy_for_each(x, axis):
    copies = jnp.broadcast_to(x, (lax.axis_size(axis), *x.shape))
    return lax.all_to_all(copies, axis, split_axis=0, concat_axis=0, tiled=True)


def gathered_copies(x, axis, dim):
    return in_order(copy_for_each(x, axis), dim)


def far_field(member):
    along = flow_vectors[member][0] * inflow_speed
    return flow_weights[member] * (
        1.0 + 3.0 * along + 4.5 * along * along - 1.5 * inflow_speed * inflow_speed
    )


def flow_collide(populations, solid):
    density = populations[0]
    for member in range(1, 19):
        density = density + populations[member]
    speeds = []
    for component in range(3):
        moment = jnp.zeros_like(density)
        for member in range(19):
            factor = flow_vectors[member][component]
            if factor != 0:
                moment = moment + factor * populations[member]
        speeds.append(moment / density)
    square = speeds[0] * speeds[0] + speeds[1] * speeds[1] + speeds[2] * speeds[2]
    equilibria = []
    for member in range(19):
        vector = flow_vectors[member]
        project = vector[0] * speeds[0] + vector[1] * speeds[1] + vector[2] * speeds[2]
        equilibria.append(
            flow_weights[member]
            * density
            * (1.0 + 3.0 * project + 4.5 * project * project - 1.5 * square)
        )
    stress = jnp.zeros_like(density)
    for first_axis in range(3):
        for second_axis in range(3):
            tensor = jnp.zeros_like(density)
            for member in range(19):
                factor = flow_vectors[member][first_axis] * flow_vectors[member][second_axis]
                if factor != 0:
                    tensor = tensor + factor * (populations[member] - equilibria[member])
            stress = stress + tensor * tensor
    relaxation = 0.5 * (
        tau_base
        + jnp.sqrt(
            tau_base * tau_base
            + 18.0 * math.sqrt(2.0) * smag_const * smag_const * jnp.sqrt(stress) / density
        )
    )
    eddy = (relaxation - tau_base) / 3.0
    fluid_part = jnp.where(solid, jnp.zeros_like(density), jnp.ones_like(density))
    updated = []
    for member in range(19):
        relaxed = populations[member] - (populations[member] - equilibria[member]) / relaxation
        updated.append(jnp.where(solid, populations[flow_mirror[member]], relaxed))
    motion = jnp.stack(
        [speeds[0] * fluid_part, speeds[1] * fluid_part, speeds[2] * fluid_part, eddy * fluid_part]
    )
    return (updated, motion)


def scalar_collide(scalar, motion, solid, source):
    amount = scalar[0]
    for member in range(1, 7):
        amount = amount + scalar[member]
    relaxation = tau_scalar_base + 4.0 * motion[3] / schmidt_turb
    updated = []
    for member in range(7):
        vector = flow_vectors[member]
        project = vector[0] * motion[0] + vector[1] * motion[1] + vector[2] * motion[2]
        equilibrium = scalar_weights[member] * amount * (1.0 + 4.0 * project)
        relaxed = (
            scalar[member]
            - (scalar[member] - equilibrium) / relaxation
            + scalar_weights[member] * source
        )
        updated.append(jnp.where(solid, scalar[flow_mirror[member]], relaxed))
    return updated


def edge_planes(pieces, vectors, component, dimension, heading):
    planes = []
    for member in range(len(pieces)):
        if vectors[member][component] == heading:
            length = pieces[member].shape[dimension]
            position = length - 1 if heading == 1 else 0
            planes.append(lax.index_in_dim(pieces[member], position, dimension, keepdims=False))
    return jnp.stack(planes)


def displace(pieces, vectors, component, dimension, from_low, from_high):
    result = []
    low_count = 0
    high_count = 0
    for member in range(len(pieces)):
        piece = pieces[member]
        length = piece.shape[dimension]
        heading = vectors[member][component]
        if heading == 1:
            entering = jnp.expand_dims(from_low[low_count], dimension)
            low_count = low_count + 1
            result.append(
                jnp.concatenate(
                    [entering, lax.slice_in_dim(piece, 0, length - 1, axis=dimension)], dimension
                )
            )
        elif heading == -1:
            entering = jnp.expand_dims(from_high[high_count], dimension)
            high_count = high_count + 1
            result.append(
                jnp.concatenate(
                    [lax.slice_in_dim(piece, 1, length, axis=dimension), entering], dimension
                )
            )
        else:
            result.append(piece)
    return result


def local_vertical(pieces, vectors, dimension):
    from_low = jnp.zeros_like(edge_planes(pieces, vectors, 2, dimension, 1))
    from_high = jnp.zeros_like(edge_planes(pieces, vectors, 2, dimension, -1))
    return displace(pieces, vectors, 2, dimension, from_low, from_high)


def send_vertical(planes, offset):
    return passed_along(planes, "row", offset)


def send_spanwise(packed, offset):
    return from_behind(packed, "gy", offset)


def send_streamwise(packed, offset):
    return passed_along(packed, "gx", offset)


def keep_spanwise(flow_in, heading):
    return flow_in


def inflow_fill(flow_in, heading):
    boundary = 0 if heading == 1 else lax.axis_size("gx") - 1
    members = [member for member in range(19) if flow_vectors[member][0] == heading]
    values = jnp.array([far_field(member) for member in members], jnp.float32).reshape(-1, 1, 1)
    return jnp.where(lax.axis_index("gx") == boundary, values + jnp.zeros_like(flow_in), flow_in)


def cross_section(flow, scalar, component, flow_dim, sender, edge_fill, keep_rows):
    arrived_flow = {}
    arrived_scalar = {}
    for heading in (1, -1):
        flow_planes = edge_planes(flow, flow_vectors, component, flow_dim, heading)
        scalar_planes = edge_planes(scalar, scalar_vectors, component, flow_dim + 1, heading)
        if keep_rows:
            width = flow_planes.shape[-1]
            packed = jnp.concatenate(
                [flow_planes.reshape(-1, width), scalar_planes.reshape(-1, width)], 0
            )
            split_at = flow_planes.size // width
        else:
            packed = jnp.concatenate([flow_planes.reshape(-1), scalar_planes.reshape(-1)], 0)
            split_at = flow_planes.size
        arrived = sender(packed, heading)
        arrived_flow[heading] = edge_fill(arrived[:split_at].reshape(flow_planes.shape), heading)
        arrived_scalar[heading] = arrived[split_at:].reshape(scalar_planes.shape)
    flow = displace(flow, flow_vectors, component, flow_dim, arrived_flow[1], arrived_flow[-1])
    scalar = displace(
        scalar, scalar_vectors, component, flow_dim + 1, arrived_scalar[1], arrived_scalar[-1]
    )
    return (flow, scalar)


def scalar_kernel(mode, span_y, depth, span_x):
    def body(*refs):
        if mode == "first":
            conc_ref, motion_ref, solid_ref, source_ref, out_ref = refs
        elif mode == "middle":
            (g_ref, lo_x_ref, hi_x_ref, lo_y_ref, hi_y_ref,
             motion_ref, solid_ref, source_ref, out_ref) = refs
        else:
            g_ref, lo_x_ref, hi_x_ref, lo_y_ref, hi_y_ref, out_ref = refs
        lane = lax.broadcasted_iota(jnp.int32, (depth, span_x), 1)
        level = lax.broadcasted_iota(jnp.int32, (depth, span_x), 0)
        for y in range(span_y):
            if mode == "first":
                block = conc_ref[0, y]
                scalar = [scalar_weights[member] * block for member in range(7)]
            else:
                moved_x = pltpu.roll(g_ref[1, 0, y], 1, 1)
                back_x = pltpu.roll(g_ref[2, 0, y], span_x - 1, 1)
                moved_z = pltpu.roll(g_ref[5, 0, y], 1, 0)
                back_z = pltpu.roll(g_ref[6, 0, y], depth - 1, 0)
                scalar = [
                    g_ref[0, 0, y],
                    jnp.where(lane == 0, lo_x_ref[0, y], moved_x),
                    jnp.where(lane == span_x - 1, hi_x_ref[0, y], back_x),
                    g_ref[3, 0, y - 1] if y > 0 else lo_y_ref[0],
                    g_ref[4, 0, y + 1] if y < span_y - 1 else hi_y_ref[0],
                    jnp.where(level == 0, 0.0, moved_z),
                    jnp.where(level == depth - 1, 0.0, back_z),
                ]
            amount = scalar[0]
            for member in range(1, 7):
                amount = amount + scalar[member]
            if mode == "final":
                out_ref[0, y] = amount
                continue
            speeds = [motion_ref[component, y] for component in range(3)]
            relaxation = tau_scalar_base + 4.0 * motion_ref[3, y] / schmidt_turb
            solid = solid_ref[y] != 0
            source = source_ref[0, y]
            for member in range(7):
                vector = flow_vectors[member]
                project = vector[0] * speeds[0] + vector[1] * speeds[1] + vector[2] * speeds[2]
                equilibrium = scalar_weights[member] * amount * (1.0 + 4.0 * project)
                relaxed = (
                    scalar[member]
                    - (scalar[member] - equilibrium) / relaxation
                    + scalar_weights[member] * source
                )
                out_ref[member, 0, y] = jnp.where(solid, scalar[flow_mirror[member]], relaxed)

    return body


def scalar_stage(mode, scalars, halos, motion, solid, source):
    count, span_y, depth, span_x = source.shape if source is not None else scalars.shape[1:]
    whole = lambda shape: pl.BlockSpec(shape, lambda s: (0,) * len(shape))
    one = lambda shape: pl.BlockSpec(shape, lambda s: (s,) + (0,) * (len(shape) - 1))
    stacked = pl.BlockSpec((7, 1, span_y, depth, span_x), lambda s: (0, s, 0, 0, 0))
    cells = (span_y, depth, span_x)
    edge_specs = [one((1, span_y, depth, 1))] * 2 + [one((1, depth, span_x))] * 2
    if mode == "first":
        operands = [scalars, motion, solid, source]
        specs = [one((1,) + cells), whole((4,) + cells), whole(cells), one((1,) + cells)]
    elif mode == "middle":
        operands = [scalars, *halos, motion, solid, source]
        specs = [stacked] + edge_specs + [whole((4,) + cells), whole(cells), one((1,) + cells)]
    else:
        operands = [scalars, *halos]
        specs = [stacked] + edge_specs
    if mode == "final":
        out_spec = one((1,) + cells)
        out_shape = jax.ShapeDtypeStruct((count,) + cells, jnp.float32)
    else:
        out_spec = stacked
        out_shape = jax.ShapeDtypeStruct((7, count) + cells, jnp.float32)
    return pl.pallas_call(
        scalar_kernel(mode, span_y, depth, span_x),
        grid=(count,),
        in_specs=specs,
        out_specs=out_spec,
        out_shape=out_shape,
    )(*operands)


def scalar_edges(post):
    span_y, span_x = post.shape[2], post.shape[4]
    lo_x = passed_along(post[1, :, :, :, span_x - 1 : span_x], "gx", 1)
    hi_x = passed_along(post[2, :, :, :, 0:1], "gx", -1)
    lo_y = from_behind(post[3, :, span_y - 1], "gy", 1)
    hi_y = from_behind(post[4, :, 0], "gy", -1)
    return (lo_x, hi_x, lo_y, hi_y)


def flow_section(flow, component, flow_dim, sender, edge_fill):
    arrived = {}
    for heading in (1, -1):
        planes = edge_planes(flow, flow_vectors, component, flow_dim, heading)
        arrived[heading] = edge_fill(sender(planes, heading), heading)
    return displace(flow, flow_vectors, component, flow_dim, arrived[1], arrived[-1])


def on_device(flow_pops, concentration, solid_mask, source_cell, source_scalar, source_rate):
    row_index = lax.axis_index("row")
    slab_depth = flow_pops.shape[2]
    scalars_here, span_y, depth, span_x = concentration.shape
    height = lax.broadcasted_iota(jnp.int32, solid_mask.shape, 1)
    solid = (solid_mask == 1) | (height == 0) | (height == depth - 1)
    total_x = span_x * lax.axis_size("gx")
    cell_y = source_cell // (depth * total_x)
    cell_z = source_cell // total_x % depth
    cell_x = source_cell % total_x
    local_y = cell_y - lax.axis_index("gy") * span_y
    local_x = cell_x - lax.axis_index("gx") * span_x
    local_scalar = source_scalar - row_index * scalars_here
    count = source_cell.shape[0]
    plane_shape = (scalars_here, span_y, depth, count)
    hit = (
        (lax.broadcasted_iota(jnp.int32, plane_shape, 0) == local_scalar)
        & (lax.broadcasted_iota(jnp.int32, plane_shape, 1) == local_y)
        & (lax.broadcasted_iota(jnp.int32, plane_shape, 2) == cell_z)
    )
    weights = jnp.where(hit, source_rate, 0.0).reshape(-1, count)
    columns = (
        lax.broadcasted_iota(jnp.int32, (count, span_x), 1) == local_x[:, None]
    ).astype(jnp.float32)
    source = jnp.dot(
        weights, columns, precision=lax.Precision.HIGHEST, preferred_element_type=jnp.float32
    ).reshape(concentration.shape)
    solid_flag = solid.astype(jnp.int32)
    whole = gathered_copies(flow_pops, "row", 2)
    flow = [whole[member] for member in range(19)]
    scalars = concentration
    halos = None
    for time_step in range(STEPS):
        flow, motion = flow_collide(flow, solid)
        mode = "first" if time_step == 0 else "middle"
        scalars = scalar_stage(mode, scalars, halos, motion, solid_flag, source)
        halos = scalar_edges(scalars)
        flow = local_vertical(flow, flow_vectors, 1)
        flow = flow_section(flow, 1, 0, send_spanwise, keep_spanwise)
        flow = flow_section(flow, 0, 2, send_streamwise, inflow_fill)
    amount = scalar_stage("final", scalars, halos, None, None, None)
    stacked = lax.dynamic_slice_in_dim(jnp.stack(flow), row_index * slab_depth, slab_depth, 2)
    return (stacked, amount)


def solution(mesh):
    in_specs = (
        P(None, "gy", "row", "gx"),
        P("row", "gy", None, "gx"),
        P("gy", None, "gx"),
        P(),
        P(),
        P(),
    )
    out_specs = (P(None, "gy", "row", "gx"), P("row", "gy", None, "gx"))
    return jax.shard_map(
        on_device, mesh=mesh, in_specs=in_specs, out_specs=out_specs, check_vma=False
    )
```

```python
import math

import jax
import jax.numpy as jnp
from jax import lax
from jax.sharding import PartitionSpec as P
from jax.experimental import pallas as pl
from jax.experimental.pallas import tpu as pltpu

STEPS = 3


flow_vectors = (
    (0, 0, 0),
    (1, 0, 0),
    (-1, 0, 0),
    (0, 1, 0),
    (0, -1, 0),
    (0, 0, 1),
    (0, 0, -1),
    (1, 1, 0),
    (-1, -1, 0),
    (1, -1, 0),
    (-1, 1, 0),
    (1, 0, 1),
    (-1, 0, -1),
    (1, 0, -1),
    (-1, 0, 1),
    (0, 1, 1),
    (0, -1, -1),
    (0, 1, -1),
    (0, -1, 1),
)
scalar_vectors = flow_vectors[:7]
flow_weights = (1.0 / 3.0,) + (1.0 / 18.0,) * 6 + (1.0 / 36.0,) * 12
flow_mirror = (0, 2, 1, 4, 3, 6, 5, 8, 7, 10, 9, 12, 11, 14, 13, 16, 15, 18, 17)
scalar_weights = (0.25,) + (0.125,) * 6
tau_base = 0.52
smag_const = 0.17
tau_scalar_base = 0.55
schmidt_turb = 0.7
inflow_speed = 0.08


def passed_along(block, axis, distance):
    devices = range(lax.axis_size(axis))
    route = [(i - distance, i) for i in devices if i - distance in devices]
    return lax.ppermute(block, axis, route)


def from_behind(value, axis, steps):
    count = lax.axis_size(axis)
    pairs = [(source, (source + steps) % count) for source in range(count)]
    return lax.ppermute(value, axis, pairs)


def in_order(tiles, dim):
    tiles = jnp.moveaxis(tiles, 0, dim)
    shape = tiles.shape
    return tiles.reshape(*shape[:dim], shape[dim] * shape[dim + 1], *shape[dim + 2 :])


def copy_for_each(x, axis):
    copies = jnp.broadcast_to(x, (lax.axis_size(axis), *x.shape))
    return lax.all_to_all(copies, axis, split_axis=0, concat_axis=0, tiled=True)


def gathered_copies(x, axis, dim):
    return in_order(copy_for_each(x, axis), dim)


def far_field(member):
    along = flow_vectors[member][0] * inflow_speed
    return flow_weights[member] * (
        1.0 + 3.0 * along + 4.5 * along * along - 1.5 * inflow_speed * inflow_speed
    )


def flow_collide(populations, solid):
    density = populations[0]
    for member in range(1, 19):
        density = density + populations[member]
    speeds = []
    for component in range(3):
        moment = jnp.zeros_like(density)
        for member in range(19):
            factor = flow_vectors[member][component]
            if factor != 0:
                moment = moment + factor * populations[member]
        speeds.append(moment / density)
    square = speeds[0] * speeds[0] + speeds[1] * speeds[1] + speeds[2] * speeds[2]
    equilibria = []
    for member in range(19):
        vector = flow_vectors[member]
        project = vector[0] * speeds[0] + vector[1] * speeds[1] + vector[2] * speeds[2]
        equilibria.append(
            flow_weights[member]
            * density
            * (1.0 + 3.0 * project + 4.5 * project * project - 1.5 * square)
        )
    stress = jnp.zeros_like(density)
    for first_axis in range(3):
        for second_axis in range(3):
            tensor = jnp.zeros_like(density)
            for member in range(19):
                factor = flow_vectors[member][first_axis] * flow_vectors[member][second_axis]
                if factor != 0:
                    tensor = tensor + factor * (populations[member] - equilibria[member])
            stress = stress + tensor * tensor
    relaxation = 0.5 * (
        tau_base
        + jnp.sqrt(
            tau_base * tau_base
            + 18.0 * math.sqrt(2.0) * smag_const * smag_const * jnp.sqrt(stress) / density
        )
    )
    eddy = (relaxation - tau_base) / 3.0
    fluid_part = jnp.where(solid, jnp.zeros_like(density), jnp.ones_like(density))
    updated = []
    for member in range(19):
        relaxed = populations[member] - (populations[member] - equilibria[member]) / relaxation
        updated.append(jnp.where(solid, populations[flow_mirror[member]], relaxed))
    motion = jnp.stack(
        [speeds[0] * fluid_part, speeds[1] * fluid_part, speeds[2] * fluid_part, eddy * fluid_part]
    )
    return (updated, motion)


def scalar_collide(scalar, motion, solid, source):
    amount = scalar[0]
    for member in range(1, 7):
        amount = amount + scalar[member]
    relaxation = tau_scalar_base + 4.0 * motion[3] / schmidt_turb
    updated = []
    for member in range(7):
        vector = flow_vectors[member]
        project = vector[0] * motion[0] + vector[1] * motion[1] + vector[2] * motion[2]
        equilibrium = scalar_weights[member] * amount * (1.0 + 4.0 * project)
        relaxed = (
            scalar[member]
            - (scalar[member] - equilibrium) / relaxation
            + scalar_weights[member] * source
        )
        updated.append(jnp.where(solid, scalar[flow_mirror[member]], relaxed))
    return updated


def edge_planes(pieces, vectors, component, dimension, heading):
    planes = []
    for member in range(len(pieces)):
        if vectors[member][component] == heading:
            length = pieces[member].shape[dimension]
            position = length - 1 if heading == 1 else 0
            planes.append(lax.index_in_dim(pieces[member], position, dimension, keepdims=False))
    return jnp.stack(planes)


def displace(pieces, vectors, component, dimension, from_low, from_high):
    result = []
    low_count = 0
    high_count = 0
    for member in range(len(pieces)):
        piece = pieces[member]
        length = piece.shape[dimension]
        heading = vectors[member][component]
        if heading == 1:
            entering = jnp.expand_dims(from_low[low_count], dimension)
            low_count = low_count + 1
            result.append(
                jnp.concatenate(
                    [entering, lax.slice_in_dim(piece, 0, length - 1, axis=dimension)], dimension
                )
            )
        elif heading == -1:
            entering = jnp.expand_dims(from_high[high_count], dimension)
            high_count = high_count + 1
            result.append(
                jnp.concatenate(
                    [lax.slice_in_dim(piece, 1, length, axis=dimension), entering], dimension
                )
            )
        else:
            result.append(piece)
    return result


def local_vertical(pieces, vectors, dimension):
    from_low = jnp.zeros_like(edge_planes(pieces, vectors, 2, dimension, 1))
    from_high = jnp.zeros_like(edge_planes(pieces, vectors, 2, dimension, -1))
    return displace(pieces, vectors, 2, dimension, from_low, from_high)


def send_vertical(planes, offset):
    return passed_along(planes, "row", offset)


def send_spanwise(packed, offset):
    return from_behind(packed, "gy", offset)


def send_streamwise(packed, offset):
    return passed_along(packed, "gx", offset)


def keep_spanwise(flow_in, heading):
    return flow_in


def inflow_fill(flow_in, heading):
    boundary = 0 if heading == 1 else lax.axis_size("gx") - 1
    members = [member for member in range(19) if flow_vectors[member][0] == heading]
    values = jnp.array([far_field(member) for member in members], jnp.float32).reshape(-1, 1, 1)
    return jnp.where(lax.axis_index("gx") == boundary, values + jnp.zeros_like(flow_in), flow_in)


def cross_section(flow, scalar, component, flow_dim, sender, edge_fill, keep_rows):
    arrived_flow = {}
    arrived_scalar = {}
    for heading in (1, -1):
        flow_planes = edge_planes(flow, flow_vectors, component, flow_dim, heading)
        scalar_planes = edge_planes(scalar, scalar_vectors, component, flow_dim + 1, heading)
        if keep_rows:
            width = flow_planes.shape[-1]
            packed = jnp.concatenate(
                [flow_planes.reshape(-1, width), scalar_planes.reshape(-1, width)], 0
            )
            split_at = flow_planes.size // width
        else:
            packed = jnp.concatenate([flow_planes.reshape(-1), scalar_planes.reshape(-1)], 0)
            split_at = flow_planes.size
        arrived = sender(packed, heading)
        arrived_flow[heading] = edge_fill(arrived[:split_at].reshape(flow_planes.shape), heading)
        arrived_scalar[heading] = arrived[split_at:].reshape(scalar_planes.shape)
    flow = displace(flow, flow_vectors, component, flow_dim, arrived_flow[1], arrived_flow[-1])
    scalar = displace(
        scalar, scalar_vectors, component, flow_dim + 1, arrived_scalar[1], arrived_scalar[-1]
    )
    return (flow, scalar)


def scalar_kernel(mode, span_y, depth, span_x):
    def body(*refs):
        if mode == "first":
            conc_ref, motion_ref, solid_ref, source_ref, out_ref = refs
        elif mode == "middle":
            (g_ref, lo_x_ref, hi_x_ref, lo_y_ref, hi_y_ref,
             motion_ref, solid_ref, source_ref, out_ref) = refs
        else:
            g_ref, lo_x_ref, hi_x_ref, lo_y_ref, hi_y_ref, out_ref = refs
        lane = lax.broadcasted_iota(jnp.int32, (depth, span_x), 1)
        level = lax.broadcasted_iota(jnp.int32, (depth, span_x), 0)
        for y in range(span_y):
            if mode == "first":
                block = conc_ref[0, y]
                scalar = [scalar_weights[member] * block for member in range(7)]
            else:
                moved_x = pltpu.roll(g_ref[1, 0, y], 1, 1)
                back_x = pltpu.roll(g_ref[2, 0, y], span_x - 1, 1)
                moved_z = pltpu.roll(g_ref[5, 0, y], 1, 0)
                back_z = pltpu.roll(g_ref[6, 0, y], depth - 1, 0)
                scalar = [
                    g_ref[0, 0, y],
                    jnp.where(lane == 0, lo_x_ref[0, y], moved_x),
                    jnp.where(lane == span_x - 1, hi_x_ref[0, y], back_x),
                    g_ref[3, 0, y - 1] if y > 0 else lo_y_ref[0],
                    g_ref[4, 0, y + 1] if y < span_y - 1 else hi_y_ref[0],
                    jnp.where(level == 0, 0.0, moved_z),
                    jnp.where(level == depth - 1, 0.0, back_z),
                ]
            amount = scalar[0]
            for member in range(1, 7):
                amount = amount + scalar[member]
            if mode == "final":
                out_ref[0, y] = amount
                continue
            speeds = [motion_ref[component, y] for component in range(3)]
            relaxation = tau_scalar_base + 4.0 * motion_ref[3, y] / schmidt_turb
            solid = solid_ref[y] != 0
            source = source_ref[0, y]
            for member in range(7):
                vector = flow_vectors[member]
                project = vector[0] * speeds[0] + vector[1] * speeds[1] + vector[2] * speeds[2]
                equilibrium = scalar_weights[member] * amount * (1.0 + 4.0 * project)
                relaxed = (
                    scalar[member]
                    - (scalar[member] - equilibrium) / relaxation
                    + scalar_weights[member] * source
                )
                out_ref[member, 0, y] = jnp.where(solid, scalar[flow_mirror[member]], relaxed)

    return body


def scalar_stage(mode, scalars, halos, motion, solid, source):
    count, span_y, depth, span_x = source.shape if source is not None else scalars.shape[1:]
    whole = lambda shape: pl.BlockSpec(shape, lambda s: (0,) * len(shape))
    one = lambda shape: pl.BlockSpec(shape, lambda s: (s,) + (0,) * (len(shape) - 1))
    stacked = pl.BlockSpec((7, 1, span_y, depth, span_x), lambda s: (0, s, 0, 0, 0))
    cells = (span_y, depth, span_x)
    edge_specs = [one((1, span_y, depth, 1))] * 2 + [one((1, depth, span_x))] * 2
    if mode == "first":
        operands = [scalars, motion, solid, source]
        specs = [one((1,) + cells), whole((4,) + cells), whole(cells), one((1,) + cells)]
    elif mode == "middle":
        operands = [scalars, *halos, motion, solid, source]
        specs = [stacked] + edge_specs + [whole((4,) + cells), whole(cells), one((1,) + cells)]
    else:
        operands = [scalars, *halos]
        specs = [stacked] + edge_specs
    if mode == "final":
        out_spec = one((1,) + cells)
        out_shape = jax.ShapeDtypeStruct((count,) + cells, jnp.float32)
    else:
        out_spec = stacked
        out_shape = jax.ShapeDtypeStruct((7, count) + cells, jnp.float32)
    return pl.pallas_call(
        scalar_kernel(mode, span_y, depth, span_x),
        grid=(count,),
        in_specs=specs,
        out_specs=out_spec,
        out_shape=out_shape,
    )(*operands)


def scalar_edges(post):
    span_y, span_x = post.shape[2], post.shape[4]
    lo_x = passed_along(post[1, :, :, :, span_x - 1 : span_x], "gx", 1)
    hi_x = passed_along(post[2, :, :, :, 0:1], "gx", -1)
    lo_y = from_behind(post[3, :, span_y - 1], "gy", 1)
    hi_y = from_behind(post[4, :, 0], "gy", -1)
    return (lo_x, hi_x, lo_y, hi_y)


def flow_section(flow, component, flow_dim, sender, edge_fill):
    arrived = {}
    for heading in (1, -1):
        planes = edge_planes(flow, flow_vectors, component, flow_dim, heading)
        arrived[heading] = edge_fill(sender(planes, heading), heading)
    return displace(flow, flow_vectors, component, flow_dim, arrived[1], arrived[-1])


def on_device(flow_pops, concentration, solid_mask, source_cell, source_scalar, source_rate):
    row_index = lax.axis_index("row")
    slab_depth = flow_pops.shape[2]
    scalars_here, span_y, depth, span_x = concentration.shape
    height = lax.broadcasted_iota(jnp.int32, solid_mask.shape, 1)
    solid = (solid_mask == 1) | (height == 0) | (height == depth - 1)
    total_x = span_x * lax.axis_size("gx")
    cell_y = source_cell // (depth * total_x)
    cell_z = source_cell // total_x % depth
    cell_x = source_cell % total_x
    local_y = cell_y - lax.axis_index("gy") * span_y
    local_x = cell_x - lax.axis_index("gx") * span_x
    local_scalar = source_scalar - row_index * scalars_here
    count = source_cell.shape[0]
    plane_shape = (scalars_here, span_y, depth, count)
    hit = (
        (lax.broadcasted_iota(jnp.int32, plane_shape, 0) == local_scalar)
        & (lax.broadcasted_iota(jnp.int32, plane_shape, 1) == local_y)
        & (lax.broadcasted_iota(jnp.int32, plane_shape, 2) == cell_z)
    )
    weights = jnp.where(hit, source_rate, 0.0).reshape(-1, count)
    columns = (
        lax.broadcasted_iota(jnp.int32, (count, span_x), 1) == local_x[:, None]
    ).astype(jnp.float32)
    source = jnp.dot(
        weights, columns, precision=lax.Precision.HIGHEST, preferred_element_type=jnp.float32
    ).reshape(concentration.shape)
    solid_flag = solid.astype(jnp.int32)
    flow_solid = lax.dynamic_slice_in_dim(solid, row_index * slab_depth, slab_depth, 1)
    flow = [flow_pops[member] for member in range(19)]
    scalars = concentration
    halos = None
    for time_step in range(STEPS):
        flow, motion = flow_collide(flow, flow_solid)
        column = gathered_copies(motion, "row", 2)
        mode = "first" if time_step == 0 else "middle"
        scalars = scalar_stage(mode, scalars, halos, column, solid_flag, source)
        halos = scalar_edges(scalars)
        from_below = send_vertical(edge_planes(flow, flow_vectors, 2, 1, 1), 1)
        from_above = send_vertical(edge_planes(flow, flow_vectors, 2, 1, -1), -1)
        flow = displace(flow, flow_vectors, 2, 1, from_below, from_above)
        flow = flow_section(flow, 1, 0, send_spanwise, keep_spanwise)
        flow = flow_section(flow, 0, 2, send_streamwise, inflow_fill)
    amount = scalar_stage("final", scalars, halos, None, None, None)
    stacked = jnp.stack(flow)
    return (stacked, amount)


def solution(mesh):
    in_specs = (
        P(None, "gy", "row", "gx"),
        P("row", "gy", None, "gx"),
        P("gy", None, "gx"),
        P(),
        P(),
        P(),
    )
    out_specs = (P(None, "gy", "row", "gx"), P("row", "gy", None, "gx"))
    return jax.shard_map(
        on_device, mesh=mesh, in_specs=in_specs, out_specs=out_specs, check_vma=False
    )
```

```python
import math

import jax
import jax.numpy as jnp
from jax import lax
from jax.sharding import PartitionSpec as P
from jax.experimental import pallas as pl
from jax.experimental.pallas import tpu as pltpu

STEPS = 3


flow_vectors = (
    (0, 0, 0),
    (1, 0, 0),
    (-1, 0, 0),
    (0, 1, 0),
    (0, -1, 0),
    (0, 0, 1),
    (0, 0, -1),
    (1, 1, 0),
    (-1, -1, 0),
    (1, -1, 0),
    (-1, 1, 0),
    (1, 0, 1),
    (-1, 0, -1),
    (1, 0, -1),
    (-1, 0, 1),
    (0, 1, 1),
    (0, -1, -1),
    (0, 1, -1),
    (0, -1, 1),
)
scalar_vectors = flow_vectors[:7]
flow_weights = (1.0 / 3.0,) + (1.0 / 18.0,) * 6 + (1.0 / 36.0,) * 12
flow_mirror = (0, 2, 1, 4, 3, 6, 5, 8, 7, 10, 9, 12, 11, 14, 13, 16, 15, 18, 17)
scalar_weights = (0.25,) + (0.125,) * 6
tau_base = 0.52
smag_const = 0.17
tau_scalar_base = 0.55
schmidt_turb = 0.7
inflow_speed = 0.08


def passed_along(block, axis, distance):
    devices = range(lax.axis_size(axis))
    route = [(i - distance, i) for i in devices if i - distance in devices]
    return lax.ppermute(block, axis, route)


def from_behind(value, axis, steps):
    count = lax.axis_size(axis)
    pairs = [(source, (source + steps) % count) for source in range(count)]
    return lax.ppermute(value, axis, pairs)


def in_order(tiles, dim):
    tiles = jnp.moveaxis(tiles, 0, dim)
    shape = tiles.shape
    return tiles.reshape(*shape[:dim], shape[dim] * shape[dim + 1], *shape[dim + 2 :])


def copy_for_each(x, axis):
    copies = jnp.broadcast_to(x, (lax.axis_size(axis), *x.shape))
    return lax.all_to_all(copies, axis, split_axis=0, concat_axis=0, tiled=True)


def gathered_copies(x, axis, dim):
    return in_order(copy_for_each(x, axis), dim)


def far_field(member):
    along = flow_vectors[member][0] * inflow_speed
    return flow_weights[member] * (
        1.0 + 3.0 * along + 4.5 * along * along - 1.5 * inflow_speed * inflow_speed
    )


def flow_collide(populations, solid):
    density = populations[0]
    for member in range(1, 19):
        density = density + populations[member]
    speeds = []
    for component in range(3):
        moment = jnp.zeros_like(density)
        for member in range(19):
            factor = flow_vectors[member][component]
            if factor != 0:
                moment = moment + factor * populations[member]
        speeds.append(moment / density)
    square = speeds[0] * speeds[0] + speeds[1] * speeds[1] + speeds[2] * speeds[2]
    equilibria = []
    for member in range(19):
        vector = flow_vectors[member]
        project = vector[0] * speeds[0] + vector[1] * speeds[1] + vector[2] * speeds[2]
        equilibria.append(
            flow_weights[member]
            * density
            * (1.0 + 3.0 * project + 4.5 * project * project - 1.5 * square)
        )
    stress = jnp.zeros_like(density)
    for first_axis in range(3):
        for second_axis in range(3):
            tensor = jnp.zeros_like(density)
            for member in range(19):
                factor = flow_vectors[member][first_axis] * flow_vectors[member][second_axis]
                if factor != 0:
                    tensor = tensor + factor * (populations[member] - equilibria[member])
            stress = stress + tensor * tensor
    relaxation = 0.5 * (
        tau_base
        + jnp.sqrt(
            tau_base * tau_base
            + 18.0 * math.sqrt(2.0) * smag_const * smag_const * jnp.sqrt(stress) / density
        )
    )
    eddy = (relaxation - tau_base) / 3.0
    fluid_part = jnp.where(solid, jnp.zeros_like(density), jnp.ones_like(density))
    updated = []
    for member in range(19):
        relaxed = populations[member] - (populations[member] - equilibria[member]) / relaxation
        updated.append(jnp.where(solid, populations[flow_mirror[member]], relaxed))
    motion = jnp.stack(
        [speeds[0] * fluid_part, speeds[1] * fluid_part, speeds[2] * fluid_part, eddy * fluid_part]
    )
    return (updated, motion)


def scalar_collide(scalar, motion, solid, source):
    amount = scalar[0]
    for member in range(1, 7):
        amount = amount + scalar[member]
    relaxation = tau_scalar_base + 4.0 * motion[3] / schmidt_turb
    updated = []
    for member in range(7):
        vector = flow_vectors[member]
        project = vector[0] * motion[0] + vector[1] * motion[1] + vector[2] * motion[2]
        equilibrium = scalar_weights[member] * amount * (1.0 + 4.0 * project)
        relaxed = (
            scalar[member]
            - (scalar[member] - equilibrium) / relaxation
            + scalar_weights[member] * source
        )
        updated.append(jnp.where(solid, scalar[flow_mirror[member]], relaxed))
    return updated


def edge_planes(pieces, vectors, component, dimension, heading):
    planes = []
    for member in range(len(pieces)):
        if vectors[member][component] == heading:
            length = pieces[member].shape[dimension]
            position = length - 1 if heading == 1 else 0
            planes.append(lax.index_in_dim(pieces[member], position, dimension, keepdims=False))
    return jnp.stack(planes)


def displace(pieces, vectors, component, dimension, from_low, from_high):
    result = []
    low_count = 0
    high_count = 0
    for member in range(len(pieces)):
        piece = pieces[member]
        length = piece.shape[dimension]
        heading = vectors[member][component]
        if heading == 1:
            entering = jnp.expand_dims(from_low[low_count], dimension)
            low_count = low_count + 1
            result.append(
                jnp.concatenate(
                    [entering, lax.slice_in_dim(piece, 0, length - 1, axis=dimension)], dimension
                )
            )
        elif heading == -1:
            entering = jnp.expand_dims(from_high[high_count], dimension)
            high_count = high_count + 1
            result.append(
                jnp.concatenate(
                    [lax.slice_in_dim(piece, 1, length, axis=dimension), entering], dimension
                )
            )
        else:
            result.append(piece)
    return result


def local_vertical(pieces, vectors, dimension):
    from_low = jnp.zeros_like(edge_planes(pieces, vectors, 2, dimension, 1))
    from_high = jnp.zeros_like(edge_planes(pieces, vectors, 2, dimension, -1))
    return displace(pieces, vectors, 2, dimension, from_low, from_high)


def send_vertical(planes, offset):
    return passed_along(planes, "row", offset)


def send_spanwise(packed, offset):
    return from_behind(packed, "gy", offset)


def send_streamwise(packed, offset):
    return passed_along(packed, "gx", offset)


def keep_spanwise(flow_in, heading):
    return flow_in


def inflow_fill(flow_in, heading):
    boundary = 0 if heading == 1 else lax.axis_size("gx") - 1
    members = [member for member in range(19) if flow_vectors[member][0] == heading]
    values = jnp.array([far_field(member) for member in members], jnp.float32).reshape(-1, 1, 1)
    return jnp.where(lax.axis_index("gx") == boundary, values + jnp.zeros_like(flow_in), flow_in)


def cross_section(flow, scalar, component, flow_dim, sender, edge_fill, keep_rows):
    arrived_flow = {}
    arrived_scalar = {}
    for heading in (1, -1):
        flow_planes = edge_planes(flow, flow_vectors, component, flow_dim, heading)
        scalar_planes = edge_planes(scalar, scalar_vectors, component, flow_dim + 1, heading)
        if keep_rows:
            width = flow_planes.shape[-1]
            packed = jnp.concatenate(
                [flow_planes.reshape(-1, width), scalar_planes.reshape(-1, width)], 0
            )
            split_at = flow_planes.size // width
        else:
            packed = jnp.concatenate([flow_planes.reshape(-1), scalar_planes.reshape(-1)], 0)
            split_at = flow_planes.size
        arrived = sender(packed, heading)
        arrived_flow[heading] = edge_fill(arrived[:split_at].reshape(flow_planes.shape), heading)
        arrived_scalar[heading] = arrived[split_at:].reshape(scalar_planes.shape)
    flow = displace(flow, flow_vectors, component, flow_dim, arrived_flow[1], arrived_flow[-1])
    scalar = displace(
        scalar, scalar_vectors, component, flow_dim + 1, arrived_scalar[1], arrived_scalar[-1]
    )
    return (flow, scalar)


def scalar_kernel(mode, span_y, depth, span_x):
    def body(*refs):
        if mode == "first":
            conc_ref, motion_ref, solid_ref, source_ref, out_ref = refs
        elif mode == "middle":
            (g_ref, lo_x_ref, hi_x_ref, lo_y_ref, hi_y_ref,
             motion_ref, solid_ref, source_ref, out_ref) = refs
        else:
            g_ref, lo_x_ref, hi_x_ref, lo_y_ref, hi_y_ref, out_ref = refs
        lane = lax.broadcasted_iota(jnp.int32, (depth, span_x), 1)
        level = lax.broadcasted_iota(jnp.int32, (depth, span_x), 0)
        for y in range(span_y):
            if mode == "first":
                block = conc_ref[0, y]
                scalar = [scalar_weights[member] * block for member in range(7)]
            else:
                moved_x = pltpu.roll(g_ref[1, 0, y], 1, 1)
                back_x = pltpu.roll(g_ref[2, 0, y], span_x - 1, 1)
                moved_z = pltpu.roll(g_ref[5, 0, y], 1, 0)
                back_z = pltpu.roll(g_ref[6, 0, y], depth - 1, 0)
                scalar = [
                    g_ref[0, 0, y],
                    jnp.where(lane == 0, lo_x_ref[0, y], moved_x),
                    jnp.where(lane == span_x - 1, hi_x_ref[0, y], back_x),
                    g_ref[3, 0, y - 1] if y > 0 else lo_y_ref[0],
                    g_ref[4, 0, y + 1] if y < span_y - 1 else hi_y_ref[0],
                    jnp.where(level == 0, 0.0, moved_z),
                    jnp.where(level == depth - 1, 0.0, back_z),
                ]
            amount = scalar[0]
            for member in range(1, 7):
                amount = amount + scalar[member]
            if mode == "final":
                out_ref[0, y] = amount
                continue
            speeds = [motion_ref[component, y] for component in range(3)]
            relaxation = tau_scalar_base + 4.0 * motion_ref[3, y] / schmidt_turb
            solid = solid_ref[y] != 0
            source = source_ref[0, y]
            for member in range(7):
                vector = flow_vectors[member]
                project = vector[0] * speeds[0] + vector[1] * speeds[1] + vector[2] * speeds[2]
                equilibrium = scalar_weights[member] * amount * (1.0 + 4.0 * project)
                relaxed = (
                    scalar[member]
                    - (scalar[member] - equilibrium) / relaxation
                    + scalar_weights[member] * source
                )
                out_ref[member, 0, y] = jnp.where(solid, scalar[flow_mirror[member]], relaxed)

    return body


def scalar_stage(mode, scalars, halos, motion, solid, source):
    count, span_y, depth, span_x = source.shape if source is not None else scalars.shape[1:]
    whole = lambda shape: pl.BlockSpec(shape, lambda s: (0,) * len(shape))
    one = lambda shape: pl.BlockSpec(shape, lambda s: (s,) + (0,) * (len(shape) - 1))
    stacked = pl.BlockSpec((7, 1, span_y, depth, span_x), lambda s: (0, s, 0, 0, 0))
    cells = (span_y, depth, span_x)
    edge_specs = [one((1, span_y, depth, 1))] * 2 + [one((1, depth, span_x))] * 2
    if mode == "first":
        operands = [scalars, motion, solid, source]
        specs = [one((1,) + cells), whole((4,) + cells), whole(cells), one((1,) + cells)]
    elif mode == "middle":
        operands = [scalars, *halos, motion, solid, source]
        specs = [stacked] + edge_specs + [whole((4,) + cells), whole(cells), one((1,) + cells)]
    else:
        operands = [scalars, *halos]
        specs = [stacked] + edge_specs
    if mode == "final":
        out_spec = one((1,) + cells)
        out_shape = jax.ShapeDtypeStruct((count,) + cells, jnp.float32)
    else:
        out_spec = stacked
        out_shape = jax.ShapeDtypeStruct((7, count) + cells, jnp.float32)
    return pl.pallas_call(
        scalar_kernel(mode, span_y, depth, span_x),
        grid=(count,),
        in_specs=specs,
        out_specs=out_spec,
        out_shape=out_shape,
    )(*operands)


def packed_section(flow, scalar_out, component, flow_dim, sender, edge_fill, keep_rows):
    arrived_flow = {}
    arrived_scalar = {}
    for heading in (1, -1):
        flow_planes = edge_planes(flow, flow_vectors, component, flow_dim, heading)
        scalar_planes = scalar_out[heading]
        if keep_rows:
            width = flow_planes.shape[-1]
            packed = jnp.concatenate(
                [flow_planes.reshape(-1, width), scalar_planes.reshape(-1, width)], 0
            )
            split_at = flow_planes.size // width
        else:
            packed = jnp.concatenate([flow_planes.reshape(-1), scalar_planes.reshape(-1)], 0)
            split_at = flow_planes.size
        arrived = sender(packed, heading)
        arrived_flow[heading] = edge_fill(arrived[:split_at].reshape(flow_planes.shape), heading)
        arrived_scalar[heading] = arrived[split_at:].reshape(scalar_planes.shape)
    flow = displace(flow, flow_vectors, component, flow_dim, arrived_flow[1], arrived_flow[-1])
    return (flow, arrived_scalar)


def flow_section(flow, component, flow_dim, sender, edge_fill):
    arrived = {}
    for heading in (1, -1):
        planes = edge_planes(flow, flow_vectors, component, flow_dim, heading)
        arrived[heading] = edge_fill(sender(planes, heading), heading)
    return displace(flow, flow_vectors, component, flow_dim, arrived[1], arrived[-1])


def on_device(flow_pops, concentration, solid_mask, source_cell, source_scalar, source_rate):
    row_index = lax.axis_index("row")
    slab_depth = flow_pops.shape[2]
    scalars_here, span_y, depth, span_x = concentration.shape
    height = lax.broadcasted_iota(jnp.int32, solid_mask.shape, 1)
    solid = (solid_mask == 1) | (height == 0) | (height == depth - 1)
    total_x = span_x * lax.axis_size("gx")
    cell_y = source_cell // (depth * total_x)
    cell_z = source_cell // total_x % depth
    cell_x = source_cell % total_x
    local_y = cell_y - lax.axis_index("gy") * span_y
    local_x = cell_x - lax.axis_index("gx") * span_x
    local_scalar = source_scalar - row_index * scalars_here
    count = source_cell.shape[0]
    plane_shape = (scalars_here, span_y, depth, count)
    hit = (
        (lax.broadcasted_iota(jnp.int32, plane_shape, 0) == local_scalar)
        & (lax.broadcasted_iota(jnp.int32, plane_shape, 1) == local_y)
        & (lax.broadcasted_iota(jnp.int32, plane_shape, 2) == cell_z)
    )
    weights = jnp.where(hit, source_rate, 0.0).reshape(-1, count)
    columns = (
        lax.broadcasted_iota(jnp.int32, (count, span_x), 1) == local_x[:, None]
    ).astype(jnp.float32)
    source = jnp.dot(
        weights, columns, precision=lax.Precision.HIGHEST, preferred_element_type=jnp.float32
    ).reshape(concentration.shape)
    solid_flag = solid.astype(jnp.int32)
    flow_solid = lax.dynamic_slice_in_dim(solid, row_index * slab_depth, slab_depth, 1)
    flow = [flow_pops[member] for member in range(19)]
    scalars = concentration
    halos = None
    for time_step in range(STEPS):
        flow, motion = flow_collide(flow, flow_solid)
        column = gathered_copies(motion, "row", 2)
        mode = "first" if time_step == 0 else "middle"
        scalars = scalar_stage(mode, scalars, halos, column, solid_flag, source)
        from_below = send_vertical(edge_planes(flow, flow_vectors, 2, 1, 1), 1)
        from_above = send_vertical(edge_planes(flow, flow_vectors, 2, 1, -1), -1)
        flow = displace(flow, flow_vectors, 2, 1, from_below, from_above)
        leaving_y = {1: scalars[3, :, span_y - 1], -1: scalars[4, :, 0]}
        flow, arrived_y = packed_section(flow, leaving_y, 1, 0, send_spanwise, keep_spanwise, True)
        leaving_x = {1: scalars[1, :, :, :, span_x - 1 :], -1: scalars[2, :, :, :, :1]}
        flow, arrived_x = packed_section(flow, leaving_x, 0, 2, send_streamwise, inflow_fill, False)
        halos = (arrived_x[1], arrived_x[-1], arrived_y[1], arrived_y[-1])
    amount = scalar_stage("final", scalars, halos, None, None, None)
    stacked = jnp.stack(flow)
    return (stacked, amount)


def solution(mesh):
    in_specs = (
        P(None, "gy", "row", "gx"),
        P("row", "gy", None, "gx"),
        P("gy", None, "gx"),
        P(),
        P(),
        P(),
    )
    out_specs = (P(None, "gy", "row", "gx"), P("row", "gy", None, "gx"))
    return jax.shard_map(
        on_device, mesh=mesh, in_specs=in_specs, out_specs=out_specs, check_vma=False
    )
```

```python
import math

import jax
import jax.numpy as jnp
from jax import lax
from jax.sharding import PartitionSpec as P
from jax.experimental import pallas as pl
from jax.experimental.pallas import tpu as pltpu

STEPS = 3


flow_vectors = (
    (0, 0, 0),
    (1, 0, 0),
    (-1, 0, 0),
    (0, 1, 0),
    (0, -1, 0),
    (0, 0, 1),
    (0, 0, -1),
    (1, 1, 0),
    (-1, -1, 0),
    (1, -1, 0),
    (-1, 1, 0),
    (1, 0, 1),
    (-1, 0, -1),
    (1, 0, -1),
    (-1, 0, 1),
    (0, 1, 1),
    (0, -1, -1),
    (0, 1, -1),
    (0, -1, 1),
)
scalar_vectors = flow_vectors[:7]
flow_weights = (1.0 / 3.0,) + (1.0 / 18.0,) * 6 + (1.0 / 36.0,) * 12
flow_mirror = (0, 2, 1, 4, 3, 6, 5, 8, 7, 10, 9, 12, 11, 14, 13, 16, 15, 18, 17)
scalar_weights = (0.25,) + (0.125,) * 6
tau_base = 0.52
smag_const = 0.17
tau_scalar_base = 0.55
schmidt_turb = 0.7
inflow_speed = 0.08


def passed_along(block, axis, distance):
    devices = range(lax.axis_size(axis))
    route = [(i - distance, i) for i in devices if i - distance in devices]
    return lax.ppermute(block, axis, route)


def from_behind(value, axis, steps):
    count = lax.axis_size(axis)
    pairs = [(source, (source + steps) % count) for source in range(count)]
    return lax.ppermute(value, axis, pairs)


def in_order(tiles, dim):
    tiles = jnp.moveaxis(tiles, 0, dim)
    shape = tiles.shape
    return tiles.reshape(*shape[:dim], shape[dim] * shape[dim + 1], *shape[dim + 2 :])


def copy_for_each(x, axis):
    copies = jnp.broadcast_to(x, (lax.axis_size(axis), *x.shape))
    return lax.all_to_all(copies, axis, split_axis=0, concat_axis=0, tiled=True)


def gathered_copies(x, axis, dim):
    return in_order(copy_for_each(x, axis), dim)


def far_field(member):
    along = flow_vectors[member][0] * inflow_speed
    return flow_weights[member] * (
        1.0 + 3.0 * along + 4.5 * along * along - 1.5 * inflow_speed * inflow_speed
    )


def flow_collide(populations, solid):
    density = populations[0]
    for member in range(1, 19):
        density = density + populations[member]
    speeds = []
    for component in range(3):
        moment = jnp.zeros_like(density)
        for member in range(19):
            factor = flow_vectors[member][component]
            if factor != 0:
                moment = moment + factor * populations[member]
        speeds.append(moment / density)
    square = speeds[0] * speeds[0] + speeds[1] * speeds[1] + speeds[2] * speeds[2]
    equilibria = []
    for member in range(19):
        vector = flow_vectors[member]
        project = vector[0] * speeds[0] + vector[1] * speeds[1] + vector[2] * speeds[2]
        equilibria.append(
            flow_weights[member]
            * density
            * (1.0 + 3.0 * project + 4.5 * project * project - 1.5 * square)
        )
    stress = jnp.zeros_like(density)
    for first_axis in range(3):
        for second_axis in range(3):
            tensor = jnp.zeros_like(density)
            for member in range(19):
                factor = flow_vectors[member][first_axis] * flow_vectors[member][second_axis]
                if factor != 0:
                    tensor = tensor + factor * (populations[member] - equilibria[member])
            stress = stress + tensor * tensor
    relaxation = 0.5 * (
        tau_base
        + jnp.sqrt(
            tau_base * tau_base
            + 18.0 * math.sqrt(2.0) * smag_const * smag_const * jnp.sqrt(stress) / density
        )
    )
    eddy = (relaxation - tau_base) / 3.0
    fluid_part = jnp.where(solid, jnp.zeros_like(density), jnp.ones_like(density))
    updated = []
    for member in range(19):
        relaxed = populations[member] - (populations[member] - equilibria[member]) / relaxation
        updated.append(jnp.where(solid, populations[flow_mirror[member]], relaxed))
    motion = jnp.stack(
        [speeds[0] * fluid_part, speeds[1] * fluid_part, speeds[2] * fluid_part, eddy * fluid_part]
    )
    return (updated, motion)


def scalar_collide(scalar, motion, solid, source):
    amount = scalar[0]
    for member in range(1, 7):
        amount = amount + scalar[member]
    relaxation = tau_scalar_base + 4.0 * motion[3] / schmidt_turb
    updated = []
    for member in range(7):
        vector = flow_vectors[member]
        project = vector[0] * motion[0] + vector[1] * motion[1] + vector[2] * motion[2]
        equilibrium = scalar_weights[member] * amount * (1.0 + 4.0 * project)
        relaxed = (
            scalar[member]
            - (scalar[member] - equilibrium) / relaxation
            + scalar_weights[member] * source
        )
        updated.append(jnp.where(solid, scalar[flow_mirror[member]], relaxed))
    return updated


def edge_planes(pieces, vectors, component, dimension, heading):
    planes = []
    for member in range(len(pieces)):
        if vectors[member][component] == heading:
            length = pieces[member].shape[dimension]
            position = length - 1 if heading == 1 else 0
            planes.append(lax.index_in_dim(pieces[member], position, dimension, keepdims=False))
    return jnp.stack(planes)


def displace(pieces, vectors, component, dimension, from_low, from_high):
    result = []
    low_count = 0
    high_count = 0
    for member in range(len(pieces)):
        piece = pieces[member]
        length = piece.shape[dimension]
        heading = vectors[member][component]
        if heading == 1:
            entering = jnp.expand_dims(from_low[low_count], dimension)
            low_count = low_count + 1
            result.append(
                jnp.concatenate(
                    [entering, lax.slice_in_dim(piece, 0, length - 1, axis=dimension)], dimension
                )
            )
        elif heading == -1:
            entering = jnp.expand_dims(from_high[high_count], dimension)
            high_count = high_count + 1
            result.append(
                jnp.concatenate(
                    [lax.slice_in_dim(piece, 1, length, axis=dimension), entering], dimension
                )
            )
        else:
            result.append(piece)
    return result


def local_vertical(pieces, vectors, dimension):
    from_low = jnp.zeros_like(edge_planes(pieces, vectors, 2, dimension, 1))
    from_high = jnp.zeros_like(edge_planes(pieces, vectors, 2, dimension, -1))
    return displace(pieces, vectors, 2, dimension, from_low, from_high)


def send_vertical(planes, offset):
    return passed_along(planes, "row", offset)


def send_spanwise(packed, offset):
    return from_behind(packed, "gy", offset)


def send_streamwise(packed, offset):
    return passed_along(packed, "gx", offset)


def keep_spanwise(flow_in, heading):
    return flow_in


def inflow_fill(flow_in, heading):
    boundary = 0 if heading == 1 else lax.axis_size("gx") - 1
    members = [member for member in range(19) if flow_vectors[member][0] == heading]
    values = jnp.array([far_field(member) for member in members], jnp.float32).reshape(-1, 1, 1)
    return jnp.where(lax.axis_index("gx") == boundary, values + jnp.zeros_like(flow_in), flow_in)


def cross_section(flow, scalar, component, flow_dim, sender, edge_fill, keep_rows):
    arrived_flow = {}
    arrived_scalar = {}
    for heading in (1, -1):
        flow_planes = edge_planes(flow, flow_vectors, component, flow_dim, heading)
        scalar_planes = edge_planes(scalar, scalar_vectors, component, flow_dim + 1, heading)
        if keep_rows:
            width = flow_planes.shape[-1]
            packed = jnp.concatenate(
                [flow_planes.reshape(-1, width), scalar_planes.reshape(-1, width)], 0
            )
            split_at = flow_planes.size // width
        else:
            packed = jnp.concatenate([flow_planes.reshape(-1), scalar_planes.reshape(-1)], 0)
            split_at = flow_planes.size
        arrived = sender(packed, heading)
        arrived_flow[heading] = edge_fill(arrived[:split_at].reshape(flow_planes.shape), heading)
        arrived_scalar[heading] = arrived[split_at:].reshape(scalar_planes.shape)
    flow = displace(flow, flow_vectors, component, flow_dim, arrived_flow[1], arrived_flow[-1])
    scalar = displace(
        scalar, scalar_vectors, component, flow_dim + 1, arrived_scalar[1], arrived_scalar[-1]
    )
    return (flow, scalar)


def scalar_kernel(mode, span_y, depth, span_x):
    def body(*refs):
        if mode == "first":
            conc_ref, motion_ref, solid_ref, source_ref, out_ref = refs
        elif mode == "middle":
            (g_ref, lo_x_ref, hi_x_ref, lo_y_ref, hi_y_ref,
             motion_ref, solid_ref, source_ref, out_ref) = refs
        else:
            g_ref, lo_x_ref, hi_x_ref, lo_y_ref, hi_y_ref, out_ref = refs
        lane = lax.broadcasted_iota(jnp.int32, (depth, span_x), 1)
        level = lax.broadcasted_iota(jnp.int32, (depth, span_x), 0)
        for y in range(span_y):
            if mode == "first":
                block = conc_ref[0, y]
                scalar = [scalar_weights[member] * block for member in range(7)]
            else:
                moved_x = pltpu.roll(g_ref[1, 0, y], 1, 1)
                back_x = pltpu.roll(g_ref[2, 0, y], span_x - 1, 1)
                moved_z = pltpu.roll(g_ref[5, 0, y], 1, 0)
                back_z = pltpu.roll(g_ref[6, 0, y], depth - 1, 0)
                scalar = [
                    g_ref[0, 0, y],
                    jnp.where(lane == 0, lo_x_ref[0, y], moved_x),
                    jnp.where(lane == span_x - 1, hi_x_ref[0, y], back_x),
                    g_ref[3, 0, y - 1] if y > 0 else lo_y_ref[0],
                    g_ref[4, 0, y + 1] if y < span_y - 1 else hi_y_ref[0],
                    jnp.where(level == 0, 0.0, moved_z),
                    jnp.where(level == depth - 1, 0.0, back_z),
                ]
            amount = scalar[0]
            for member in range(1, 7):
                amount = amount + scalar[member]
            if mode == "final":
                out_ref[0, y] = amount
                continue
            speeds = [motion_ref[component, y] for component in range(3)]
            relaxation = tau_scalar_base + 4.0 * motion_ref[3, y] / schmidt_turb
            solid = solid_ref[y] != 0
            source = source_ref[0, y]
            for member in range(7):
                vector = flow_vectors[member]
                project = vector[0] * speeds[0] + vector[1] * speeds[1] + vector[2] * speeds[2]
                equilibrium = scalar_weights[member] * amount * (1.0 + 4.0 * project)
                relaxed = (
                    scalar[member]
                    - (scalar[member] - equilibrium) / relaxation
                    + scalar_weights[member] * source
                )
                out_ref[member, 0, y] = jnp.where(solid, scalar[flow_mirror[member]], relaxed)

    return body


def scalar_stage(mode, scalars, halos, motion, solid, source):
    count, span_y, depth, span_x = source.shape if source is not None else scalars.shape[1:]
    whole = lambda shape: pl.BlockSpec(shape, lambda s: (0,) * len(shape))
    one = lambda shape: pl.BlockSpec(shape, lambda s: (s,) + (0,) * (len(shape) - 1))
    stacked = pl.BlockSpec((7, 1, span_y, depth, span_x), lambda s: (0, s, 0, 0, 0))
    cells = (span_y, depth, span_x)
    edge_specs = [one((1, span_y, depth, 1))] * 2 + [one((1, depth, span_x))] * 2
    if mode == "first":
        operands = [scalars, motion, solid, source]
        specs = [one((1,) + cells), whole((4,) + cells), whole(cells), one((1,) + cells)]
    elif mode == "middle":
        operands = [scalars, *halos, motion, solid, source]
        specs = [stacked] + edge_specs + [whole((4,) + cells), whole(cells), one((1,) + cells)]
    else:
        operands = [scalars, *halos]
        specs = [stacked] + edge_specs
    if mode == "final":
        out_spec = one((1,) + cells)
        out_shape = jax.ShapeDtypeStruct((count,) + cells, jnp.float32)
    else:
        out_spec = stacked
        out_shape = jax.ShapeDtypeStruct((7, count) + cells, jnp.float32)
    return pl.pallas_call(
        scalar_kernel(mode, span_y, depth, span_x),
        grid=(count,),
        in_specs=specs,
        out_specs=out_spec,
        out_shape=out_shape,
    )(*operands)


def packed_section(flow, scalar_out, component, flow_dim, sender, edge_fill, keep_rows):
    arrived_flow = {}
    arrived_scalar = {}
    for heading in (1, -1):
        flow_planes = edge_planes(flow, flow_vectors, component, flow_dim, heading)
        scalar_planes = scalar_out[heading]
        if keep_rows:
            width = flow_planes.shape[-1]
            packed = jnp.concatenate(
                [flow_planes.reshape(-1, width), scalar_planes.reshape(-1, width)], 0
            )
            split_at = flow_planes.size // width
        else:
            packed = jnp.concatenate([flow_planes.reshape(-1), scalar_planes.reshape(-1)], 0)
            split_at = flow_planes.size
        arrived = sender(packed, heading)
        arrived_flow[heading] = edge_fill(arrived[:split_at].reshape(flow_planes.shape), heading)
        arrived_scalar[heading] = arrived[split_at:].reshape(scalar_planes.shape)
    flow = displace(flow, flow_vectors, component, flow_dim, arrived_flow[1], arrived_flow[-1])
    return (flow, arrived_scalar)


def flow_section(flow, component, flow_dim, sender, edge_fill):
    arrived = {}
    for heading in (1, -1):
        planes = edge_planes(flow, flow_vectors, component, flow_dim, heading)
        arrived[heading] = edge_fill(sender(planes, heading), heading)
    return displace(flow, flow_vectors, component, flow_dim, arrived[1], arrived[-1])


def on_device(flow_pops, concentration, solid_mask, source_cell, source_scalar, source_rate):
    row_index = lax.axis_index("row")
    slab_depth = flow_pops.shape[2]
    scalars_here, span_y, depth, span_x = concentration.shape
    height = lax.broadcasted_iota(jnp.int32, solid_mask.shape, 1)
    solid = (solid_mask == 1) | (height == 0) | (height == depth - 1)
    total_x = span_x * lax.axis_size("gx")
    cell_y = source_cell // (depth * total_x)
    cell_z = source_cell // total_x % depth
    cell_x = source_cell % total_x
    local_y = cell_y - lax.axis_index("gy") * span_y
    local_x = cell_x - lax.axis_index("gx") * span_x
    local_scalar = source_scalar - row_index * scalars_here
    count = source_cell.shape[0]
    plane_shape = (scalars_here, span_y, depth, count)
    hit = (
        (lax.broadcasted_iota(jnp.int32, plane_shape, 0) == local_scalar)
        & (lax.broadcasted_iota(jnp.int32, plane_shape, 1) == local_y)
        & (lax.broadcasted_iota(jnp.int32, plane_shape, 2) == cell_z)
    )
    weights = jnp.where(hit, source_rate, 0.0).reshape(-1, count)
    columns = (
        lax.broadcasted_iota(jnp.int32, (count, span_x), 1) == local_x[:, None]
    ).astype(jnp.float32)
    source = jnp.dot(
        weights, columns, precision=lax.Precision.HIGHEST, preferred_element_type=jnp.float32
    ).reshape(concentration.shape)
    solid_flag = solid.astype(jnp.int32)
    flow_solid = lax.dynamic_slice_in_dim(solid, row_index * slab_depth, slab_depth, 1)
    flow = [flow_pops[member] for member in range(19)]
    scalars = concentration
    halos = None
    for time_step in range(STEPS):
        flow, motion = flow_collide(flow, flow_solid)
        column = lax.all_gather(motion, "row", axis=2, tiled=True)
        mode = "first" if time_step == 0 else "middle"
        scalars = scalar_stage(mode, scalars, halos, column, solid_flag, source)
        from_below = send_vertical(edge_planes(flow, flow_vectors, 2, 1, 1), 1)
        from_above = send_vertical(edge_planes(flow, flow_vectors, 2, 1, -1), -1)
        flow = displace(flow, flow_vectors, 2, 1, from_below, from_above)
        leaving_y = {1: scalars[3, :, span_y - 1], -1: scalars[4, :, 0]}
        flow, arrived_y = packed_section(flow, leaving_y, 1, 0, send_spanwise, keep_spanwise, True)
        leaving_x = {1: scalars[1, :, :, :, span_x - 1 :], -1: scalars[2, :, :, :, :1]}
        flow, arrived_x = packed_section(flow, leaving_x, 0, 2, send_streamwise, inflow_fill, False)
        halos = (arrived_x[1], arrived_x[-1], arrived_y[1], arrived_y[-1])
    amount = scalar_stage("final", scalars, halos, None, None, None)
    stacked = jnp.stack(flow)
    return (stacked, amount)


def solution(mesh):
    in_specs = (
        P(None, "gy", "row", "gx"),
        P("row", "gy", None, "gx"),
        P("gy", None, "gx"),
        P(),
        P(),
        P(),
    )
    out_specs = (P(None, "gy", "row", "gx"), P("row", "gy", None, "gx"))
    return jax.shard_map(
        on_device, mesh=mesh, in_specs=in_specs, out_specs=out_specs, check_vma=False
    )
```

```python
import math

import jax
import jax.numpy as jnp
from jax import lax
from jax.sharding import PartitionSpec as P
from jax.experimental import pallas as pl
from jax.experimental.pallas import tpu as pltpu

STEPS = 3


flow_vectors = (
    (0, 0, 0),
    (1, 0, 0),
    (-1, 0, 0),
    (0, 1, 0),
    (0, -1, 0),
    (0, 0, 1),
    (0, 0, -1),
    (1, 1, 0),
    (-1, -1, 0),
    (1, -1, 0),
    (-1, 1, 0),
    (1, 0, 1),
    (-1, 0, -1),
    (1, 0, -1),
    (-1, 0, 1),
    (0, 1, 1),
    (0, -1, -1),
    (0, 1, -1),
    (0, -1, 1),
)
scalar_vectors = flow_vectors[:7]
flow_weights = (1.0 / 3.0,) + (1.0 / 18.0,) * 6 + (1.0 / 36.0,) * 12
flow_mirror = (0, 2, 1, 4, 3, 6, 5, 8, 7, 10, 9, 12, 11, 14, 13, 16, 15, 18, 17)
scalar_weights = (0.25,) + (0.125,) * 6
tau_base = 0.52
smag_const = 0.17
tau_scalar_base = 0.55
schmidt_turb = 0.7
inflow_speed = 0.08


def passed_along(block, axis, distance):
    devices = range(lax.axis_size(axis))
    route = [(i - distance, i) for i in devices if i - distance in devices]
    return lax.ppermute(block, axis, route)


def from_behind(value, axis, steps):
    count = lax.axis_size(axis)
    pairs = [(source, (source + steps) % count) for source in range(count)]
    return lax.ppermute(value, axis, pairs)


def in_order(tiles, dim):
    tiles = jnp.moveaxis(tiles, 0, dim)
    shape = tiles.shape
    return tiles.reshape(*shape[:dim], shape[dim] * shape[dim + 1], *shape[dim + 2 :])


def copy_for_each(x, axis):
    copies = jnp.broadcast_to(x, (lax.axis_size(axis), *x.shape))
    return lax.all_to_all(copies, axis, split_axis=0, concat_axis=0, tiled=True)


def gathered_copies(x, axis, dim):
    return in_order(copy_for_each(x, axis), dim)


def far_field(member):
    along = flow_vectors[member][0] * inflow_speed
    return flow_weights[member] * (
        1.0 + 3.0 * along + 4.5 * along * along - 1.5 * inflow_speed * inflow_speed
    )


def flow_collide(populations, solid):
    density = populations[0]
    for member in range(1, 19):
        density = density + populations[member]
    speeds = []
    for component in range(3):
        moment = jnp.zeros_like(density)
        for member in range(19):
            factor = flow_vectors[member][component]
            if factor != 0:
                moment = moment + factor * populations[member]
        speeds.append(moment / density)
    square = speeds[0] * speeds[0] + speeds[1] * speeds[1] + speeds[2] * speeds[2]
    equilibria = []
    for member in range(19):
        vector = flow_vectors[member]
        project = vector[0] * speeds[0] + vector[1] * speeds[1] + vector[2] * speeds[2]
        equilibria.append(
            flow_weights[member]
            * density
            * (1.0 + 3.0 * project + 4.5 * project * project - 1.5 * square)
        )
    stress = jnp.zeros_like(density)
    for first_axis in range(3):
        for second_axis in range(3):
            tensor = jnp.zeros_like(density)
            for member in range(19):
                factor = flow_vectors[member][first_axis] * flow_vectors[member][second_axis]
                if factor != 0:
                    tensor = tensor + factor * (populations[member] - equilibria[member])
            stress = stress + tensor * tensor
    relaxation = 0.5 * (
        tau_base
        + jnp.sqrt(
            tau_base * tau_base
            + 18.0 * math.sqrt(2.0) * smag_const * smag_const * jnp.sqrt(stress) / density
        )
    )
    eddy = (relaxation - tau_base) / 3.0
    fluid_part = jnp.where(solid, jnp.zeros_like(density), jnp.ones_like(density))
    updated = []
    for member in range(19):
        relaxed = populations[member] - (populations[member] - equilibria[member]) / relaxation
        updated.append(jnp.where(solid, populations[flow_mirror[member]], relaxed))
    motion = jnp.stack(
        [speeds[0] * fluid_part, speeds[1] * fluid_part, speeds[2] * fluid_part, eddy * fluid_part]
    )
    return (updated, motion)


def scalar_collide(scalar, motion, solid, source):
    amount = scalar[0]
    for member in range(1, 7):
        amount = amount + scalar[member]
    relaxation = tau_scalar_base + 4.0 * motion[3] / schmidt_turb
    updated = []
    for member in range(7):
        vector = flow_vectors[member]
        project = vector[0] * motion[0] + vector[1] * motion[1] + vector[2] * motion[2]
        equilibrium = scalar_weights[member] * amount * (1.0 + 4.0 * project)
        relaxed = (
            scalar[member]
            - (scalar[member] - equilibrium) / relaxation
            + scalar_weights[member] * source
        )
        updated.append(jnp.where(solid, scalar[flow_mirror[member]], relaxed))
    return updated


def edge_planes(pieces, vectors, component, dimension, heading):
    planes = []
    for member in range(len(pieces)):
        if vectors[member][component] == heading:
            length = pieces[member].shape[dimension]
            position = length - 1 if heading == 1 else 0
            planes.append(lax.index_in_dim(pieces[member], position, dimension, keepdims=False))
    return jnp.stack(planes)


def displace(pieces, vectors, component, dimension, from_low, from_high):
    result = []
    low_count = 0
    high_count = 0
    for member in range(len(pieces)):
        piece = pieces[member]
        length = piece.shape[dimension]
        heading = vectors[member][component]
        if heading == 1:
            entering = jnp.expand_dims(from_low[low_count], dimension)
            low_count = low_count + 1
            result.append(
                jnp.concatenate(
                    [entering, lax.slice_in_dim(piece, 0, length - 1, axis=dimension)], dimension
                )
            )
        elif heading == -1:
            entering = jnp.expand_dims(from_high[high_count], dimension)
            high_count = high_count + 1
            result.append(
                jnp.concatenate(
                    [lax.slice_in_dim(piece, 1, length, axis=dimension), entering], dimension
                )
            )
        else:
            result.append(piece)
    return result


def local_vertical(pieces, vectors, dimension):
    from_low = jnp.zeros_like(edge_planes(pieces, vectors, 2, dimension, 1))
    from_high = jnp.zeros_like(edge_planes(pieces, vectors, 2, dimension, -1))
    return displace(pieces, vectors, 2, dimension, from_low, from_high)


def send_vertical(planes, offset):
    return passed_along(planes, "row", offset)


def send_spanwise(packed, offset):
    return from_behind(packed, "gy", offset)


def send_streamwise(packed, offset):
    return passed_along(packed, "gx", offset)


def keep_spanwise(flow_in, heading):
    return flow_in


def inflow_fill(flow_in, heading):
    boundary = 0 if heading == 1 else lax.axis_size("gx") - 1
    members = [member for member in range(19) if flow_vectors[member][0] == heading]
    values = jnp.array([far_field(member) for member in members], jnp.float32).reshape(-1, 1, 1)
    return jnp.where(lax.axis_index("gx") == boundary, values + jnp.zeros_like(flow_in), flow_in)


def cross_section(flow, scalar, component, flow_dim, sender, edge_fill, keep_rows):
    arrived_flow = {}
    arrived_scalar = {}
    for heading in (1, -1):
        flow_planes = edge_planes(flow, flow_vectors, component, flow_dim, heading)
        scalar_planes = edge_planes(scalar, scalar_vectors, component, flow_dim + 1, heading)
        if keep_rows:
            width = flow_planes.shape[-1]
            packed = jnp.concatenate(
                [flow_planes.reshape(-1, width), scalar_planes.reshape(-1, width)], 0
            )
            split_at = flow_planes.size // width
        else:
            packed = jnp.concatenate([flow_planes.reshape(-1), scalar_planes.reshape(-1)], 0)
            split_at = flow_planes.size
        arrived = sender(packed, heading)
        arrived_flow[heading] = edge_fill(arrived[:split_at].reshape(flow_planes.shape), heading)
        arrived_scalar[heading] = arrived[split_at:].reshape(scalar_planes.shape)
    flow = displace(flow, flow_vectors, component, flow_dim, arrived_flow[1], arrived_flow[-1])
    scalar = displace(
        scalar, scalar_vectors, component, flow_dim + 1, arrived_scalar[1], arrived_scalar[-1]
    )
    return (flow, scalar)


def scalar_kernel(mode, span_y, depth, span_x):
    def body(*refs):
        if mode == "first":
            conc_ref, motion_ref, solid_ref, source_ref, out_ref = refs
        elif mode == "middle":
            (g_ref, lo_x_ref, hi_x_ref, lo_y_ref, hi_y_ref,
             motion_ref, solid_ref, source_ref, out_ref) = refs
        else:
            g_ref, lo_x_ref, hi_x_ref, lo_y_ref, hi_y_ref, out_ref = refs
        lane = lax.broadcasted_iota(jnp.int32, (depth, span_x), 1)
        level = lax.broadcasted_iota(jnp.int32, (depth, span_x), 0)
        for y in range(span_y):
            if mode == "first":
                block = conc_ref[0, y]
                scalar = [scalar_weights[member] * block for member in range(7)]
            else:
                moved_x = pltpu.roll(g_ref[1, 0, y], 1, 1)
                back_x = pltpu.roll(g_ref[2, 0, y], span_x - 1, 1)
                moved_z = pltpu.roll(g_ref[5, 0, y], 1, 0)
                back_z = pltpu.roll(g_ref[6, 0, y], depth - 1, 0)
                scalar = [
                    g_ref[0, 0, y],
                    jnp.where(lane == 0, lo_x_ref[0, y], moved_x),
                    jnp.where(lane == span_x - 1, hi_x_ref[0, y], back_x),
                    g_ref[3, 0, y - 1] if y > 0 else lo_y_ref[0],
                    g_ref[4, 0, y + 1] if y < span_y - 1 else hi_y_ref[0],
                    jnp.where(level == 0, 0.0, moved_z),
                    jnp.where(level == depth - 1, 0.0, back_z),
                ]
            amount = scalar[0]
            for member in range(1, 7):
                amount = amount + scalar[member]
            if mode == "final":
                out_ref[0, y] = amount
                continue
            speeds = [motion_ref[component, y] for component in range(3)]
            relaxation = tau_scalar_base + 4.0 * motion_ref[3, y] / schmidt_turb
            solid = solid_ref[y] != 0
            source = source_ref[0, y]
            for member in range(7):
                vector = flow_vectors[member]
                project = vector[0] * speeds[0] + vector[1] * speeds[1] + vector[2] * speeds[2]
                equilibrium = scalar_weights[member] * amount * (1.0 + 4.0 * project)
                relaxed = (
                    scalar[member]
                    - (scalar[member] - equilibrium) / relaxation
                    + scalar_weights[member] * source
                )
                out_ref[member, 0, y] = jnp.where(solid, scalar[flow_mirror[member]], relaxed)

    return body


def scalar_stage(mode, scalars, halos, motion, solid, source):
    count, span_y, depth, span_x = source.shape if source is not None else scalars.shape[1:]
    whole = lambda shape: pl.BlockSpec(shape, lambda s: (0,) * len(shape))
    one = lambda shape: pl.BlockSpec(shape, lambda s: (s,) + (0,) * (len(shape) - 1))
    stacked = pl.BlockSpec((7, 1, span_y, depth, span_x), lambda s: (0, s, 0, 0, 0))
    cells = (span_y, depth, span_x)
    edge_specs = [one((1, span_y, depth, 1))] * 2 + [one((1, depth, span_x))] * 2
    if mode == "first":
        operands = [scalars, motion, solid, source]
        specs = [one((1,) + cells), whole((4,) + cells), whole(cells), one((1,) + cells)]
    elif mode == "middle":
        operands = [scalars, *halos, motion, solid, source]
        specs = [stacked] + edge_specs + [whole((4,) + cells), whole(cells), one((1,) + cells)]
    else:
        operands = [scalars, *halos]
        specs = [stacked] + edge_specs
    if mode == "final":
        out_spec = one((1,) + cells)
        out_shape = jax.ShapeDtypeStruct((count,) + cells, jnp.float32)
    else:
        out_spec = stacked
        out_shape = jax.ShapeDtypeStruct((7, count) + cells, jnp.float32)
    return pl.pallas_call(
        scalar_kernel(mode, span_y, depth, span_x),
        grid=(count,),
        in_specs=specs,
        out_specs=out_spec,
        out_shape=out_shape,
    )(*operands)


def packed_section(flow, scalar_out, component, flow_dim, sender, edge_fill, keep_rows):
    arrived_flow = {}
    arrived_scalar = {}
    for heading in (1, -1):
        flow_planes = edge_planes(flow, flow_vectors, component, flow_dim, heading)
        scalar_planes = scalar_out[heading]
        if keep_rows:
            width = flow_planes.shape[-1]
            packed = jnp.concatenate(
                [flow_planes.reshape(-1, width), scalar_planes.reshape(-1, width)], 0
            )
            split_at = flow_planes.size // width
        else:
            packed = jnp.concatenate([flow_planes.reshape(-1), scalar_planes.reshape(-1)], 0)
            split_at = flow_planes.size
        arrived = sender(packed, heading)
        arrived_flow[heading] = edge_fill(arrived[:split_at].reshape(flow_planes.shape), heading)
        arrived_scalar[heading] = arrived[split_at:].reshape(scalar_planes.shape)
    flow = displace(flow, flow_vectors, component, flow_dim, arrived_flow[1], arrived_flow[-1])
    return (flow, arrived_scalar)


def flow_section(flow, component, flow_dim, sender, edge_fill):
    arrived = {}
    for heading in (1, -1):
        planes = edge_planes(flow, flow_vectors, component, flow_dim, heading)
        arrived[heading] = edge_fill(sender(planes, heading), heading)
    return displace(flow, flow_vectors, component, flow_dim, arrived[1], arrived[-1])


def on_device(flow_pops, concentration, solid_mask, source_cell, source_scalar, source_rate):
    row_index = lax.axis_index("row")
    slab_depth = flow_pops.shape[2]
    scalars_here, span_y, depth, span_x = concentration.shape
    height = lax.broadcasted_iota(jnp.int32, solid_mask.shape, 1)
    solid = (solid_mask == 1) | (height == 0) | (height == depth - 1)
    total_x = span_x * lax.axis_size("gx")
    cell_y = source_cell // (depth * total_x)
    cell_z = source_cell // total_x % depth
    cell_x = source_cell % total_x
    local_y = cell_y - lax.axis_index("gy") * span_y
    local_x = cell_x - lax.axis_index("gx") * span_x
    local_scalar = source_scalar - row_index * scalars_here
    count = source_cell.shape[0]
    plane_shape = (scalars_here, span_y, depth, count)
    hit = (
        (lax.broadcasted_iota(jnp.int32, plane_shape, 0) == local_scalar)
        & (lax.broadcasted_iota(jnp.int32, plane_shape, 1) == local_y)
        & (lax.broadcasted_iota(jnp.int32, plane_shape, 2) == cell_z)
    )
    weights = jnp.where(hit, source_rate, 0.0).reshape(-1, count)
    columns = (
        lax.broadcasted_iota(jnp.int32, (count, span_x), 1) == local_x[:, None]
    ).astype(jnp.float32)
    source = jnp.dot(
        weights, columns, precision=lax.Precision.HIGHEST, preferred_element_type=jnp.float32
    ).reshape(concentration.shape)
    solid_flag = solid.astype(jnp.int32)
    flow_solid = lax.dynamic_slice_in_dim(solid, row_index * slab_depth, slab_depth, 1)
    flow = [flow_pops[member] for member in range(19)]
    scalars = concentration
    halos = None
    leaving = None
    for time_step in range(STEPS):
        flow, motion = flow_collide(flow, flow_solid)
        column = gathered_copies(motion, "row", 2)
        from_below = send_vertical(edge_planes(flow, flow_vectors, 2, 1, 1), 1)
        from_above = send_vertical(edge_planes(flow, flow_vectors, 2, 1, -1), -1)
        flow = displace(flow, flow_vectors, 2, 1, from_below, from_above)
        if leaving is None:
            flow = flow_section(flow, 1, 0, send_spanwise, keep_spanwise)
            flow = flow_section(flow, 0, 2, send_streamwise, inflow_fill)
            scalars = scalar_stage("first", scalars, None, column, solid_flag, source)
        else:
            flow, arrived_y = packed_section(
                flow, leaving[1], 1, 0, send_spanwise, keep_spanwise, True
            )
            flow, arrived_x = packed_section(
                flow, leaving[0], 0, 2, send_streamwise, inflow_fill, False
            )
            halos = (arrived_x[1], arrived_x[-1], arrived_y[1], arrived_y[-1])
            scalars = scalar_stage("middle", scalars, halos, column, solid_flag, source)
        leaving = (
            {1: scalars[1, :, :, :, span_x - 1 :], -1: scalars[2, :, :, :, :1]},
            {1: scalars[3, :, span_y - 1], -1: scalars[4, :, 0]},
        )
    halos = (
        send_streamwise(leaving[0][1], 1),
        send_streamwise(leaving[0][-1], -1),
        send_spanwise(leaving[1][1], 1),
        send_spanwise(leaving[1][-1], -1),
    )
    amount = scalar_stage("final", scalars, halos, None, None, None)
    stacked = jnp.stack(flow)
    return (stacked, amount)


def solution(mesh):
    in_specs = (
        P(None, "gy", "row", "gx"),
        P("row", "gy", None, "gx"),
        P("gy", None, "gx"),
        P(),
        P(),
        P(),
    )
    out_specs = (P(None, "gy", "row", "gx"), P("row", "gy", None, "gx"))
    return jax.shard_map(
        on_device, mesh=mesh, in_specs=in_specs, out_specs=out_specs, check_vma=False
    )
```

```python
import math

import jax
import jax.numpy as jnp
from jax import lax
from jax.sharding import PartitionSpec as P
from jax.experimental import pallas as pl
from jax.experimental.pallas import tpu as pltpu

STEPS = 3


flow_vectors = (
    (0, 0, 0),
    (1, 0, 0),
    (-1, 0, 0),
    (0, 1, 0),
    (0, -1, 0),
    (0, 0, 1),
    (0, 0, -1),
    (1, 1, 0),
    (-1, -1, 0),
    (1, -1, 0),
    (-1, 1, 0),
    (1, 0, 1),
    (-1, 0, -1),
    (1, 0, -1),
    (-1, 0, 1),
    (0, 1, 1),
    (0, -1, -1),
    (0, 1, -1),
    (0, -1, 1),
)
scalar_vectors = flow_vectors[:7]
flow_weights = (1.0 / 3.0,) + (1.0 / 18.0,) * 6 + (1.0 / 36.0,) * 12
flow_mirror = (0, 2, 1, 4, 3, 6, 5, 8, 7, 10, 9, 12, 11, 14, 13, 16, 15, 18, 17)
scalar_weights = (0.25,) + (0.125,) * 6
tau_base = 0.52
smag_const = 0.17
tau_scalar_base = 0.55
schmidt_turb = 0.7
inflow_speed = 0.08


def passed_along(block, axis, distance):
    devices = range(lax.axis_size(axis))
    route = [(i - distance, i) for i in devices if i - distance in devices]
    return lax.ppermute(block, axis, route)


def from_behind(value, axis, steps):
    count = lax.axis_size(axis)
    pairs = [(source, (source + steps) % count) for source in range(count)]
    return lax.ppermute(value, axis, pairs)


def in_order(tiles, dim):
    tiles = jnp.moveaxis(tiles, 0, dim)
    shape = tiles.shape
    return tiles.reshape(*shape[:dim], shape[dim] * shape[dim + 1], *shape[dim + 2 :])


def copy_for_each(x, axis):
    copies = jnp.broadcast_to(x, (lax.axis_size(axis), *x.shape))
    return lax.all_to_all(copies, axis, split_axis=0, concat_axis=0, tiled=True)


def gathered_copies(x, axis, dim):
    return in_order(copy_for_each(x, axis), dim)


def far_field(member):
    along = flow_vectors[member][0] * inflow_speed
    return flow_weights[member] * (
        1.0 + 3.0 * along + 4.5 * along * along - 1.5 * inflow_speed * inflow_speed
    )


def flow_collide(populations, solid):
    density = populations[0]
    for member in range(1, 19):
        density = density + populations[member]
    speeds = []
    for component in range(3):
        moment = jnp.zeros_like(density)
        for member in range(19):
            factor = flow_vectors[member][component]
            if factor != 0:
                moment = moment + factor * populations[member]
        speeds.append(moment / density)
    square = speeds[0] * speeds[0] + speeds[1] * speeds[1] + speeds[2] * speeds[2]
    equilibria = []
    for member in range(19):
        vector = flow_vectors[member]
        project = vector[0] * speeds[0] + vector[1] * speeds[1] + vector[2] * speeds[2]
        equilibria.append(
            flow_weights[member]
            * density
            * (1.0 + 3.0 * project + 4.5 * project * project - 1.5 * square)
        )
    stress = jnp.zeros_like(density)
    for first_axis in range(3):
        for second_axis in range(3):
            tensor = jnp.zeros_like(density)
            for member in range(19):
                factor = flow_vectors[member][first_axis] * flow_vectors[member][second_axis]
                if factor != 0:
                    tensor = tensor + factor * (populations[member] - equilibria[member])
            stress = stress + tensor * tensor
    relaxation = 0.5 * (
        tau_base
        + jnp.sqrt(
            tau_base * tau_base
            + 18.0 * math.sqrt(2.0) * smag_const * smag_const * jnp.sqrt(stress) / density
        )
    )
    eddy = (relaxation - tau_base) / 3.0
    fluid_part = jnp.where(solid, jnp.zeros_like(density), jnp.ones_like(density))
    updated = []
    for member in range(19):
        relaxed = populations[member] - (populations[member] - equilibria[member]) / relaxation
        updated.append(jnp.where(solid, populations[flow_mirror[member]], relaxed))
    motion = jnp.stack(
        [speeds[0] * fluid_part, speeds[1] * fluid_part, speeds[2] * fluid_part, eddy * fluid_part]
    )
    return (updated, motion)


def scalar_collide(scalar, motion, solid, source):
    amount = scalar[0]
    for member in range(1, 7):
        amount = amount + scalar[member]
    relaxation = tau_scalar_base + 4.0 * motion[3] / schmidt_turb
    updated = []
    for member in range(7):
        vector = flow_vectors[member]
        project = vector[0] * motion[0] + vector[1] * motion[1] + vector[2] * motion[2]
        equilibrium = scalar_weights[member] * amount * (1.0 + 4.0 * project)
        relaxed = (
            scalar[member]
            - (scalar[member] - equilibrium) / relaxation
            + scalar_weights[member] * source
        )
        updated.append(jnp.where(solid, scalar[flow_mirror[member]], relaxed))
    return updated


def edge_planes(pieces, vectors, component, dimension, heading):
    planes = []
    for member in range(len(pieces)):
        if vectors[member][component] == heading:
            length = pieces[member].shape[dimension]
            position = length - 1 if heading == 1 else 0
            planes.append(lax.index_in_dim(pieces[member], position, dimension, keepdims=False))
    return jnp.stack(planes)


def displace(pieces, vectors, component, dimension, from_low, from_high):
    result = []
    low_count = 0
    high_count = 0
    for member in range(len(pieces)):
        piece = pieces[member]
        length = piece.shape[dimension]
        heading = vectors[member][component]
        if heading == 1:
            entering = jnp.expand_dims(from_low[low_count], dimension)
            low_count = low_count + 1
            result.append(
                jnp.concatenate(
                    [entering, lax.slice_in_dim(piece, 0, length - 1, axis=dimension)], dimension
                )
            )
        elif heading == -1:
            entering = jnp.expand_dims(from_high[high_count], dimension)
            high_count = high_count + 1
            result.append(
                jnp.concatenate(
                    [lax.slice_in_dim(piece, 1, length, axis=dimension), entering], dimension
                )
            )
        else:
            result.append(piece)
    return result


def local_vertical(pieces, vectors, dimension):
    from_low = jnp.zeros_like(edge_planes(pieces, vectors, 2, dimension, 1))
    from_high = jnp.zeros_like(edge_planes(pieces, vectors, 2, dimension, -1))
    return displace(pieces, vectors, 2, dimension, from_low, from_high)


def send_vertical(planes, offset):
    return passed_along(planes, "row", offset)


def send_spanwise(packed, offset):
    return from_behind(packed, "gy", offset)


def send_streamwise(packed, offset):
    return passed_along(packed, "gx", offset)


def keep_spanwise(flow_in, heading):
    return flow_in


def inflow_fill(flow_in, heading):
    boundary = 0 if heading == 1 else lax.axis_size("gx") - 1
    members = [member for member in range(19) if flow_vectors[member][0] == heading]
    values = jnp.array([far_field(member) for member in members], jnp.float32).reshape(-1, 1, 1)
    return jnp.where(lax.axis_index("gx") == boundary, values + jnp.zeros_like(flow_in), flow_in)


def cross_section(flow, scalar, component, flow_dim, sender, edge_fill, keep_rows):
    arrived_flow = {}
    arrived_scalar = {}
    for heading in (1, -1):
        flow_planes = edge_planes(flow, flow_vectors, component, flow_dim, heading)
        scalar_planes = edge_planes(scalar, scalar_vectors, component, flow_dim + 1, heading)
        if keep_rows:
            width = flow_planes.shape[-1]
            packed = jnp.concatenate(
                [flow_planes.reshape(-1, width), scalar_planes.reshape(-1, width)], 0
            )
            split_at = flow_planes.size // width
        else:
            packed = jnp.concatenate([flow_planes.reshape(-1), scalar_planes.reshape(-1)], 0)
            split_at = flow_planes.size
        arrived = sender(packed, heading)
        arrived_flow[heading] = edge_fill(arrived[:split_at].reshape(flow_planes.shape), heading)
        arrived_scalar[heading] = arrived[split_at:].reshape(scalar_planes.shape)
    flow = displace(flow, flow_vectors, component, flow_dim, arrived_flow[1], arrived_flow[-1])
    scalar = displace(
        scalar, scalar_vectors, component, flow_dim + 1, arrived_scalar[1], arrived_scalar[-1]
    )
    return (flow, scalar)


def scalar_kernel(mode, span_y, depth, span_x):
    def body(*refs):
        if mode == "first":
            conc_ref, motion_ref, solid_ref, source_ref, out_ref = refs
        elif mode == "middle":
            (g_ref, lo_x_ref, hi_x_ref, lo_y_ref, hi_y_ref,
             motion_ref, solid_ref, source_ref, out_ref) = refs
        else:
            g_ref, lo_x_ref, hi_x_ref, lo_y_ref, hi_y_ref, out_ref = refs
        lane = lax.broadcasted_iota(jnp.int32, (depth, span_x), 1)
        level = lax.broadcasted_iota(jnp.int32, (depth, span_x), 0)
        for y in range(span_y):
            if mode == "first":
                block = conc_ref[0, y]
                scalar = [scalar_weights[member] * block for member in range(7)]
            else:
                moved_x = pltpu.roll(g_ref[1, 0, y], 1, 1)
                back_x = pltpu.roll(g_ref[2, 0, y], span_x - 1, 1)
                moved_z = pltpu.roll(g_ref[5, 0, y], 1, 0)
                back_z = pltpu.roll(g_ref[6, 0, y], depth - 1, 0)
                scalar = [
                    g_ref[0, 0, y],
                    jnp.where(lane == 0, lo_x_ref[0, y], moved_x),
                    jnp.where(lane == span_x - 1, hi_x_ref[0, y], back_x),
                    g_ref[3, 0, y - 1] if y > 0 else lo_y_ref[0],
                    g_ref[4, 0, y + 1] if y < span_y - 1 else hi_y_ref[0],
                    jnp.where(level == 0, 0.0, moved_z),
                    jnp.where(level == depth - 1, 0.0, back_z),
                ]
            amount = scalar[0]
            for member in range(1, 7):
                amount = amount + scalar[member]
            if mode == "final":
                out_ref[0, y] = amount
                continue
            speeds = [motion_ref[component, y] for component in range(3)]
            relaxation = tau_scalar_base + 4.0 * motion_ref[3, y] / schmidt_turb
            solid = solid_ref[y] != 0
            source = source_ref[0, y]
            for member in range(7):
                vector = flow_vectors[member]
                project = vector[0] * speeds[0] + vector[1] * speeds[1] + vector[2] * speeds[2]
                equilibrium = scalar_weights[member] * amount * (1.0 + 4.0 * project)
                relaxed = (
                    scalar[member]
                    - (scalar[member] - equilibrium) / relaxation
                    + scalar_weights[member] * source
                )
                out_ref[member, 0, y] = jnp.where(solid, scalar[flow_mirror[member]], relaxed)

    return body


def scalar_stage(mode, scalars, halos, motion, solid, source):
    count, span_y, depth, span_x = source.shape if source is not None else scalars.shape[1:]
    whole = lambda shape: pl.BlockSpec(shape, lambda s: (0,) * len(shape))
    one = lambda shape: pl.BlockSpec(shape, lambda s: (s,) + (0,) * (len(shape) - 1))
    stacked = pl.BlockSpec((7, 1, span_y, depth, span_x), lambda s: (0, s, 0, 0, 0))
    cells = (span_y, depth, span_x)
    edge_specs = [one((1, span_y, depth, 1))] * 2 + [one((1, depth, span_x))] * 2
    if mode == "first":
        operands = [scalars, motion, solid, source]
        specs = [one((1,) + cells), whole((4,) + cells), whole(cells), one((1,) + cells)]
    elif mode == "middle":
        operands = [scalars, *halos, motion, solid, source]
        specs = [stacked] + edge_specs + [whole((4,) + cells), whole(cells), one((1,) + cells)]
    else:
        operands = [scalars, *halos]
        specs = [stacked] + edge_specs
    if mode == "final":
        out_spec = one((1,) + cells)
        out_shape = jax.ShapeDtypeStruct((count,) + cells, jnp.float32)
    else:
        out_spec = stacked
        out_shape = jax.ShapeDtypeStruct((7, count) + cells, jnp.float32)
    return pl.pallas_call(
        scalar_kernel(mode, span_y, depth, span_x),
        grid=(count,),
        in_specs=specs,
        out_specs=out_spec,
        out_shape=out_shape,
    )(*operands)


def packed_section(flow, scalar_out, component, flow_dim, sender, edge_fill, keep_rows):
    arrived_flow = {}
    arrived_scalar = {}
    for heading in (1, -1):
        flow_planes = edge_planes(flow, flow_vectors, component, flow_dim, heading)
        scalar_planes = scalar_out[heading]
        if keep_rows:
            width = flow_planes.shape[-1]
            packed = jnp.concatenate(
                [flow_planes.reshape(-1, width), scalar_planes.reshape(-1, width)], 0
            )
            split_at = flow_planes.size // width
        else:
            packed = jnp.concatenate([flow_planes.reshape(-1), scalar_planes.reshape(-1)], 0)
            split_at = flow_planes.size
        arrived = sender(packed, heading)
        arrived_flow[heading] = edge_fill(arrived[:split_at].reshape(flow_planes.shape), heading)
        arrived_scalar[heading] = arrived[split_at:].reshape(scalar_planes.shape)
    flow = displace(flow, flow_vectors, component, flow_dim, arrived_flow[1], arrived_flow[-1])
    return (flow, arrived_scalar)


def swapped_section(flow, scalar_out, sender, edge_fill):
    first = lax.axis_index("gx") == 0
    leaving = {}
    for heading in (1, -1):
        flow_planes = edge_planes(flow, flow_vectors, 0, 2, heading)
        leaving[heading] = (flow_planes, scalar_out[heading])
    split_at = leaving[1][0].size
    packed = {
        heading: jnp.concatenate([part.reshape(-1) for part in leaving[heading]], 0)
        for heading in (1, -1)
    }
    arrived = lax.ppermute(jnp.where(first, packed[1], packed[-1]), "gx", [(0, 1), (1, 0)])
    outside = jnp.zeros_like(arrived)
    incoming = {1: jnp.where(first, outside, arrived), -1: jnp.where(first, arrived, outside)}
    arrived_flow = {}
    arrived_scalar = {}
    for heading in (1, -1):
        flow_planes, scalar_planes = leaving[heading]
        arrived_flow[heading] = edge_fill(
            incoming[heading][:split_at].reshape(flow_planes.shape), heading
        )
        arrived_scalar[heading] = incoming[heading][split_at:].reshape(scalar_planes.shape)
    flow = displace(flow, flow_vectors, 0, 2, arrived_flow[1], arrived_flow[-1])
    return (flow, arrived_scalar)


def flow_section(flow, component, flow_dim, sender, edge_fill):
    arrived = {}
    for heading in (1, -1):
        planes = edge_planes(flow, flow_vectors, component, flow_dim, heading)
        arrived[heading] = edge_fill(sender(planes, heading), heading)
    return displace(flow, flow_vectors, component, flow_dim, arrived[1], arrived[-1])


def on_device(flow_pops, concentration, solid_mask, source_cell, source_scalar, source_rate):
    row_index = lax.axis_index("row")
    slab_depth = flow_pops.shape[2]
    scalars_here, span_y, depth, span_x = concentration.shape
    height = lax.broadcasted_iota(jnp.int32, solid_mask.shape, 1)
    solid = (solid_mask == 1) | (height == 0) | (height == depth - 1)
    total_x = span_x * lax.axis_size("gx")
    cell_y = source_cell // (depth * total_x)
    cell_z = source_cell // total_x % depth
    cell_x = source_cell % total_x
    local_y = cell_y - lax.axis_index("gy") * span_y
    local_x = cell_x - lax.axis_index("gx") * span_x
    local_scalar = source_scalar - row_index * scalars_here
    count = source_cell.shape[0]
    plane_shape = (scalars_here, span_y, depth, count)
    hit = (
        (lax.broadcasted_iota(jnp.int32, plane_shape, 0) == local_scalar)
        & (lax.broadcasted_iota(jnp.int32, plane_shape, 1) == local_y)
        & (lax.broadcasted_iota(jnp.int32, plane_shape, 2) == cell_z)
    )
    weights = jnp.where(hit, source_rate, 0.0).reshape(-1, count)
    columns = (
        lax.broadcasted_iota(jnp.int32, (count, span_x), 1) == local_x[:, None]
    ).astype(jnp.float32)
    source = jnp.dot(
        weights, columns, precision=lax.Precision.HIGHEST, preferred_element_type=jnp.float32
    ).reshape(concentration.shape)
    solid_flag = solid.astype(jnp.int32)
    flow_solid = lax.dynamic_slice_in_dim(solid, row_index * slab_depth, slab_depth, 1)
    rows = lax.axis_size("row")
    flow = [flow_pops[member] for member in range(19)]
    scalars = concentration
    halos = None
    for time_step in range(STEPS):
        flow, motion = flow_collide(flow, flow_solid)
        rising = edge_planes(flow, flow_vectors, 2, 1, 1)
        sinking = edge_planes(flow, flow_vectors, 2, 1, -1)
        payload = jnp.concatenate([motion.reshape(-1), rising.reshape(-1), sinking.reshape(-1)], 0)
        everyone = copy_for_each(payload, "row")
        column = in_order(everyone[:, : motion.size].reshape((rows,) + motion.shape), 2)
        below = lax.dynamic_index_in_dim(everyone, jnp.maximum(row_index - 1, 0), 0, False)
        above = lax.dynamic_index_in_dim(everyone, jnp.minimum(row_index + 1, rows - 1), 0, False)
        from_below = jnp.where(
            row_index == 0, 0.0, below[motion.size : motion.size + rising.size]
        ).reshape(rising.shape)
        from_above = jnp.where(
            row_index == rows - 1, 0.0, above[motion.size + rising.size :]
        ).reshape(sinking.shape)
        mode = "first" if time_step == 0 else "middle"
        scalars = scalar_stage(mode, scalars, halos, column, solid_flag, source)
        flow = displace(flow, flow_vectors, 2, 1, from_below, from_above)
        leaving_y = {1: scalars[3, :, span_y - 1], -1: scalars[4, :, 0]}
        flow, arrived_y = packed_section(flow, leaving_y, 1, 0, send_spanwise, keep_spanwise, True)
        leaving_x = {1: scalars[1, :, :, :, span_x - 1 :], -1: scalars[2, :, :, :, :1]}
        if lax.axis_size("gx") == 2:
            flow, arrived_x = swapped_section(flow, leaving_x, send_streamwise, inflow_fill)
        else:
            flow, arrived_x = packed_section(
                flow, leaving_x, 0, 2, send_streamwise, inflow_fill, False
            )
        halos = (arrived_x[1], arrived_x[-1], arrived_y[1], arrived_y[-1])
    amount = scalar_stage("final", scalars, halos, None, None, None)
    stacked = jnp.stack(flow)
    return (stacked, amount)


def solution(mesh):
    in_specs = (
        P(None, "gy", "row", "gx"),
        P("row", "gy", None, "gx"),
        P("gy", None, "gx"),
        P(),
        P(),
        P(),
    )
    out_specs = (P(None, "gy", "row", "gx"), P("row", "gy", None, "gx"))
    return jax.shard_map(
        on_device, mesh=mesh, in_specs=in_specs, out_specs=out_specs, check_vma=False
    )
```

```python
import math

import jax
import jax.numpy as jnp
from jax import lax
from jax.sharding import PartitionSpec as P
from jax.experimental import pallas as pl
from jax.experimental.pallas import tpu as pltpu

STEPS = 3


flow_vectors = (
    (0, 0, 0),
    (1, 0, 0),
    (-1, 0, 0),
    (0, 1, 0),
    (0, -1, 0),
    (0, 0, 1),
    (0, 0, -1),
    (1, 1, 0),
    (-1, -1, 0),
    (1, -1, 0),
    (-1, 1, 0),
    (1, 0, 1),
    (-1, 0, -1),
    (1, 0, -1),
    (-1, 0, 1),
    (0, 1, 1),
    (0, -1, -1),
    (0, 1, -1),
    (0, -1, 1),
)
scalar_vectors = flow_vectors[:7]
flow_weights = (1.0 / 3.0,) + (1.0 / 18.0,) * 6 + (1.0 / 36.0,) * 12
flow_mirror = (0, 2, 1, 4, 3, 6, 5, 8, 7, 10, 9, 12, 11, 14, 13, 16, 15, 18, 17)
scalar_weights = (0.25,) + (0.125,) * 6
tau_base = 0.52
smag_const = 0.17
tau_scalar_base = 0.55
schmidt_turb = 0.7
inflow_speed = 0.08


def passed_along(block, axis, distance):
    devices = range(lax.axis_size(axis))
    route = [(i - distance, i) for i in devices if i - distance in devices]
    return lax.ppermute(block, axis, route)


def from_behind(value, axis, steps):
    count = lax.axis_size(axis)
    pairs = [(source, (source + steps) % count) for source in range(count)]
    return lax.ppermute(value, axis, pairs)


def in_order(tiles, dim):
    tiles = jnp.moveaxis(tiles, 0, dim)
    shape = tiles.shape
    return tiles.reshape(*shape[:dim], shape[dim] * shape[dim + 1], *shape[dim + 2 :])


def copy_for_each(x, axis):
    copies = jnp.broadcast_to(x, (lax.axis_size(axis), *x.shape))
    return lax.all_to_all(copies, axis, split_axis=0, concat_axis=0, tiled=True)


def gathered_copies(x, axis, dim):
    return in_order(copy_for_each(x, axis), dim)


def far_field(member):
    along = flow_vectors[member][0] * inflow_speed
    return flow_weights[member] * (
        1.0 + 3.0 * along + 4.5 * along * along - 1.5 * inflow_speed * inflow_speed
    )


def flow_collide(populations, solid):
    density = populations[0]
    for member in range(1, 19):
        density = density + populations[member]
    speeds = []
    for component in range(3):
        moment = jnp.zeros_like(density)
        for member in range(19):
            factor = flow_vectors[member][component]
            if factor != 0:
                moment = moment + factor * populations[member]
        speeds.append(moment / density)
    square = speeds[0] * speeds[0] + speeds[1] * speeds[1] + speeds[2] * speeds[2]
    equilibria = []
    for member in range(19):
        vector = flow_vectors[member]
        project = vector[0] * speeds[0] + vector[1] * speeds[1] + vector[2] * speeds[2]
        equilibria.append(
            flow_weights[member]
            * density
            * (1.0 + 3.0 * project + 4.5 * project * project - 1.5 * square)
        )
    stress = jnp.zeros_like(density)
    for first_axis in range(3):
        for second_axis in range(3):
            tensor = jnp.zeros_like(density)
            for member in range(19):
                factor = flow_vectors[member][first_axis] * flow_vectors[member][second_axis]
                if factor != 0:
                    tensor = tensor + factor * (populations[member] - equilibria[member])
            stress = stress + tensor * tensor
    relaxation = 0.5 * (
        tau_base
        + jnp.sqrt(
            tau_base * tau_base
            + 18.0 * math.sqrt(2.0) * smag_const * smag_const * jnp.sqrt(stress) / density
        )
    )
    eddy = (relaxation - tau_base) / 3.0
    fluid_part = jnp.where(solid, jnp.zeros_like(density), jnp.ones_like(density))
    updated = []
    for member in range(19):
        relaxed = populations[member] - (populations[member] - equilibria[member]) / relaxation
        updated.append(jnp.where(solid, populations[flow_mirror[member]], relaxed))
    motion = jnp.stack(
        [speeds[0] * fluid_part, speeds[1] * fluid_part, speeds[2] * fluid_part, eddy * fluid_part]
    )
    return (updated, motion)


def scalar_collide(scalar, motion, solid, source):
    amount = scalar[0]
    for member in range(1, 7):
        amount = amount + scalar[member]
    relaxation = tau_scalar_base + 4.0 * motion[3] / schmidt_turb
    updated = []
    for member in range(7):
        vector = flow_vectors[member]
        project = vector[0] * motion[0] + vector[1] * motion[1] + vector[2] * motion[2]
        equilibrium = scalar_weights[member] * amount * (1.0 + 4.0 * project)
        relaxed = (
            scalar[member]
            - (scalar[member] - equilibrium) / relaxation
            + scalar_weights[member] * source
        )
        updated.append(jnp.where(solid, scalar[flow_mirror[member]], relaxed))
    return updated


def edge_planes(pieces, vectors, component, dimension, heading):
    planes = []
    for member in range(len(pieces)):
        if vectors[member][component] == heading:
            length = pieces[member].shape[dimension]
            position = length - 1 if heading == 1 else 0
            planes.append(lax.index_in_dim(pieces[member], position, dimension, keepdims=False))
    return jnp.stack(planes)


def displace(pieces, vectors, component, dimension, from_low, from_high):
    result = []
    low_count = 0
    high_count = 0
    for member in range(len(pieces)):
        piece = pieces[member]
        length = piece.shape[dimension]
        heading = vectors[member][component]
        if heading == 1:
            entering = jnp.expand_dims(from_low[low_count], dimension)
            low_count = low_count + 1
            result.append(
                jnp.concatenate(
                    [entering, lax.slice_in_dim(piece, 0, length - 1, axis=dimension)], dimension
                )
            )
        elif heading == -1:
            entering = jnp.expand_dims(from_high[high_count], dimension)
            high_count = high_count + 1
            result.append(
                jnp.concatenate(
                    [lax.slice_in_dim(piece, 1, length, axis=dimension), entering], dimension
                )
            )
        else:
            result.append(piece)
    return result


def local_vertical(pieces, vectors, dimension):
    from_low = jnp.zeros_like(edge_planes(pieces, vectors, 2, dimension, 1))
    from_high = jnp.zeros_like(edge_planes(pieces, vectors, 2, dimension, -1))
    return displace(pieces, vectors, 2, dimension, from_low, from_high)


def send_vertical(planes, offset):
    return passed_along(planes, "row", offset)


def send_spanwise(packed, offset):
    return from_behind(packed, "gy", offset)


def send_streamwise(packed, offset):
    return passed_along(packed, "gx", offset)


def keep_spanwise(flow_in, heading):
    return flow_in


def inflow_fill(flow_in, heading):
    boundary = 0 if heading == 1 else lax.axis_size("gx") - 1
    members = [member for member in range(19) if flow_vectors[member][0] == heading]
    values = jnp.array([far_field(member) for member in members], jnp.float32).reshape(-1, 1, 1)
    return jnp.where(lax.axis_index("gx") == boundary, values + jnp.zeros_like(flow_in), flow_in)


def cross_section(flow, scalar, component, flow_dim, sender, edge_fill, keep_rows):
    arrived_flow = {}
    arrived_scalar = {}
    for heading in (1, -1):
        flow_planes = edge_planes(flow, flow_vectors, component, flow_dim, heading)
        scalar_planes = edge_planes(scalar, scalar_vectors, component, flow_dim + 1, heading)
        if keep_rows:
            width = flow_planes.shape[-1]
            packed = jnp.concatenate(
                [flow_planes.reshape(-1, width), scalar_planes.reshape(-1, width)], 0
            )
            split_at = flow_planes.size // width
        else:
            packed = jnp.concatenate([flow_planes.reshape(-1), scalar_planes.reshape(-1)], 0)
            split_at = flow_planes.size
        arrived = sender(packed, heading)
        arrived_flow[heading] = edge_fill(arrived[:split_at].reshape(flow_planes.shape), heading)
        arrived_scalar[heading] = arrived[split_at:].reshape(scalar_planes.shape)
    flow = displace(flow, flow_vectors, component, flow_dim, arrived_flow[1], arrived_flow[-1])
    scalar = displace(
        scalar, scalar_vectors, component, flow_dim + 1, arrived_scalar[1], arrived_scalar[-1]
    )
    return (flow, scalar)


def scalar_kernel(mode, span_y, depth, span_x):
    def body(*refs):
        if mode == "first":
            conc_ref, motion_ref, solid_ref, source_ref, out_ref = refs
        elif mode == "middle":
            (g_ref, lo_x_ref, hi_x_ref, lo_y_ref, hi_y_ref,
             motion_ref, solid_ref, source_ref, out_ref) = refs
        else:
            g_ref, lo_x_ref, hi_x_ref, lo_y_ref, hi_y_ref, out_ref = refs
        lane = lax.broadcasted_iota(jnp.int32, (depth, span_x), 1)
        level = lax.broadcasted_iota(jnp.int32, (depth, span_x), 0)
        for y in range(span_y):
            if mode == "first":
                block = conc_ref[0, y]
                scalar = [scalar_weights[member] * block for member in range(7)]
            else:
                moved_x = pltpu.roll(g_ref[1, 0, y], 1, 1)
                back_x = pltpu.roll(g_ref[2, 0, y], span_x - 1, 1)
                moved_z = pltpu.roll(g_ref[5, 0, y], 1, 0)
                back_z = pltpu.roll(g_ref[6, 0, y], depth - 1, 0)
                scalar = [
                    g_ref[0, 0, y],
                    jnp.where(lane == 0, lo_x_ref[0, y], moved_x),
                    jnp.where(lane == span_x - 1, hi_x_ref[0, y], back_x),
                    g_ref[3, 0, y - 1] if y > 0 else lo_y_ref[0],
                    g_ref[4, 0, y + 1] if y < span_y - 1 else hi_y_ref[0],
                    jnp.where(level == 0, 0.0, moved_z),
                    jnp.where(level == depth - 1, 0.0, back_z),
                ]
            amount = scalar[0]
            for member in range(1, 7):
                amount = amount + scalar[member]
            if mode == "final":
                out_ref[0, y] = amount
                continue
            speeds = [motion_ref[component, y] for component in range(3)]
            relaxation = tau_scalar_base + 4.0 * motion_ref[3, y] / schmidt_turb
            solid = solid_ref[y] != 0
            source = source_ref[0, y]
            for member in range(7):
                vector = flow_vectors[member]
                project = vector[0] * speeds[0] + vector[1] * speeds[1] + vector[2] * speeds[2]
                equilibrium = scalar_weights[member] * amount * (1.0 + 4.0 * project)
                relaxed = (
                    scalar[member]
                    - (scalar[member] - equilibrium) / relaxation
                    + scalar_weights[member] * source
                )
                out_ref[member, 0, y] = jnp.where(solid, scalar[flow_mirror[member]], relaxed)

    return body


def scalar_stage(mode, scalars, halos, motion, solid, source):
    count, span_y, depth, span_x = source.shape if source is not None else scalars.shape[1:]
    whole = lambda shape: pl.BlockSpec(shape, lambda s: (0,) * len(shape))
    one = lambda shape: pl.BlockSpec(shape, lambda s: (s,) + (0,) * (len(shape) - 1))
    stacked = pl.BlockSpec((7, 1, span_y, depth, span_x), lambda s: (0, s, 0, 0, 0))
    cells = (span_y, depth, span_x)
    edge_specs = [one((1, span_y, depth, 1))] * 2 + [one((1, depth, span_x))] * 2
    if mode == "first":
        operands = [scalars, motion, solid, source]
        specs = [one((1,) + cells), whole((4,) + cells), whole(cells), one((1,) + cells)]
    elif mode == "middle":
        operands = [scalars, *halos, motion, solid, source]
        specs = [stacked] + edge_specs + [whole((4,) + cells), whole(cells), one((1,) + cells)]
    else:
        operands = [scalars, *halos]
        specs = [stacked] + edge_specs
    if mode == "final":
        out_spec = one((1,) + cells)
        out_shape = jax.ShapeDtypeStruct((count,) + cells, jnp.float32)
    else:
        out_spec = stacked
        out_shape = jax.ShapeDtypeStruct((7, count) + cells, jnp.float32)
    return pl.pallas_call(
        scalar_kernel(mode, span_y, depth, span_x),
        grid=(count,),
        in_specs=specs,
        out_specs=out_spec,
        out_shape=out_shape,
    )(*operands)


def packed_section(flow, scalar_out, component, flow_dim, sender, edge_fill, keep_rows):
    arrived_flow = {}
    arrived_scalar = {}
    for heading in (1, -1):
        flow_planes = edge_planes(flow, flow_vectors, component, flow_dim, heading)
        scalar_planes = scalar_out[heading]
        if keep_rows:
            width = flow_planes.shape[-1]
            packed = jnp.concatenate(
                [flow_planes.reshape(-1, width), scalar_planes.reshape(-1, width)], 0
            )
            split_at = flow_planes.size // width
        else:
            packed = jnp.concatenate([flow_planes.reshape(-1), scalar_planes.reshape(-1)], 0)
            split_at = flow_planes.size
        arrived = sender(packed, heading)
        arrived_flow[heading] = edge_fill(arrived[:split_at].reshape(flow_planes.shape), heading)
        arrived_scalar[heading] = arrived[split_at:].reshape(scalar_planes.shape)
    flow = displace(flow, flow_vectors, component, flow_dim, arrived_flow[1], arrived_flow[-1])
    return (flow, arrived_scalar)


def swapped_section(flow, scalar_out, sender, edge_fill):
    first = lax.axis_index("gx") == 0
    leaving = {}
    for heading in (1, -1):
        flow_planes = edge_planes(flow, flow_vectors, 0, 2, heading)
        leaving[heading] = (flow_planes, scalar_out[heading])
    split_at = leaving[1][0].size
    packed = {
        heading: jnp.concatenate([part.reshape(-1) for part in leaving[heading]], 0)
        for heading in (1, -1)
    }
    arrived = lax.ppermute(jnp.where(first, packed[1], packed[-1]), "gx", [(0, 1), (1, 0)])
    outside = jnp.zeros_like(arrived)
    incoming = {1: jnp.where(first, outside, arrived), -1: jnp.where(first, arrived, outside)}
    arrived_flow = {}
    arrived_scalar = {}
    for heading in (1, -1):
        flow_planes, scalar_planes = leaving[heading]
        arrived_flow[heading] = edge_fill(
            incoming[heading][:split_at].reshape(flow_planes.shape), heading
        )
        arrived_scalar[heading] = incoming[heading][split_at:].reshape(scalar_planes.shape)
    flow = displace(flow, flow_vectors, 0, 2, arrived_flow[1], arrived_flow[-1])
    return (flow, arrived_scalar)


def flow_section(flow, component, flow_dim, sender, edge_fill):
    arrived = {}
    for heading in (1, -1):
        planes = edge_planes(flow, flow_vectors, component, flow_dim, heading)
        arrived[heading] = edge_fill(sender(planes, heading), heading)
    return displace(flow, flow_vectors, component, flow_dim, arrived[1], arrived[-1])


def on_device(flow_pops, concentration, solid_mask, source_cell, source_scalar, source_rate):
    row_index = lax.axis_index("row")
    slab_depth = flow_pops.shape[2]
    scalars_here, span_y, depth, span_x = concentration.shape
    height = lax.broadcasted_iota(jnp.int32, solid_mask.shape, 1)
    solid = (solid_mask == 1) | (height == 0) | (height == depth - 1)
    total_x = span_x * lax.axis_size("gx")
    cell_y = source_cell // (depth * total_x)
    cell_z = source_cell // total_x % depth
    cell_x = source_cell % total_x
    local_y = cell_y - lax.axis_index("gy") * span_y
    local_x = cell_x - lax.axis_index("gx") * span_x
    local_scalar = source_scalar - row_index * scalars_here
    count = source_cell.shape[0]
    plane_shape = (scalars_here, span_y, depth, count)
    hit = (
        (lax.broadcasted_iota(jnp.int32, plane_shape, 0) == local_scalar)
        & (lax.broadcasted_iota(jnp.int32, plane_shape, 1) == local_y)
        & (lax.broadcasted_iota(jnp.int32, plane_shape, 2) == cell_z)
    )
    weights = jnp.where(hit, source_rate, 0.0).reshape(-1, count)
    columns = (
        lax.broadcasted_iota(jnp.int32, (count, span_x), 1) == local_x[:, None]
    ).astype(jnp.float32)
    source = jnp.dot(
        weights, columns, precision=lax.Precision.HIGHEST, preferred_element_type=jnp.float32
    ).reshape(concentration.shape)
    solid_flag = solid.astype(jnp.int32)
    flow_solid = lax.dynamic_slice_in_dim(solid, row_index * slab_depth, slab_depth, 1)
    rows = lax.axis_size("row")
    flow = [flow_pops[member] for member in range(19)]
    scalars = concentration
    leaving = None
    for time_step in range(STEPS):
        flow, motion = flow_collide(flow, flow_solid)
        rising = edge_planes(flow, flow_vectors, 2, 1, 1)
        sinking = edge_planes(flow, flow_vectors, 2, 1, -1)
        payload = jnp.concatenate([motion.reshape(-1), rising.reshape(-1), sinking.reshape(-1)], 0)
        everyone = copy_for_each(payload, "row")
        column = in_order(everyone[:, : motion.size].reshape((rows,) + motion.shape), 2)
        below = lax.dynamic_index_in_dim(everyone, jnp.maximum(row_index - 1, 0), 0, False)
        above = lax.dynamic_index_in_dim(everyone, jnp.minimum(row_index + 1, rows - 1), 0, False)
        from_below = jnp.where(
            row_index == 0, 0.0, below[motion.size : motion.size + rising.size]
        ).reshape(rising.shape)
        from_above = jnp.where(
            row_index == rows - 1, 0.0, above[motion.size + rising.size :]
        ).reshape(sinking.shape)
        flow = displace(flow, flow_vectors, 2, 1, from_below, from_above)
        if leaving is None:
            flow = flow_section(flow, 1, 0, send_spanwise, keep_spanwise)
            flow = flow_section(flow, 0, 2, send_streamwise, inflow_fill)
            scalars = scalar_stage("first", scalars, None, column, solid_flag, source)
        else:
            flow, arrived_y = packed_section(
                flow, leaving[1], 1, 0, send_spanwise, keep_spanwise, True
            )
            if lax.axis_size("gx") == 2:
                flow, arrived_x = swapped_section(flow, leaving[0], send_streamwise, inflow_fill)
            else:
                flow, arrived_x = packed_section(
                    flow, leaving[0], 0, 2, send_streamwise, inflow_fill, False
                )
            halos = (arrived_x[1], arrived_x[-1], arrived_y[1], arrived_y[-1])
            scalars = scalar_stage("middle", scalars, halos, column, solid_flag, source)
        leaving = (
            {1: scalars[1, :, :, :, span_x - 1 :], -1: scalars[2, :, :, :, :1]},
            {1: scalars[3, :, span_y - 1], -1: scalars[4, :, 0]},
        )
    halos = (
        send_streamwise(leaving[0][1], 1),
        send_streamwise(leaving[0][-1], -1),
        send_spanwise(leaving[1][1], 1),
        send_spanwise(leaving[1][-1], -1),
    )
    amount = scalar_stage("final", scalars, halos, None, None, None)
    stacked = jnp.stack(flow)
    return (stacked, amount)


def solution(mesh):
    in_specs = (
        P(None, "gy", "row", "gx"),
        P("row", "gy", None, "gx"),
        P("gy", None, "gx"),
        P(),
        P(),
        P(),
    )
    out_specs = (P(None, "gy", "row", "gx"), P("row", "gy", None, "gx"))
    return jax.shard_map(
        on_device, mesh=mesh, in_specs=in_specs, out_specs=out_specs, check_vma=False
    )
```

```python
import math

import jax
import jax.numpy as jnp
from jax import lax
from jax.sharding import PartitionSpec as P
from jax.experimental import pallas as pl
from jax.experimental.pallas import tpu as pltpu

STEPS = 3


flow_vectors = (
    (0, 0, 0),
    (1, 0, 0),
    (-1, 0, 0),
    (0, 1, 0),
    (0, -1, 0),
    (0, 0, 1),
    (0, 0, -1),
    (1, 1, 0),
    (-1, -1, 0),
    (1, -1, 0),
    (-1, 1, 0),
    (1, 0, 1),
    (-1, 0, -1),
    (1, 0, -1),
    (-1, 0, 1),
    (0, 1, 1),
    (0, -1, -1),
    (0, 1, -1),
    (0, -1, 1),
)
scalar_vectors = flow_vectors[:7]
flow_weights = (1.0 / 3.0,) + (1.0 / 18.0,) * 6 + (1.0 / 36.0,) * 12
flow_mirror = (0, 2, 1, 4, 3, 6, 5, 8, 7, 10, 9, 12, 11, 14, 13, 16, 15, 18, 17)
scalar_weights = (0.25,) + (0.125,) * 6
tau_base = 0.52
smag_const = 0.17
tau_scalar_base = 0.55
schmidt_turb = 0.7
inflow_speed = 0.08


def passed_along(block, axis, distance):
    devices = range(lax.axis_size(axis))
    route = [(i - distance, i) for i in devices if i - distance in devices]
    return lax.ppermute(block, axis, route)


def from_behind(value, axis, steps):
    count = lax.axis_size(axis)
    pairs = [(source, (source + steps) % count) for source in range(count)]
    return lax.ppermute(value, axis, pairs)


def in_order(tiles, dim):
    tiles = jnp.moveaxis(tiles, 0, dim)
    shape = tiles.shape
    return tiles.reshape(*shape[:dim], shape[dim] * shape[dim + 1], *shape[dim + 2 :])


def copy_for_each(x, axis):
    copies = jnp.broadcast_to(x, (lax.axis_size(axis), *x.shape))
    return lax.all_to_all(copies, axis, split_axis=0, concat_axis=0, tiled=True)


def gathered_copies(x, axis, dim):
    return in_order(copy_for_each(x, axis), dim)


def far_field(member):
    along = flow_vectors[member][0] * inflow_speed
    return flow_weights[member] * (
        1.0 + 3.0 * along + 4.5 * along * along - 1.5 * inflow_speed * inflow_speed
    )


def flow_collide(populations, solid):
    density = populations[0]
    for member in range(1, 19):
        density = density + populations[member]
    speeds = []
    for component in range(3):
        moment = jnp.zeros_like(density)
        for member in range(19):
            factor = flow_vectors[member][component]
            if factor != 0:
                moment = moment + factor * populations[member]
        speeds.append(moment / density)
    square = speeds[0] * speeds[0] + speeds[1] * speeds[1] + speeds[2] * speeds[2]
    equilibria = []
    for member in range(19):
        vector = flow_vectors[member]
        project = vector[0] * speeds[0] + vector[1] * speeds[1] + vector[2] * speeds[2]
        equilibria.append(
            flow_weights[member]
            * density
            * (1.0 + 3.0 * project + 4.5 * project * project - 1.5 * square)
        )
    stress = jnp.zeros_like(density)
    for first_axis in range(3):
        for second_axis in range(3):
            tensor = jnp.zeros_like(density)
            for member in range(19):
                factor = flow_vectors[member][first_axis] * flow_vectors[member][second_axis]
                if factor != 0:
                    tensor = tensor + factor * (populations[member] - equilibria[member])
            stress = stress + tensor * tensor
    relaxation = 0.5 * (
        tau_base
        + jnp.sqrt(
            tau_base * tau_base
            + 18.0 * math.sqrt(2.0) * smag_const * smag_const * jnp.sqrt(stress) / density
        )
    )
    eddy = (relaxation - tau_base) / 3.0
    fluid_part = jnp.where(solid, jnp.zeros_like(density), jnp.ones_like(density))
    updated = []
    for member in range(19):
        relaxed = populations[member] - (populations[member] - equilibria[member]) / relaxation
        updated.append(jnp.where(solid, populations[flow_mirror[member]], relaxed))
    motion = jnp.stack(
        [speeds[0] * fluid_part, speeds[1] * fluid_part, speeds[2] * fluid_part, eddy * fluid_part]
    )
    return (updated, motion)


def scalar_collide(scalar, motion, solid, source):
    amount = scalar[0]
    for member in range(1, 7):
        amount = amount + scalar[member]
    relaxation = tau_scalar_base + 4.0 * motion[3] / schmidt_turb
    updated = []
    for member in range(7):
        vector = flow_vectors[member]
        project = vector[0] * motion[0] + vector[1] * motion[1] + vector[2] * motion[2]
        equilibrium = scalar_weights[member] * amount * (1.0 + 4.0 * project)
        relaxed = (
            scalar[member]
            - (scalar[member] - equilibrium) / relaxation
            + scalar_weights[member] * source
        )
        updated.append(jnp.where(solid, scalar[flow_mirror[member]], relaxed))
    return updated


def edge_planes(pieces, vectors, component, dimension, heading):
    planes = []
    for member in range(len(pieces)):
        if vectors[member][component] == heading:
            length = pieces[member].shape[dimension]
            position = length - 1 if heading == 1 else 0
            planes.append(lax.index_in_dim(pieces[member], position, dimension, keepdims=False))
    return jnp.stack(planes)


def displace(pieces, vectors, component, dimension, from_low, from_high):
    result = []
    low_count = 0
    high_count = 0
    for member in range(len(pieces)):
        piece = pieces[member]
        length = piece.shape[dimension]
        heading = vectors[member][component]
        if heading == 1:
            entering = jnp.expand_dims(from_low[low_count], dimension)
            low_count = low_count + 1
            result.append(
                jnp.concatenate(
                    [entering, lax.slice_in_dim(piece, 0, length - 1, axis=dimension)], dimension
                )
            )
        elif heading == -1:
            entering = jnp.expand_dims(from_high[high_count], dimension)
            high_count = high_count + 1
            result.append(
                jnp.concatenate(
                    [lax.slice_in_dim(piece, 1, length, axis=dimension), entering], dimension
                )
            )
        else:
            result.append(piece)
    return result


def local_vertical(pieces, vectors, dimension):
    from_low = jnp.zeros_like(edge_planes(pieces, vectors, 2, dimension, 1))
    from_high = jnp.zeros_like(edge_planes(pieces, vectors, 2, dimension, -1))
    return displace(pieces, vectors, 2, dimension, from_low, from_high)


def send_vertical(planes, offset):
    return passed_along(planes, "row", offset)


def send_spanwise(packed, offset):
    return from_behind(packed, "gy", offset)


def send_streamwise(packed, offset):
    return passed_along(packed, "gx", offset)


def keep_spanwise(flow_in, heading):
    return flow_in


def inflow_fill(flow_in, heading):
    boundary = 0 if heading == 1 else lax.axis_size("gx") - 1
    members = [member for member in range(19) if flow_vectors[member][0] == heading]
    values = jnp.array([far_field(member) for member in members], jnp.float32).reshape(-1, 1, 1)
    return jnp.where(lax.axis_index("gx") == boundary, values + jnp.zeros_like(flow_in), flow_in)


def cross_section(flow, scalar, component, flow_dim, sender, edge_fill, keep_rows):
    arrived_flow = {}
    arrived_scalar = {}
    for heading in (1, -1):
        flow_planes = edge_planes(flow, flow_vectors, component, flow_dim, heading)
        scalar_planes = edge_planes(scalar, scalar_vectors, component, flow_dim + 1, heading)
        if keep_rows:
            width = flow_planes.shape[-1]
            packed = jnp.concatenate(
                [flow_planes.reshape(-1, width), scalar_planes.reshape(-1, width)], 0
            )
            split_at = flow_planes.size // width
        else:
            packed = jnp.concatenate([flow_planes.reshape(-1), scalar_planes.reshape(-1)], 0)
            split_at = flow_planes.size
        arrived = sender(packed, heading)
        arrived_flow[heading] = edge_fill(arrived[:split_at].reshape(flow_planes.shape), heading)
        arrived_scalar[heading] = arrived[split_at:].reshape(scalar_planes.shape)
    flow = displace(flow, flow_vectors, component, flow_dim, arrived_flow[1], arrived_flow[-1])
    scalar = displace(
        scalar, scalar_vectors, component, flow_dim + 1, arrived_scalar[1], arrived_scalar[-1]
    )
    return (flow, scalar)


def scalar_kernel(mode, span_y, depth, span_x):
    exact = lax.Precision.HIGHEST

    def body(*refs):
        if mode == "first":
            conc_ref, motion_ref, solid_ref, source_ref, out_ref, edge_ref = refs
        elif mode == "middle":
            (g_ref, side_ref, lo_y_ref, hi_y_ref,
             motion_ref, solid_ref, source_ref, out_ref, edge_ref) = refs
        else:
            g_ref, side_ref, lo_y_ref, hi_y_ref, out_ref = refs
        lane = lax.broadcasted_iota(jnp.int32, (depth, span_x), 1)
        level = lax.broadcasted_iota(jnp.int32, (depth, span_x), 0)
        diagonal = lax.broadcasted_iota(jnp.int32, (depth, depth), 0) == lax.broadcasted_iota(
            jnp.int32, (depth, depth), 1
        )
        at_low = (lane == 0).astype(jnp.float32)
        at_high = (lane == span_x - 1).astype(jnp.float32)
        pick_lane = lax.broadcasted_iota(jnp.int32, (8, span_x), 1)
        pick_high = (pick_lane == span_x - 1).astype(jnp.float32)
        pick_low = (pick_lane == 0).astype(jnp.float32)
        edge_row = lax.broadcasted_iota(jnp.int32, (2, depth), 0)
        by_lanes = (((1,), (1,)), ((), ()))
        for y in range(span_y):
            if mode == "first":
                block = conc_ref[0, y]
                scalar = [scalar_weights[member] * block for member in range(7)]
            else:
                side = side_ref[0, y]
                spread_low = jnp.where(diagonal, side[0:1, :], 0.0)
                spread_high = jnp.where(diagonal, side[1:2, :], 0.0)
                column = jnp.dot(spread_low, at_low, precision=exact) + jnp.dot(
                    spread_high, at_high, precision=exact
                )
                moved_x = pltpu.roll(g_ref[1, 0, y], 1, 1)
                back_x = pltpu.roll(g_ref[2, 0, y], span_x - 1, 1)
                moved_z = pltpu.roll(g_ref[5, 0, y], 1, 0)
                back_z = pltpu.roll(g_ref[6, 0, y], depth - 1, 0)
                scalar = [
                    g_ref[0, 0, y],
                    jnp.where(lane == 0, column, moved_x),
                    jnp.where(lane == span_x - 1, column, back_x),
                    g_ref[3, 0, y - 1] if y > 0 else lo_y_ref[0],
                    g_ref[4, 0, y + 1] if y < span_y - 1 else hi_y_ref[0],
                    jnp.where(level == 0, 0.0, moved_z),
                    jnp.where(level == depth - 1, 0.0, back_z),
                ]
            amount = scalar[0]
            for member in range(1, 7):
                amount = amount + scalar[member]
            if mode == "final":
                out_ref[0, y] = amount
                continue
            speeds = [motion_ref[component, y] for component in range(3)]
            relaxation = tau_scalar_base + 4.0 * motion_ref[3, y] / schmidt_turb
            solid = solid_ref[y] != 0
            source = source_ref[0, y]
            post = []
            for member in range(7):
                vector = flow_vectors[member]
                project = vector[0] * speeds[0] + vector[1] * speeds[1] + vector[2] * speeds[2]
                equilibrium = scalar_weights[member] * amount * (1.0 + 4.0 * project)
                relaxed = (
                    scalar[member]
                    - (scalar[member] - equilibrium) / relaxation
                    + scalar_weights[member] * source
                )
                post.append(jnp.where(solid, scalar[flow_mirror[member]], relaxed))
                out_ref[member, 0, y] = post[member]
            leaving_high = lax.dot_general(pick_high, post[1], by_lanes, precision=exact)
            leaving_low = lax.dot_general(pick_low, post[2], by_lanes, precision=exact)
            edge_ref[0, y] = jnp.where(edge_row == 0, leaving_high[0:2], leaving_low[0:2])

    return body


def scalar_stage(mode, scalars, halos, motion, solid, source):
    count, span_y, depth, span_x = source.shape if source is not None else scalars.shape[1:]
    whole = lambda shape: pl.BlockSpec(shape, lambda s: (0,) * len(shape))
    one = lambda shape: pl.BlockSpec(shape, lambda s: (s,) + (0,) * (len(shape) - 1))
    stacked = pl.BlockSpec((7, 1, span_y, depth, span_x), lambda s: (0, s, 0, 0, 0))
    cells = (span_y, depth, span_x)
    edge_specs = [one((1, span_y, 2, depth))] + [one((1, depth, span_x))] * 2
    if mode == "first":
        operands = [scalars, motion, solid, source]
        specs = [one((1,) + cells), whole((4,) + cells), whole(cells), one((1,) + cells)]
    elif mode == "middle":
        operands = [scalars, *halos, motion, solid, source]
        specs = [stacked] + edge_specs + [whole((4,) + cells), whole(cells), one((1,) + cells)]
    else:
        operands = [scalars, *halos]
        specs = [stacked] + edge_specs
    if mode == "final":
        out_spec = one((1,) + cells)
        out_shape = jax.ShapeDtypeStruct((count,) + cells, jnp.float32)
    else:
        out_spec = [stacked, one((1, span_y, 2, depth))]
        out_shape = [
            jax.ShapeDtypeStruct((7, count) + cells, jnp.float32),
            jax.ShapeDtypeStruct((count, span_y, 2, depth), jnp.float32),
        ]
    return pl.pallas_call(
        scalar_kernel(mode, span_y, depth, span_x),
        grid=(count,),
        in_specs=specs,
        out_specs=out_spec,
        out_shape=out_shape,
    )(*operands)


def packed_section(flow, scalar_out, component, flow_dim, sender, edge_fill, keep_rows):
    arrived_flow = {}
    arrived_scalar = {}
    for heading in (1, -1):
        flow_planes = edge_planes(flow, flow_vectors, component, flow_dim, heading)
        scalar_planes = scalar_out[heading]
        if keep_rows:
            width = flow_planes.shape[-1]
            packed = jnp.concatenate(
                [flow_planes.reshape(-1, width), scalar_planes.reshape(-1, width)], 0
            )
            split_at = flow_planes.size // width
        else:
            packed = jnp.concatenate([flow_planes.reshape(-1), scalar_planes.reshape(-1)], 0)
            split_at = flow_planes.size
        arrived = sender(packed, heading)
        arrived_flow[heading] = edge_fill(arrived[:split_at].reshape(flow_planes.shape), heading)
        arrived_scalar[heading] = arrived[split_at:].reshape(scalar_planes.shape)
    flow = displace(flow, flow_vectors, component, flow_dim, arrived_flow[1], arrived_flow[-1])
    return (flow, arrived_scalar)


def swapped_section(flow, scalar_out, sender, edge_fill):
    first = lax.axis_index("gx") == 0
    leaving = {}
    for heading in (1, -1):
        flow_planes = edge_planes(flow, flow_vectors, 0, 2, heading)
        leaving[heading] = (flow_planes, scalar_out[heading])
    split_at = leaving[1][0].size
    packed = {
        heading: jnp.concatenate([part.reshape(-1) for part in leaving[heading]], 0)
        for heading in (1, -1)
    }
    arrived = lax.ppermute(jnp.where(first, packed[1], packed[-1]), "gx", [(0, 1), (1, 0)])
    outside = jnp.zeros_like(arrived)
    incoming = {1: jnp.where(first, outside, arrived), -1: jnp.where(first, arrived, outside)}
    arrived_flow = {}
    arrived_scalar = {}
    for heading in (1, -1):
        flow_planes, scalar_planes = leaving[heading]
        arrived_flow[heading] = edge_fill(
            incoming[heading][:split_at].reshape(flow_planes.shape), heading
        )
        arrived_scalar[heading] = incoming[heading][split_at:].reshape(scalar_planes.shape)
    flow = displace(flow, flow_vectors, 0, 2, arrived_flow[1], arrived_flow[-1])
    return (flow, arrived_scalar)


def flow_section(flow, component, flow_dim, sender, edge_fill):
    arrived = {}
    for heading in (1, -1):
        planes = edge_planes(flow, flow_vectors, component, flow_dim, heading)
        arrived[heading] = edge_fill(sender(planes, heading), heading)
    return displace(flow, flow_vectors, component, flow_dim, arrived[1], arrived[-1])


def on_device(flow_pops, concentration, solid_mask, source_cell, source_scalar, source_rate):
    row_index = lax.axis_index("row")
    slab_depth = flow_pops.shape[2]
    scalars_here, span_y, depth, span_x = concentration.shape
    height = lax.broadcasted_iota(jnp.int32, solid_mask.shape, 1)
    solid = (solid_mask == 1) | (height == 0) | (height == depth - 1)
    total_x = span_x * lax.axis_size("gx")
    cell_y = source_cell // (depth * total_x)
    cell_z = source_cell // total_x % depth
    cell_x = source_cell % total_x
    local_y = cell_y - lax.axis_index("gy") * span_y
    local_x = cell_x - lax.axis_index("gx") * span_x
    local_scalar = source_scalar - row_index * scalars_here
    count = source_cell.shape[0]
    plane_shape = (scalars_here, span_y, depth, count)
    hit = (
        (lax.broadcasted_iota(jnp.int32, plane_shape, 0) == local_scalar)
        & (lax.broadcasted_iota(jnp.int32, plane_shape, 1) == local_y)
        & (lax.broadcasted_iota(jnp.int32, plane_shape, 2) == cell_z)
    )
    weights = jnp.where(hit, source_rate, 0.0).reshape(-1, count)
    columns = (
        lax.broadcasted_iota(jnp.int32, (count, span_x), 1) == local_x[:, None]
    ).astype(jnp.float32)
    source = jnp.dot(
        weights, columns, precision=lax.Precision.HIGHEST, preferred_element_type=jnp.float32
    ).reshape(concentration.shape)
    solid_flag = solid.astype(jnp.int32)
    flow_solid = lax.dynamic_slice_in_dim(solid, row_index * slab_depth, slab_depth, 1)
    rows = lax.axis_size("row")
    flow = [flow_pops[member] for member in range(19)]
    scalars = concentration
    halos = None
    for time_step in range(STEPS):
        flow, motion = flow_collide(flow, flow_solid)
        rising = edge_planes(flow, flow_vectors, 2, 1, 1)
        sinking = edge_planes(flow, flow_vectors, 2, 1, -1)
        payload = jnp.concatenate([motion.reshape(-1), rising.reshape(-1), sinking.reshape(-1)], 0)
        everyone = copy_for_each(payload, "row")
        column = in_order(everyone[:, : motion.size].reshape((rows,) + motion.shape), 2)
        below = lax.dynamic_index_in_dim(everyone, jnp.maximum(row_index - 1, 0), 0, False)
        above = lax.dynamic_index_in_dim(everyone, jnp.minimum(row_index + 1, rows - 1), 0, False)
        from_below = jnp.where(
            row_index == 0, 0.0, below[motion.size : motion.size + rising.size]
        ).reshape(rising.shape)
        from_above = jnp.where(
            row_index == rows - 1, 0.0, above[motion.size + rising.size :]
        ).reshape(sinking.shape)
        mode = "first" if time_step == 0 else "middle"
        scalars, sides = scalar_stage(mode, scalars, halos, column, solid_flag, source)
        flow = displace(flow, flow_vectors, 2, 1, from_below, from_above)
        leaving_y = {1: scalars[3, :, span_y - 1], -1: scalars[4, :, 0]}
        flow, arrived_y = packed_section(flow, leaving_y, 1, 0, send_spanwise, keep_spanwise, True)
        leaving_x = {1: sides[:, :, 0], -1: sides[:, :, 1]}
        if lax.axis_size("gx") == 2:
            flow, arrived_x = swapped_section(flow, leaving_x, send_streamwise, inflow_fill)
        else:
            flow, arrived_x = packed_section(
                flow, leaving_x, 0, 2, send_streamwise, inflow_fill, False
            )
        halos = (jnp.stack([arrived_x[1], arrived_x[-1]], 2), arrived_y[1], arrived_y[-1])
    amount = scalar_stage("final", scalars, halos, None, None, None)
    stacked = jnp.stack(flow)
    return (stacked, amount)


def solution(mesh):
    in_specs = (
        P(None, "gy", "row", "gx"),
        P("row", "gy", None, "gx"),
        P("gy", None, "gx"),
        P(),
        P(),
        P(),
    )
    out_specs = (P(None, "gy", "row", "gx"), P("row", "gy", None, "gx"))
    return jax.shard_map(
        on_device, mesh=mesh, in_specs=in_specs, out_specs=out_specs, check_vma=False
    )
```

```python
import math

import jax
import jax.numpy as jnp
from jax import lax
from jax.sharding import PartitionSpec as P
from jax.experimental import pallas as pl
from jax.experimental.pallas import tpu as pltpu

STEPS = 3


flow_vectors = (
    (0, 0, 0),
    (1, 0, 0),
    (-1, 0, 0),
    (0, 1, 0),
    (0, -1, 0),
    (0, 0, 1),
    (0, 0, -1),
    (1, 1, 0),
    (-1, -1, 0),
    (1, -1, 0),
    (-1, 1, 0),
    (1, 0, 1),
    (-1, 0, -1),
    (1, 0, -1),
    (-1, 0, 1),
    (0, 1, 1),
    (0, -1, -1),
    (0, 1, -1),
    (0, -1, 1),
)
scalar_vectors = flow_vectors[:7]
flow_weights = (1.0 / 3.0,) + (1.0 / 18.0,) * 6 + (1.0 / 36.0,) * 12
flow_mirror = (0, 2, 1, 4, 3, 6, 5, 8, 7, 10, 9, 12, 11, 14, 13, 16, 15, 18, 17)
scalar_weights = (0.25,) + (0.125,) * 6
tau_base = 0.52
smag_const = 0.17
tau_scalar_base = 0.55
schmidt_turb = 0.7
inflow_speed = 0.08


def passed_along(block, axis, distance):
    devices = range(lax.axis_size(axis))
    route = [(i - distance, i) for i in devices if i - distance in devices]
    return lax.ppermute(block, axis, route)


def from_behind(value, axis, steps):
    count = lax.axis_size(axis)
    pairs = [(source, (source + steps) % count) for source in range(count)]
    return lax.ppermute(value, axis, pairs)


def in_order(tiles, dim):
    tiles = jnp.moveaxis(tiles, 0, dim)
    shape = tiles.shape
    return tiles.reshape(*shape[:dim], shape[dim] * shape[dim + 1], *shape[dim + 2 :])


def copy_for_each(x, axis):
    copies = jnp.broadcast_to(x, (lax.axis_size(axis), *x.shape))
    return lax.all_to_all(copies, axis, split_axis=0, concat_axis=0, tiled=True)


def gathered_copies(x, axis, dim):
    return in_order(copy_for_each(x, axis), dim)


def far_field(member):
    along = flow_vectors[member][0] * inflow_speed
    return flow_weights[member] * (
        1.0 + 3.0 * along + 4.5 * along * along - 1.5 * inflow_speed * inflow_speed
    )


def flow_collide(populations, solid):
    density = populations[0]
    for member in range(1, 19):
        density = density + populations[member]
    speeds = []
    for component in range(3):
        moment = jnp.zeros_like(density)
        for member in range(19):
            factor = flow_vectors[member][component]
            if factor != 0:
                moment = moment + factor * populations[member]
        speeds.append(moment / density)
    square = speeds[0] * speeds[0] + speeds[1] * speeds[1] + speeds[2] * speeds[2]
    equilibria = []
    for member in range(19):
        vector = flow_vectors[member]
        project = vector[0] * speeds[0] + vector[1] * speeds[1] + vector[2] * speeds[2]
        equilibria.append(
            flow_weights[member]
            * density
            * (1.0 + 3.0 * project + 4.5 * project * project - 1.5 * square)
        )
    stress = jnp.zeros_like(density)
    for first_axis in range(3):
        for second_axis in range(3):
            tensor = jnp.zeros_like(density)
            for member in range(19):
                factor = flow_vectors[member][first_axis] * flow_vectors[member][second_axis]
                if factor != 0:
                    tensor = tensor + factor * (populations[member] - equilibria[member])
            stress = stress + tensor * tensor
    relaxation = 0.5 * (
        tau_base
        + jnp.sqrt(
            tau_base * tau_base
            + 18.0 * math.sqrt(2.0) * smag_const * smag_const * jnp.sqrt(stress) / density
        )
    )
    eddy = (relaxation - tau_base) / 3.0
    fluid_part = jnp.where(solid, jnp.zeros_like(density), jnp.ones_like(density))
    updated = []
    for member in range(19):
        relaxed = populations[member] - (populations[member] - equilibria[member]) / relaxation
        updated.append(jnp.where(solid, populations[flow_mirror[member]], relaxed))
    motion = jnp.stack(
        [speeds[0] * fluid_part, speeds[1] * fluid_part, speeds[2] * fluid_part, eddy * fluid_part]
    )
    return (updated, motion)


def scalar_collide(scalar, motion, solid, source):
    amount = scalar[0]
    for member in range(1, 7):
        amount = amount + scalar[member]
    relaxation = tau_scalar_base + 4.0 * motion[3] / schmidt_turb
    updated = []
    for member in range(7):
        vector = flow_vectors[member]
        project = vector[0] * motion[0] + vector[1] * motion[1] + vector[2] * motion[2]
        equilibrium = scalar_weights[member] * amount * (1.0 + 4.0 * project)
        relaxed = (
            scalar[member]
            - (scalar[member] - equilibrium) / relaxation
            + scalar_weights[member] * source
        )
        updated.append(jnp.where(solid, scalar[flow_mirror[member]], relaxed))
    return updated


def edge_planes(pieces, vectors, component, dimension, heading):
    planes = []
    for member in range(len(pieces)):
        if vectors[member][component] == heading:
            length = pieces[member].shape[dimension]
            position = length - 1 if heading == 1 else 0
            planes.append(lax.index_in_dim(pieces[member], position, dimension, keepdims=False))
    return jnp.stack(planes)


def displace(pieces, vectors, component, dimension, from_low, from_high):
    result = []
    low_count = 0
    high_count = 0
    for member in range(len(pieces)):
        piece = pieces[member]
        length = piece.shape[dimension]
        heading = vectors[member][component]
        if heading == 1:
            entering = jnp.expand_dims(from_low[low_count], dimension)
            low_count = low_count + 1
            result.append(
                jnp.concatenate(
                    [entering, lax.slice_in_dim(piece, 0, length - 1, axis=dimension)], dimension
                )
            )
        elif heading == -1:
            entering = jnp.expand_dims(from_high[high_count], dimension)
            high_count = high_count + 1
            result.append(
                jnp.concatenate(
                    [lax.slice_in_dim(piece, 1, length, axis=dimension), entering], dimension
                )
            )
        else:
            result.append(piece)
    return result


def local_vertical(pieces, vectors, dimension):
    from_low = jnp.zeros_like(edge_planes(pieces, vectors, 2, dimension, 1))
    from_high = jnp.zeros_like(edge_planes(pieces, vectors, 2, dimension, -1))
    return displace(pieces, vectors, 2, dimension, from_low, from_high)


def send_vertical(planes, offset):
    return passed_along(planes, "row", offset)


def send_spanwise(packed, offset):
    return from_behind(packed, "gy", offset)


def send_streamwise(packed, offset):
    return passed_along(packed, "gx", offset)


def keep_spanwise(flow_in, heading):
    return flow_in


def inflow_fill(flow_in, heading):
    boundary = 0 if heading == 1 else lax.axis_size("gx") - 1
    members = [member for member in range(19) if flow_vectors[member][0] == heading]
    values = jnp.array([far_field(member) for member in members], jnp.float32).reshape(-1, 1, 1)
    return jnp.where(lax.axis_index("gx") == boundary, values + jnp.zeros_like(flow_in), flow_in)


def cross_section(flow, scalar, component, flow_dim, sender, edge_fill, keep_rows):
    arrived_flow = {}
    arrived_scalar = {}
    for heading in (1, -1):
        flow_planes = edge_planes(flow, flow_vectors, component, flow_dim, heading)
        scalar_planes = edge_planes(scalar, scalar_vectors, component, flow_dim + 1, heading)
        if keep_rows:
            width = flow_planes.shape[-1]
            packed = jnp.concatenate(
                [flow_planes.reshape(-1, width), scalar_planes.reshape(-1, width)], 0
            )
            split_at = flow_planes.size // width
        else:
            packed = jnp.concatenate([flow_planes.reshape(-1), scalar_planes.reshape(-1)], 0)
            split_at = flow_planes.size
        arrived = sender(packed, heading)
        arrived_flow[heading] = edge_fill(arrived[:split_at].reshape(flow_planes.shape), heading)
        arrived_scalar[heading] = arrived[split_at:].reshape(scalar_planes.shape)
    flow = displace(flow, flow_vectors, component, flow_dim, arrived_flow[1], arrived_flow[-1])
    scalar = displace(
        scalar, scalar_vectors, component, flow_dim + 1, arrived_scalar[1], arrived_scalar[-1]
    )
    return (flow, scalar)


def scalar_kernel(mode, span_y, depth, span_x):
    exact = lax.Precision.HIGHEST

    def body(*refs):
        if mode == "first":
            conc_ref, motion_ref, solid_ref, source_ref, out_ref, edge_ref = refs
        elif mode == "middle":
            (g_ref, side_ref, lo_y_ref, hi_y_ref,
             motion_ref, solid_ref, source_ref, out_ref, edge_ref) = refs
        else:
            g_ref, side_ref, lo_y_ref, hi_y_ref, out_ref = refs
        lane = lax.broadcasted_iota(jnp.int32, (depth, span_x), 1)
        level = lax.broadcasted_iota(jnp.int32, (depth, span_x), 0)
        pick_lane = lax.broadcasted_iota(jnp.int32, (8, span_x), 1)
        pick_high = (pick_lane == span_x - 1).astype(jnp.float32)
        pick_low = (pick_lane == 0).astype(jnp.float32)
        edge_row = lax.broadcasted_iota(jnp.int32, (2, depth), 0)
        by_lanes = (((1,), (1,)), ((), ()))
        for y in range(span_y):
            if mode == "first":
                block = conc_ref[0, y]
                scalar = [scalar_weights[member] * block for member in range(7)]
            else:
                side = jnp.transpose(side_ref[0, y])[0:depth]
                column = jnp.where(lane == 0, side[:, 0:1], side[:, 1:2])
                moved_x = pltpu.roll(g_ref[1, 0, y], 1, 1)
                back_x = pltpu.roll(g_ref[2, 0, y], span_x - 1, 1)
                moved_z = pltpu.roll(g_ref[5, 0, y], 1, 0)
                back_z = pltpu.roll(g_ref[6, 0, y], depth - 1, 0)
                scalar = [
                    g_ref[0, 0, y],
                    jnp.where(lane == 0, column, moved_x),
                    jnp.where(lane == span_x - 1, column, back_x),
                    g_ref[3, 0, y - 1] if y > 0 else lo_y_ref[0],
                    g_ref[4, 0, y + 1] if y < span_y - 1 else hi_y_ref[0],
                    jnp.where(level == 0, 0.0, moved_z),
                    jnp.where(level == depth - 1, 0.0, back_z),
                ]
            amount = scalar[0]
            for member in range(1, 7):
                amount = amount + scalar[member]
            if mode == "final":
                out_ref[0, y] = amount
                continue
            speeds = [motion_ref[component, y] for component in range(3)]
            relaxation = tau_scalar_base + 4.0 * motion_ref[3, y] / schmidt_turb
            solid = solid_ref[y] != 0
            source = source_ref[0, y]
            post = []
            for member in range(7):
                vector = flow_vectors[member]
                project = vector[0] * speeds[0] + vector[1] * speeds[1] + vector[2] * speeds[2]
                equilibrium = scalar_weights[member] * amount * (1.0 + 4.0 * project)
                relaxed = (
                    scalar[member]
                    - (scalar[member] - equilibrium) / relaxation
                    + scalar_weights[member] * source
                )
                post.append(jnp.where(solid, scalar[flow_mirror[member]], relaxed))
                out_ref[member, 0, y] = post[member]
            leaving_high = lax.dot_general(pick_high, post[1], by_lanes, precision=exact)
            leaving_low = lax.dot_general(pick_low, post[2], by_lanes, precision=exact)
            edge_ref[0, y] = jnp.where(edge_row == 0, leaving_high[0:2], leaving_low[0:2])

    return body


def scalar_stage(mode, scalars, halos, motion, solid, source):
    count, span_y, depth, span_x = source.shape if source is not None else scalars.shape[1:]
    whole = lambda shape: pl.BlockSpec(shape, lambda s: (0,) * len(shape))
    one = lambda shape: pl.BlockSpec(shape, lambda s: (s,) + (0,) * (len(shape) - 1))
    stacked = pl.BlockSpec((7, 1, span_y, depth, span_x), lambda s: (0, s, 0, 0, 0))
    cells = (span_y, depth, span_x)
    edge_specs = [one((1, span_y, 8, span_x))] + [one((1, depth, span_x))] * 2
    if mode == "first":
        operands = [scalars, motion, solid, source]
        specs = [one((1,) + cells), whole((4,) + cells), whole(cells), one((1,) + cells)]
    elif mode == "middle":
        operands = [scalars, *halos, motion, solid, source]
        specs = [stacked] + edge_specs + [whole((4,) + cells), whole(cells), one((1,) + cells)]
    else:
        operands = [scalars, *halos]
        specs = [stacked] + edge_specs
    if mode == "final":
        out_spec = one((1,) + cells)
        out_shape = jax.ShapeDtypeStruct((count,) + cells, jnp.float32)
    else:
        out_spec = [stacked, one((1, span_y, 2, depth))]
        out_shape = [
            jax.ShapeDtypeStruct((7, count) + cells, jnp.float32),
            jax.ShapeDtypeStruct((count, span_y, 2, depth), jnp.float32),
        ]
    return pl.pallas_call(
        scalar_kernel(mode, span_y, depth, span_x),
        grid=(count,),
        in_specs=specs,
        out_specs=out_spec,
        out_shape=out_shape,
    )(*operands)


def packed_section(flow, scalar_out, component, flow_dim, sender, edge_fill, keep_rows):
    arrived_flow = {}
    arrived_scalar = {}
    for heading in (1, -1):
        flow_planes = edge_planes(flow, flow_vectors, component, flow_dim, heading)
        scalar_planes = scalar_out[heading]
        if keep_rows:
            width = flow_planes.shape[-1]
            packed = jnp.concatenate(
                [flow_planes.reshape(-1, width), scalar_planes.reshape(-1, width)], 0
            )
            split_at = flow_planes.size // width
        else:
            packed = jnp.concatenate([flow_planes.reshape(-1), scalar_planes.reshape(-1)], 0)
            split_at = flow_planes.size
        arrived = sender(packed, heading)
        arrived_flow[heading] = edge_fill(arrived[:split_at].reshape(flow_planes.shape), heading)
        arrived_scalar[heading] = arrived[split_at:].reshape(scalar_planes.shape)
    flow = displace(flow, flow_vectors, component, flow_dim, arrived_flow[1], arrived_flow[-1])
    return (flow, arrived_scalar)


def swapped_section(flow, scalar_out, sender, edge_fill):
    first = lax.axis_index("gx") == 0
    leaving = {}
    for heading in (1, -1):
        flow_planes = edge_planes(flow, flow_vectors, 0, 2, heading)
        leaving[heading] = (flow_planes, scalar_out[heading])
    split_at = leaving[1][0].size
    packed = {
        heading: jnp.concatenate([part.reshape(-1) for part in leaving[heading]], 0)
        for heading in (1, -1)
    }
    arrived = lax.ppermute(jnp.where(first, packed[1], packed[-1]), "gx", [(0, 1), (1, 0)])
    outside = jnp.zeros_like(arrived)
    incoming = {1: jnp.where(first, outside, arrived), -1: jnp.where(first, arrived, outside)}
    arrived_flow = {}
    arrived_scalar = {}
    for heading in (1, -1):
        flow_planes, scalar_planes = leaving[heading]
        arrived_flow[heading] = edge_fill(
            incoming[heading][:split_at].reshape(flow_planes.shape), heading
        )
        arrived_scalar[heading] = incoming[heading][split_at:].reshape(scalar_planes.shape)
    flow = displace(flow, flow_vectors, 0, 2, arrived_flow[1], arrived_flow[-1])
    return (flow, arrived_scalar)


def flow_section(flow, component, flow_dim, sender, edge_fill):
    arrived = {}
    for heading in (1, -1):
        planes = edge_planes(flow, flow_vectors, component, flow_dim, heading)
        arrived[heading] = edge_fill(sender(planes, heading), heading)
    return displace(flow, flow_vectors, component, flow_dim, arrived[1], arrived[-1])


def on_device(flow_pops, concentration, solid_mask, source_cell, source_scalar, source_rate):
    row_index = lax.axis_index("row")
    slab_depth = flow_pops.shape[2]
    scalars_here, span_y, depth, span_x = concentration.shape
    height = lax.broadcasted_iota(jnp.int32, solid_mask.shape, 1)
    solid = (solid_mask == 1) | (height == 0) | (height == depth - 1)
    total_x = span_x * lax.axis_size("gx")
    cell_y = source_cell // (depth * total_x)
    cell_z = source_cell // total_x % depth
    cell_x = source_cell % total_x
    local_y = cell_y - lax.axis_index("gy") * span_y
    local_x = cell_x - lax.axis_index("gx") * span_x
    local_scalar = source_scalar - row_index * scalars_here
    count = source_cell.shape[0]
    plane_shape = (scalars_here, span_y, depth, count)
    hit = (
        (lax.broadcasted_iota(jnp.int32, plane_shape, 0) == local_scalar)
        & (lax.broadcasted_iota(jnp.int32, plane_shape, 1) == local_y)
        & (lax.broadcasted_iota(jnp.int32, plane_shape, 2) == cell_z)
    )
    weights = jnp.where(hit, source_rate, 0.0).reshape(-1, count)
    columns = (
        lax.broadcasted_iota(jnp.int32, (count, span_x), 1) == local_x[:, None]
    ).astype(jnp.float32)
    source = jnp.dot(
        weights, columns, precision=lax.Precision.HIGHEST, preferred_element_type=jnp.float32
    ).reshape(concentration.shape)
    solid_flag = solid.astype(jnp.int32)
    flow_solid = lax.dynamic_slice_in_dim(solid, row_index * slab_depth, slab_depth, 1)
    rows = lax.axis_size("row")
    flow = [flow_pops[member] for member in range(19)]
    scalars = concentration
    halos = None
    for time_step in range(STEPS):
        flow, motion = flow_collide(flow, flow_solid)
        rising = edge_planes(flow, flow_vectors, 2, 1, 1)
        sinking = edge_planes(flow, flow_vectors, 2, 1, -1)
        payload = jnp.concatenate([motion.reshape(-1), rising.reshape(-1), sinking.reshape(-1)], 0)
        everyone = copy_for_each(payload, "row")
        column = in_order(everyone[:, : motion.size].reshape((rows,) + motion.shape), 2)
        below = lax.dynamic_index_in_dim(everyone, jnp.maximum(row_index - 1, 0), 0, False)
        above = lax.dynamic_index_in_dim(everyone, jnp.minimum(row_index + 1, rows - 1), 0, False)
        from_below = jnp.where(
            row_index == 0, 0.0, below[motion.size : motion.size + rising.size]
        ).reshape(rising.shape)
        from_above = jnp.where(
            row_index == rows - 1, 0.0, above[motion.size + rising.size :]
        ).reshape(sinking.shape)
        mode = "first" if time_step == 0 else "middle"
        scalars, sides = scalar_stage(mode, scalars, halos, column, solid_flag, source)
        flow = displace(flow, flow_vectors, 2, 1, from_below, from_above)
        leaving_y = {1: scalars[3, :, span_y - 1], -1: scalars[4, :, 0]}
        flow, arrived_y = packed_section(flow, leaving_y, 1, 0, send_spanwise, keep_spanwise, True)
        leaving_x = {1: sides[:, :, 0], -1: sides[:, :, 1]}
        if lax.axis_size("gx") == 2:
            flow, arrived_x = swapped_section(flow, leaving_x, send_streamwise, inflow_fill)
        else:
            flow, arrived_x = packed_section(
                flow, leaving_x, 0, 2, send_streamwise, inflow_fill, False
            )
        sides = jnp.stack([arrived_x[1], arrived_x[-1]], 2)
        sides = jnp.pad(sides, ((0, 0), (0, 0), (0, 6), (0, span_x - depth)))
        halos = (sides, arrived_y[1], arrived_y[-1])
    amount = scalar_stage("final", scalars, halos, None, None, None)
    stacked = jnp.stack(flow)
    return (stacked, amount)


def solution(mesh):
    in_specs = (
        P(None, "gy", "row", "gx"),
        P("row", "gy", None, "gx"),
        P("gy", None, "gx"),
        P(),
        P(),
        P(),
    )
    out_specs = (P(None, "gy", "row", "gx"), P("row", "gy", None, "gx"))
    return jax.shard_map(
        on_device, mesh=mesh, in_specs=in_specs, out_specs=out_specs, check_vma=False
    )
```

```python
import math

import jax
import jax.numpy as jnp
from jax import lax
from jax.sharding import PartitionSpec as P
from jax.experimental import pallas as pl
from jax.experimental.pallas import tpu as pltpu

STEPS = 3


flow_vectors = (
    (0, 0, 0),
    (1, 0, 0),
    (-1, 0, 0),
    (0, 1, 0),
    (0, -1, 0),
    (0, 0, 1),
    (0, 0, -1),
    (1, 1, 0),
    (-1, -1, 0),
    (1, -1, 0),
    (-1, 1, 0),
    (1, 0, 1),
    (-1, 0, -1),
    (1, 0, -1),
    (-1, 0, 1),
    (0, 1, 1),
    (0, -1, -1),
    (0, 1, -1),
    (0, -1, 1),
)
scalar_vectors = flow_vectors[:7]
flow_weights = (1.0 / 3.0,) + (1.0 / 18.0,) * 6 + (1.0 / 36.0,) * 12
flow_mirror = (0, 2, 1, 4, 3, 6, 5, 8, 7, 10, 9, 12, 11, 14, 13, 16, 15, 18, 17)
scalar_weights = (0.25,) + (0.125,) * 6
tau_base = 0.52
smag_const = 0.17
tau_scalar_base = 0.55
schmidt_turb = 0.7
inflow_speed = 0.08


def passed_along(block, axis, distance):
    devices = range(lax.axis_size(axis))
    route = [(i - distance, i) for i in devices if i - distance in devices]
    return lax.ppermute(block, axis, route)


def from_behind(value, axis, steps):
    count = lax.axis_size(axis)
    pairs = [(source, (source + steps) % count) for source in range(count)]
    return lax.ppermute(value, axis, pairs)


def in_order(tiles, dim):
    tiles = jnp.moveaxis(tiles, 0, dim)
    shape = tiles.shape
    return tiles.reshape(*shape[:dim], shape[dim] * shape[dim + 1], *shape[dim + 2 :])


def copy_for_each(x, axis):
    copies = jnp.broadcast_to(x, (lax.axis_size(axis), *x.shape))
    return lax.all_to_all(copies, axis, split_axis=0, concat_axis=0, tiled=True)


def gathered_copies(x, axis, dim):
    return in_order(copy_for_each(x, axis), dim)


def far_field(member):
    along = flow_vectors[member][0] * inflow_speed
    return flow_weights[member] * (
        1.0 + 3.0 * along + 4.5 * along * along - 1.5 * inflow_speed * inflow_speed
    )


def flow_collide(populations, solid):
    density = populations[0]
    for member in range(1, 19):
        density = density + populations[member]
    speeds = []
    for component in range(3):
        moment = jnp.zeros_like(density)
        for member in range(19):
            factor = flow_vectors[member][component]
            if factor != 0:
                moment = moment + factor * populations[member]
        speeds.append(moment / density)
    square = speeds[0] * speeds[0] + speeds[1] * speeds[1] + speeds[2] * speeds[2]
    equilibria = []
    for member in range(19):
        vector = flow_vectors[member]
        project = vector[0] * speeds[0] + vector[1] * speeds[1] + vector[2] * speeds[2]
        equilibria.append(
            flow_weights[member]
            * density
            * (1.0 + 3.0 * project + 4.5 * project * project - 1.5 * square)
        )
    stress = jnp.zeros_like(density)
    for first_axis in range(3):
        for second_axis in range(3):
            tensor = jnp.zeros_like(density)
            for member in range(19):
                factor = flow_vectors[member][first_axis] * flow_vectors[member][second_axis]
                if factor != 0:
                    tensor = tensor + factor * (populations[member] - equilibria[member])
            stress = stress + tensor * tensor
    relaxation = 0.5 * (
        tau_base
        + jnp.sqrt(
            tau_base * tau_base
            + 18.0 * math.sqrt(2.0) * smag_const * smag_const * jnp.sqrt(stress) / density
        )
    )
    eddy = (relaxation - tau_base) / 3.0
    fluid_part = jnp.where(solid, jnp.zeros_like(density), jnp.ones_like(density))
    updated = []
    for member in range(19):
        relaxed = populations[member] - (populations[member] - equilibria[member]) / relaxation
        updated.append(jnp.where(solid, populations[flow_mirror[member]], relaxed))
    motion = jnp.stack(
        [speeds[0] * fluid_part, speeds[1] * fluid_part, speeds[2] * fluid_part, eddy * fluid_part]
    )
    return (updated, motion)


def scalar_collide(scalar, motion, solid, source):
    amount = scalar[0]
    for member in range(1, 7):
        amount = amount + scalar[member]
    relaxation = tau_scalar_base + 4.0 * motion[3] / schmidt_turb
    updated = []
    for member in range(7):
        vector = flow_vectors[member]
        project = vector[0] * motion[0] + vector[1] * motion[1] + vector[2] * motion[2]
        equilibrium = scalar_weights[member] * amount * (1.0 + 4.0 * project)
        relaxed = (
            scalar[member]
            - (scalar[member] - equilibrium) / relaxation
            + scalar_weights[member] * source
        )
        updated.append(jnp.where(solid, scalar[flow_mirror[member]], relaxed))
    return updated


def edge_planes(pieces, vectors, component, dimension, heading):
    planes = []
    for member in range(len(pieces)):
        if vectors[member][component] == heading:
            length = pieces[member].shape[dimension]
            position = length - 1 if heading == 1 else 0
            planes.append(lax.index_in_dim(pieces[member], position, dimension, keepdims=False))
    return jnp.stack(planes)


def displace(pieces, vectors, component, dimension, from_low, from_high):
    result = []
    low_count = 0
    high_count = 0
    for member in range(len(pieces)):
        piece = pieces[member]
        length = piece.shape[dimension]
        heading = vectors[member][component]
        if heading == 1:
            entering = jnp.expand_dims(from_low[low_count], dimension)
            low_count = low_count + 1
            result.append(
                jnp.concatenate(
                    [entering, lax.slice_in_dim(piece, 0, length - 1, axis=dimension)], dimension
                )
            )
        elif heading == -1:
            entering = jnp.expand_dims(from_high[high_count], dimension)
            high_count = high_count + 1
            result.append(
                jnp.concatenate(
                    [lax.slice_in_dim(piece, 1, length, axis=dimension), entering], dimension
                )
            )
        else:
            result.append(piece)
    return result


def local_vertical(pieces, vectors, dimension):
    from_low = jnp.zeros_like(edge_planes(pieces, vectors, 2, dimension, 1))
    from_high = jnp.zeros_like(edge_planes(pieces, vectors, 2, dimension, -1))
    return displace(pieces, vectors, 2, dimension, from_low, from_high)


def send_vertical(planes, offset):
    return passed_along(planes, "row", offset)


def send_spanwise(packed, offset):
    return from_behind(packed, "gy", offset)


def send_streamwise(packed, offset):
    return passed_along(packed, "gx", offset)


def keep_spanwise(flow_in, heading):
    return flow_in


def inflow_fill(flow_in, heading):
    boundary = 0 if heading == 1 else lax.axis_size("gx") - 1
    members = [member for member in range(19) if flow_vectors[member][0] == heading]
    values = jnp.array([far_field(member) for member in members], jnp.float32).reshape(-1, 1, 1)
    return jnp.where(lax.axis_index("gx") == boundary, values + jnp.zeros_like(flow_in), flow_in)


def cross_section(flow, scalar, component, flow_dim, sender, edge_fill, keep_rows):
    arrived_flow = {}
    arrived_scalar = {}
    for heading in (1, -1):
        flow_planes = edge_planes(flow, flow_vectors, component, flow_dim, heading)
        scalar_planes = edge_planes(scalar, scalar_vectors, component, flow_dim + 1, heading)
        if keep_rows:
            width = flow_planes.shape[-1]
            packed = jnp.concatenate(
                [flow_planes.reshape(-1, width), scalar_planes.reshape(-1, width)], 0
            )
            split_at = flow_planes.size // width
        else:
            packed = jnp.concatenate([flow_planes.reshape(-1), scalar_planes.reshape(-1)], 0)
            split_at = flow_planes.size
        arrived = sender(packed, heading)
        arrived_flow[heading] = edge_fill(arrived[:split_at].reshape(flow_planes.shape), heading)
        arrived_scalar[heading] = arrived[split_at:].reshape(scalar_planes.shape)
    flow = displace(flow, flow_vectors, component, flow_dim, arrived_flow[1], arrived_flow[-1])
    scalar = displace(
        scalar, scalar_vectors, component, flow_dim + 1, arrived_scalar[1], arrived_scalar[-1]
    )
    return (flow, scalar)


def scalar_kernel(mode, span_y, depth, span_x):
    def body(*refs):
        if mode == "first":
            conc_ref, motion_ref, solid_ref, source_ref, out_ref = refs
        elif mode == "middle":
            (g_ref, lo_x_ref, hi_x_ref, lo_y_ref, hi_y_ref,
             motion_ref, solid_ref, source_ref, out_ref) = refs
        else:
            g_ref, lo_x_ref, hi_x_ref, lo_y_ref, hi_y_ref, out_ref = refs
        lane = lax.broadcasted_iota(jnp.int32, (depth, span_x), 1)
        level = lax.broadcasted_iota(jnp.int32, (depth, span_x), 0)
        for y in range(span_y):
            if mode == "first":
                block = conc_ref[0, y]
                scalar = [scalar_weights[member] * block for member in range(7)]
            else:
                moved_x = pltpu.roll(g_ref[1, 0, y], 1, 1)
                back_x = pltpu.roll(g_ref[2, 0, y], span_x - 1, 1)
                moved_z = pltpu.roll(g_ref[5, 0, y], 1, 0)
                back_z = pltpu.roll(g_ref[6, 0, y], depth - 1, 0)
                scalar = [
                    g_ref[0, 0, y],
                    jnp.where(lane == 0, lo_x_ref[0, y], moved_x),
                    jnp.where(lane == span_x - 1, hi_x_ref[0, y], back_x),
                    g_ref[3, 0, y - 1] if y > 0 else lo_y_ref[0],
                    g_ref[4, 0, y + 1] if y < span_y - 1 else hi_y_ref[0],
                    jnp.where(level == 0, 0.0, moved_z),
                    jnp.where(level == depth - 1, 0.0, back_z),
                ]
            amount = scalar[0]
            for member in range(1, 7):
                amount = amount + scalar[member]
            if mode == "final":
                out_ref[0, y] = amount
                continue
            speeds = [motion_ref[component, y] for component in range(3)]
            relaxation = tau_scalar_base + 4.0 * motion_ref[3, y] / schmidt_turb
            solid = solid_ref[y] != 0
            source = source_ref[0, y]
            for member in range(7):
                vector = flow_vectors[member]
                project = vector[0] * speeds[0] + vector[1] * speeds[1] + vector[2] * speeds[2]
                equilibrium = scalar_weights[member] * amount * (1.0 + 4.0 * project)
                relaxed = (
                    scalar[member]
                    - (scalar[member] - equilibrium) / relaxation
                    + scalar_weights[member] * source
                )
                out_ref[member, 0, y] = jnp.where(solid, scalar[flow_mirror[member]], relaxed)

    return body


def scalar_stage(mode, scalars, halos, motion, solid, source):
    count, span_y, depth, span_x = source.shape if source is not None else scalars.shape[1:]
    whole = lambda shape: pl.BlockSpec(shape, lambda s: (0,) * len(shape))
    one = lambda shape: pl.BlockSpec(shape, lambda s: (s,) + (0,) * (len(shape) - 1))
    stacked = pl.BlockSpec((7, 1, span_y, depth, span_x), lambda s: (0, s, 0, 0, 0))
    cells = (span_y, depth, span_x)
    edge_specs = [one((1, span_y, depth, 1))] * 2 + [one((1, depth, span_x))] * 2
    if mode == "first":
        operands = [scalars, motion, solid, source]
        specs = [one((1,) + cells), whole((4,) + cells), whole(cells), one((1,) + cells)]
    elif mode == "middle":
        operands = [scalars, *halos, motion, solid, source]
        specs = [stacked] + edge_specs + [whole((4,) + cells), whole(cells), one((1,) + cells)]
    else:
        operands = [scalars, *halos]
        specs = [stacked] + edge_specs
    if mode == "final":
        out_spec = one((1,) + cells)
        out_shape = jax.ShapeDtypeStruct((count,) + cells, jnp.float32)
    else:
        out_spec = stacked
        out_shape = jax.ShapeDtypeStruct((7, count) + cells, jnp.float32)
    return pl.pallas_call(
        scalar_kernel(mode, span_y, depth, span_x),
        grid=(count,),
        in_specs=specs,
        out_specs=out_spec,
        out_shape=out_shape,
    )(*operands)


def packed_section(flow, scalar_out, component, flow_dim, sender, edge_fill, keep_rows):
    arrived_flow = {}
    arrived_scalar = {}
    for heading in (1, -1):
        flow_planes = edge_planes(flow, flow_vectors, component, flow_dim, heading)
        scalar_planes = scalar_out[heading]
        if keep_rows:
            width = flow_planes.shape[-1]
            packed = jnp.concatenate(
                [flow_planes.reshape(-1, width), scalar_planes.reshape(-1, width)], 0
            )
            split_at = flow_planes.size // width
        else:
            packed = jnp.concatenate([flow_planes.reshape(-1), scalar_planes.reshape(-1)], 0)
            split_at = flow_planes.size
        arrived = sender(packed, heading)
        arrived_flow[heading] = edge_fill(arrived[:split_at].reshape(flow_planes.shape), heading)
        arrived_scalar[heading] = arrived[split_at:].reshape(scalar_planes.shape)
    flow = displace(flow, flow_vectors, component, flow_dim, arrived_flow[1], arrived_flow[-1])
    return (flow, arrived_scalar)


def swapped_section(flow, scalar_out, sender, edge_fill):
    first = lax.axis_index("gx") == 0
    leaving = {}
    for heading in (1, -1):
        flow_planes = edge_planes(flow, flow_vectors, 0, 2, heading)
        leaving[heading] = (flow_planes, scalar_out[heading])
    split_at = leaving[1][0].size
    packed = {
        heading: jnp.concatenate([part.reshape(-1) for part in leaving[heading]], 0)
        for heading in (1, -1)
    }
    arrived = lax.ppermute(jnp.where(first, packed[1], packed[-1]), "gx", [(0, 1), (1, 0)])
    outside = jnp.zeros_like(arrived)
    incoming = {1: jnp.where(first, outside, arrived), -1: jnp.where(first, arrived, outside)}
    arrived_flow = {}
    arrived_scalar = {}
    for heading in (1, -1):
        flow_planes, scalar_planes = leaving[heading]
        arrived_flow[heading] = edge_fill(
            incoming[heading][:split_at].reshape(flow_planes.shape), heading
        )
        arrived_scalar[heading] = incoming[heading][split_at:].reshape(scalar_planes.shape)
    flow = displace(flow, flow_vectors, 0, 2, arrived_flow[1], arrived_flow[-1])
    return (flow, arrived_scalar)


def flow_section(flow, component, flow_dim, sender, edge_fill):
    arrived = {}
    for heading in (1, -1):
        planes = edge_planes(flow, flow_vectors, component, flow_dim, heading)
        arrived[heading] = edge_fill(sender(planes, heading), heading)
    return displace(flow, flow_vectors, component, flow_dim, arrived[1], arrived[-1])


def on_device(flow_pops, concentration, solid_mask, source_cell, source_scalar, source_rate):
    row_index = lax.axis_index("row")
    slab_depth = flow_pops.shape[2]
    scalars_here, span_y, depth, span_x = concentration.shape
    height = lax.broadcasted_iota(jnp.int32, solid_mask.shape, 1)
    solid = (solid_mask == 1) | (height == 0) | (height == depth - 1)
    total_x = span_x * lax.axis_size("gx")
    cell_y = source_cell // (depth * total_x)
    cell_z = source_cell // total_x % depth
    cell_x = source_cell % total_x
    local_y = cell_y - lax.axis_index("gy") * span_y
    local_x = cell_x - lax.axis_index("gx") * span_x
    local_scalar = source_scalar - row_index * scalars_here
    count = source_cell.shape[0]
    plane_shape = (scalars_here, span_y, depth, count)
    hit = (
        (lax.broadcasted_iota(jnp.int32, plane_shape, 0) == local_scalar)
        & (lax.broadcasted_iota(jnp.int32, plane_shape, 1) == local_y)
        & (lax.broadcasted_iota(jnp.int32, plane_shape, 2) == cell_z)
    )
    weights = jnp.where(hit, source_rate, 0.0).reshape(-1, count)
    columns = (
        lax.broadcasted_iota(jnp.int32, (count, span_x), 1) == local_x[:, None]
    ).astype(jnp.float32)
    source = jnp.dot(
        weights, columns, precision=lax.Precision.HIGHEST, preferred_element_type=jnp.float32
    ).reshape(concentration.shape)
    solid_flag = solid.astype(jnp.int32)
    flow_solid = lax.dynamic_slice_in_dim(solid, row_index * slab_depth, slab_depth, 1)
    rows = lax.axis_size("row")
    flow = [flow_pops[member] for member in range(19)]
    scalars = concentration
    halos = None
    for time_step in range(STEPS):
        flow, motion = flow_collide(flow, flow_solid)
        rising = edge_planes(flow, flow_vectors, 2, 1, 1)
        sinking = edge_planes(flow, flow_vectors, 2, 1, -1)
        target = lax.broadcasted_iota(jnp.int32, (rows, 1), 0)
        planes = jnp.where(
            target == row_index + 1,
            rising.reshape(1, -1),
            jnp.where(target == row_index - 1, sinking.reshape(1, -1), 0.0),
        )
        spread = jnp.broadcast_to(motion.reshape(1, -1), (rows, motion.size))
        everyone = lax.all_to_all(
            jnp.concatenate([spread, planes], 1), "row", split_axis=0, concat_axis=0, tiled=True
        )
        column = in_order(everyone[:, : motion.size].reshape((rows,) + motion.shape), 2)
        below = lax.dynamic_index_in_dim(everyone, jnp.maximum(row_index - 1, 0), 0, False)
        above = lax.dynamic_index_in_dim(everyone, jnp.minimum(row_index + 1, rows - 1), 0, False)
        from_below = jnp.where(row_index == 0, 0.0, below[motion.size :]).reshape(rising.shape)
        from_above = jnp.where(row_index == rows - 1, 0.0, above[motion.size :]).reshape(
            sinking.shape
        )
        mode = "first" if time_step == 0 else "middle"
        scalars = scalar_stage(mode, scalars, halos, column, solid_flag, source)
        flow = displace(flow, flow_vectors, 2, 1, from_below, from_above)
        leaving_y = {1: scalars[3, :, span_y - 1], -1: scalars[4, :, 0]}
        flow, arrived_y = packed_section(flow, leaving_y, 1, 0, send_spanwise, keep_spanwise, True)
        leaving_x = {1: scalars[1, :, :, :, span_x - 1 :], -1: scalars[2, :, :, :, :1]}
        if lax.axis_size("gx") == 2:
            flow, arrived_x = swapped_section(flow, leaving_x, send_streamwise, inflow_fill)
        else:
            flow, arrived_x = packed_section(
                flow, leaving_x, 0, 2, send_streamwise, inflow_fill, False
            )
        halos = (arrived_x[1], arrived_x[-1], arrived_y[1], arrived_y[-1])
    amount = scalar_stage("final", scalars, halos, None, None, None)
    stacked = jnp.stack(flow)
    return (stacked, amount)


def solution(mesh):
    in_specs = (
        P(None, "gy", "row", "gx"),
        P("row", "gy", None, "gx"),
        P("gy", None, "gx"),
        P(),
        P(),
        P(),
    )
    out_specs = (P(None, "gy", "row", "gx"), P("row", "gy", None, "gx"))
    return jax.shard_map(
        on_device, mesh=mesh, in_specs=in_specs, out_specs=out_specs, check_vma=False
    )
```

```python
import math

import jax
import jax.numpy as jnp
from jax import lax
from jax.sharding import PartitionSpec as P
from jax.experimental import pallas as pl
from jax.experimental.pallas import tpu as pltpu

STEPS = 3


flow_vectors = (
    (0, 0, 0),
    (1, 0, 0),
    (-1, 0, 0),
    (0, 1, 0),
    (0, -1, 0),
    (0, 0, 1),
    (0, 0, -1),
    (1, 1, 0),
    (-1, -1, 0),
    (1, -1, 0),
    (-1, 1, 0),
    (1, 0, 1),
    (-1, 0, -1),
    (1, 0, -1),
    (-1, 0, 1),
    (0, 1, 1),
    (0, -1, -1),
    (0, 1, -1),
    (0, -1, 1),
)
scalar_vectors = flow_vectors[:7]
flow_weights = (1.0 / 3.0,) + (1.0 / 18.0,) * 6 + (1.0 / 36.0,) * 12
flow_mirror = (0, 2, 1, 4, 3, 6, 5, 8, 7, 10, 9, 12, 11, 14, 13, 16, 15, 18, 17)
scalar_weights = (0.25,) + (0.125,) * 6
tau_base = 0.52
smag_const = 0.17
tau_scalar_base = 0.55
schmidt_turb = 0.7
inflow_speed = 0.08


def passed_along(block, axis, distance):
    devices = range(lax.axis_size(axis))
    route = [(i - distance, i) for i in devices if i - distance in devices]
    return lax.ppermute(block, axis, route)


def from_behind(value, axis, steps):
    count = lax.axis_size(axis)
    pairs = [(source, (source + steps) % count) for source in range(count)]
    return lax.ppermute(value, axis, pairs)


def in_order(tiles, dim):
    tiles = jnp.moveaxis(tiles, 0, dim)
    shape = tiles.shape
    return tiles.reshape(*shape[:dim], shape[dim] * shape[dim + 1], *shape[dim + 2 :])


def copy_for_each(x, axis):
    copies = jnp.broadcast_to(x, (lax.axis_size(axis), *x.shape))
    return lax.all_to_all(copies, axis, split_axis=0, concat_axis=0, tiled=True)


def gathered_copies(x, axis, dim):
    return in_order(copy_for_each(x, axis), dim)


def far_field(member):
    along = flow_vectors[member][0] * inflow_speed
    return flow_weights[member] * (
        1.0 + 3.0 * along + 4.5 * along * along - 1.5 * inflow_speed * inflow_speed
    )


def flow_collide(populations, solid):
    density = populations[0]
    for member in range(1, 19):
        density = density + populations[member]
    speeds = []
    for component in range(3):
        moment = jnp.zeros_like(density)
        for member in range(19):
            factor = flow_vectors[member][component]
            if factor != 0:
                moment = moment + factor * populations[member]
        speeds.append(moment / density)
    square = speeds[0] * speeds[0] + speeds[1] * speeds[1] + speeds[2] * speeds[2]
    equilibria = []
    for member in range(19):
        vector = flow_vectors[member]
        project = vector[0] * speeds[0] + vector[1] * speeds[1] + vector[2] * speeds[2]
        equilibria.append(
            flow_weights[member]
            * density
            * (1.0 + 3.0 * project + 4.5 * project * project - 1.5 * square)
        )
    stress = jnp.zeros_like(density)
    for first_axis in range(3):
        for second_axis in range(3):
            tensor = jnp.zeros_like(density)
            for member in range(19):
                factor = flow_vectors[member][first_axis] * flow_vectors[member][second_axis]
                if factor != 0:
                    tensor = tensor + factor * (populations[member] - equilibria[member])
            stress = stress + tensor * tensor
    relaxation = 0.5 * (
        tau_base
        + jnp.sqrt(
            tau_base * tau_base
            + 18.0 * math.sqrt(2.0) * smag_const * smag_const * jnp.sqrt(stress) / density
        )
    )
    eddy = (relaxation - tau_base) / 3.0
    fluid_part = jnp.where(solid, jnp.zeros_like(density), jnp.ones_like(density))
    updated = []
    for member in range(19):
        relaxed = populations[member] - (populations[member] - equilibria[member]) / relaxation
        updated.append(jnp.where(solid, populations[flow_mirror[member]], relaxed))
    motion = jnp.stack(
        [speeds[0] * fluid_part, speeds[1] * fluid_part, speeds[2] * fluid_part, eddy * fluid_part]
    )
    return (updated, motion)


def scalar_collide(scalar, motion, solid, source):
    amount = scalar[0]
    for member in range(1, 7):
        amount = amount + scalar[member]
    relaxation = tau_scalar_base + 4.0 * motion[3] / schmidt_turb
    updated = []
    for member in range(7):
        vector = flow_vectors[member]
        project = vector[0] * motion[0] + vector[1] * motion[1] + vector[2] * motion[2]
        equilibrium = scalar_weights[member] * amount * (1.0 + 4.0 * project)
        relaxed = (
            scalar[member]
            - (scalar[member] - equilibrium) / relaxation
            + scalar_weights[member] * source
        )
        updated.append(jnp.where(solid, scalar[flow_mirror[member]], relaxed))
    return updated


def edge_planes(pieces, vectors, component, dimension, heading):
    planes = []
    for member in range(len(pieces)):
        if vectors[member][component] == heading:
            length = pieces[member].shape[dimension]
            position = length - 1 if heading == 1 else 0
            planes.append(lax.index_in_dim(pieces[member], position, dimension, keepdims=False))
    return jnp.stack(planes)


def displace(pieces, vectors, component, dimension, from_low, from_high):
    result = []
    low_count = 0
    high_count = 0
    for member in range(len(pieces)):
        piece = pieces[member]
        length = piece.shape[dimension]
        heading = vectors[member][component]
        if heading == 1:
            entering = jnp.expand_dims(from_low[low_count], dimension)
            low_count = low_count + 1
            result.append(
                jnp.concatenate(
                    [entering, lax.slice_in_dim(piece, 0, length - 1, axis=dimension)], dimension
                )
            )
        elif heading == -1:
            entering = jnp.expand_dims(from_high[high_count], dimension)
            high_count = high_count + 1
            result.append(
                jnp.concatenate(
                    [lax.slice_in_dim(piece, 1, length, axis=dimension), entering], dimension
                )
            )
        else:
            result.append(piece)
    return result


def local_vertical(pieces, vectors, dimension):
    from_low = jnp.zeros_like(edge_planes(pieces, vectors, 2, dimension, 1))
    from_high = jnp.zeros_like(edge_planes(pieces, vectors, 2, dimension, -1))
    return displace(pieces, vectors, 2, dimension, from_low, from_high)


def send_vertical(planes, offset):
    return passed_along(planes, "row", offset)


def send_spanwise(packed, offset):
    return from_behind(packed, "gy", offset)


def send_streamwise(packed, offset):
    return passed_along(packed, "gx", offset)


def keep_spanwise(flow_in, heading):
    return flow_in


def inflow_fill(flow_in, heading):
    boundary = 0 if heading == 1 else lax.axis_size("gx") - 1
    members = [member for member in range(19) if flow_vectors[member][0] == heading]
    values = jnp.array([far_field(member) for member in members], jnp.float32).reshape(-1, 1, 1)
    return jnp.where(lax.axis_index("gx") == boundary, values + jnp.zeros_like(flow_in), flow_in)


def cross_section(flow, scalar, component, flow_dim, sender, edge_fill, keep_rows):
    arrived_flow = {}
    arrived_scalar = {}
    for heading in (1, -1):
        flow_planes = edge_planes(flow, flow_vectors, component, flow_dim, heading)
        scalar_planes = edge_planes(scalar, scalar_vectors, component, flow_dim + 1, heading)
        if keep_rows:
            width = flow_planes.shape[-1]
            packed = jnp.concatenate(
                [flow_planes.reshape(-1, width), scalar_planes.reshape(-1, width)], 0
            )
            split_at = flow_planes.size // width
        else:
            packed = jnp.concatenate([flow_planes.reshape(-1), scalar_planes.reshape(-1)], 0)
            split_at = flow_planes.size
        arrived = sender(packed, heading)
        arrived_flow[heading] = edge_fill(arrived[:split_at].reshape(flow_planes.shape), heading)
        arrived_scalar[heading] = arrived[split_at:].reshape(scalar_planes.shape)
    flow = displace(flow, flow_vectors, component, flow_dim, arrived_flow[1], arrived_flow[-1])
    scalar = displace(
        scalar, scalar_vectors, component, flow_dim + 1, arrived_scalar[1], arrived_scalar[-1]
    )
    return (flow, scalar)


def scalar_kernel(mode, span_y, depth, span_x):
    exact = lax.Precision.HIGHEST

    def body(*refs):
        if mode == "first":
            conc_ref, motion_ref, solid_ref, source_ref, out_ref, edge_ref = refs
        elif mode == "middle":
            (g_ref, side_ref, lo_y_ref, hi_y_ref,
             motion_ref, solid_ref, source_ref, out_ref, edge_ref) = refs
        else:
            g_ref, side_ref, lo_y_ref, hi_y_ref, out_ref = refs
        lane = lax.broadcasted_iota(jnp.int32, (depth, span_x), 1)
        level = lax.broadcasted_iota(jnp.int32, (depth, span_x), 0)
        pick_lane = lax.broadcasted_iota(jnp.int32, (8, span_x), 1)
        pick_high = (pick_lane == span_x - 1).astype(jnp.float32)
        pick_low = (pick_lane == 0).astype(jnp.float32)
        edge_row = lax.broadcasted_iota(jnp.int32, (2, depth), 0)
        by_lanes = (((1,), (1,)), ((), ()))
        for y in range(span_y):
            if mode == "first":
                block = conc_ref[0, y]
                scalar = [scalar_weights[member] * block for member in range(7)]
            else:
                side = jnp.transpose(side_ref[0, y])[0:depth]
                column = jnp.where(lane == 0, side[:, 0:1], side[:, 1:2])
                moved_x = pltpu.roll(g_ref[1, 0, y], 1, 1)
                back_x = pltpu.roll(g_ref[2, 0, y], span_x - 1, 1)
                moved_z = pltpu.roll(g_ref[5, 0, y], 1, 0)
                back_z = pltpu.roll(g_ref[6, 0, y], depth - 1, 0)
                scalar = [
                    g_ref[0, 0, y],
                    jnp.where(lane == 0, column, moved_x),
                    jnp.where(lane == span_x - 1, column, back_x),
                    g_ref[3, 0, y - 1] if y > 0 else lo_y_ref[0],
                    g_ref[4, 0, y + 1] if y < span_y - 1 else hi_y_ref[0],
                    jnp.where(level == 0, 0.0, moved_z),
                    jnp.where(level == depth - 1, 0.0, back_z),
                ]
            amount = scalar[0]
            for member in range(1, 7):
                amount = amount + scalar[member]
            if mode == "final":
                out_ref[0, y] = amount
                continue
            speeds = [motion_ref[component, y] for component in range(3)]
            relaxation = tau_scalar_base + 4.0 * motion_ref[3, y] / schmidt_turb
            solid = solid_ref[y] != 0
            source = source_ref[0, y]
            post = []
            for member in range(7):
                vector = flow_vectors[member]
                project = vector[0] * speeds[0] + vector[1] * speeds[1] + vector[2] * speeds[2]
                equilibrium = scalar_weights[member] * amount * (1.0 + 4.0 * project)
                relaxed = (
                    scalar[member]
                    - (scalar[member] - equilibrium) / relaxation
                    + scalar_weights[member] * source
                )
                post.append(jnp.where(solid, scalar[flow_mirror[member]], relaxed))
                out_ref[member, 0, y] = post[member]
            leaving_high = lax.dot_general(pick_high, post[1], by_lanes, precision=exact)
            leaving_low = lax.dot_general(pick_low, post[2], by_lanes, precision=exact)
            edge_ref[0, y] = jnp.where(edge_row == 0, leaving_high[0:2], leaving_low[0:2])

    return body


def scalar_stage(mode, scalars, halos, motion, solid, source):
    count, span_y, depth, span_x = source.shape if source is not None else scalars.shape[1:]
    whole = lambda shape: pl.BlockSpec(shape, lambda s: (0,) * len(shape))
    one = lambda shape: pl.BlockSpec(shape, lambda s: (s,) + (0,) * (len(shape) - 1))
    stacked = pl.BlockSpec((7, 1, span_y, depth, span_x), lambda s: (0, s, 0, 0, 0))
    cells = (span_y, depth, span_x)
    edge_specs = [one((1, span_y, 8, span_x))] + [one((1, depth, span_x))] * 2
    if mode == "first":
        operands = [scalars, motion, solid, source]
        specs = [one((1,) + cells), whole((4,) + cells), whole(cells), one((1,) + cells)]
    elif mode == "middle":
        operands = [scalars, *halos, motion, solid, source]
        specs = [stacked] + edge_specs + [whole((4,) + cells), whole(cells), one((1,) + cells)]
    else:
        operands = [scalars, *halos]
        specs = [stacked] + edge_specs
    if mode == "final":
        out_spec = one((1,) + cells)
        out_shape = jax.ShapeDtypeStruct((count,) + cells, jnp.float32)
    else:
        out_spec = [stacked, one((1, span_y, 2, depth))]
        out_shape = [
            jax.ShapeDtypeStruct((7, count) + cells, jnp.float32),
            jax.ShapeDtypeStruct((count, span_y, 2, depth), jnp.float32),
        ]
    return pl.pallas_call(
        scalar_kernel(mode, span_y, depth, span_x),
        grid=(count,),
        in_specs=specs,
        out_specs=out_spec,
        out_shape=out_shape,
    )(*operands)


def packed_section(flow, scalar_out, component, flow_dim, sender, edge_fill, keep_rows):
    arrived_flow = {}
    arrived_scalar = {}
    for heading in (1, -1):
        flow_planes = edge_planes(flow, flow_vectors, component, flow_dim, heading)
        scalar_planes = scalar_out[heading]
        if keep_rows:
            width = flow_planes.shape[-1]
            packed = jnp.concatenate(
                [flow_planes.reshape(-1, width), scalar_planes.reshape(-1, width)], 0
            )
            split_at = flow_planes.size // width
        else:
            packed = jnp.concatenate([flow_planes.reshape(-1), scalar_planes.reshape(-1)], 0)
            split_at = flow_planes.size
        arrived = sender(packed, heading)
        arrived_flow[heading] = edge_fill(arrived[:split_at].reshape(flow_planes.shape), heading)
        arrived_scalar[heading] = arrived[split_at:].reshape(scalar_planes.shape)
    flow = displace(flow, flow_vectors, component, flow_dim, arrived_flow[1], arrived_flow[-1])
    return (flow, arrived_scalar)


def swapped_section(flow, scalar_out, sender, edge_fill):
    first = lax.axis_index("gx") == 0
    leaving = {}
    for heading in (1, -1):
        flow_planes = edge_planes(flow, flow_vectors, 0, 2, heading)
        leaving[heading] = (flow_planes, scalar_out[heading])
    split_at = leaving[1][0].size
    packed = {
        heading: jnp.concatenate([part.reshape(-1) for part in leaving[heading]], 0)
        for heading in (1, -1)
    }
    arrived = lax.ppermute(jnp.where(first, packed[1], packed[-1]), "gx", [(0, 1), (1, 0)])
    outside = jnp.zeros_like(arrived)
    incoming = {1: jnp.where(first, outside, arrived), -1: jnp.where(first, arrived, outside)}
    arrived_flow = {}
    arrived_scalar = {}
    for heading in (1, -1):
        flow_planes, scalar_planes = leaving[heading]
        arrived_flow[heading] = edge_fill(
            incoming[heading][:split_at].reshape(flow_planes.shape), heading
        )
        arrived_scalar[heading] = incoming[heading][split_at:].reshape(scalar_planes.shape)
    flow = displace(flow, flow_vectors, 0, 2, arrived_flow[1], arrived_flow[-1])
    return (flow, arrived_scalar)


def flow_section(flow, component, flow_dim, sender, edge_fill):
    arrived = {}
    for heading in (1, -1):
        planes = edge_planes(flow, flow_vectors, component, flow_dim, heading)
        arrived[heading] = edge_fill(sender(planes, heading), heading)
    return displace(flow, flow_vectors, component, flow_dim, arrived[1], arrived[-1])


def on_device(flow_pops, concentration, solid_mask, source_cell, source_scalar, source_rate):
    row_index = lax.axis_index("row")
    slab_depth = flow_pops.shape[2]
    scalars_here, span_y, depth, span_x = concentration.shape
    height = lax.broadcasted_iota(jnp.int32, solid_mask.shape, 1)
    solid = (solid_mask == 1) | (height == 0) | (height == depth - 1)
    total_x = span_x * lax.axis_size("gx")
    cell_y = source_cell // (depth * total_x)
    cell_z = source_cell // total_x % depth
    cell_x = source_cell % total_x
    local_y = cell_y - lax.axis_index("gy") * span_y
    local_x = cell_x - lax.axis_index("gx") * span_x
    local_scalar = source_scalar - row_index * scalars_here
    count = source_cell.shape[0]
    plane_shape = (scalars_here, span_y, depth, count)
    hit = (
        (lax.broadcasted_iota(jnp.int32, plane_shape, 0) == local_scalar)
        & (lax.broadcasted_iota(jnp.int32, plane_shape, 1) == local_y)
        & (lax.broadcasted_iota(jnp.int32, plane_shape, 2) == cell_z)
    )
    weights = jnp.where(hit, source_rate, 0.0).reshape(-1, count)
    columns = (
        lax.broadcasted_iota(jnp.int32, (count, span_x), 1) == local_x[:, None]
    ).astype(jnp.float32)
    source = jnp.dot(
        weights, columns, precision=lax.Precision.HIGHEST, preferred_element_type=jnp.float32
    ).reshape(concentration.shape)
    solid_flag = solid.astype(jnp.int32)
    flow_solid = lax.dynamic_slice_in_dim(solid, row_index * slab_depth, slab_depth, 1)
    rows = lax.axis_size("row")
    flow = [flow_pops[member] for member in range(19)]
    scalars = concentration
    halos = None
    for time_step in range(STEPS):
        flow, motion = flow_collide(flow, flow_solid)
        rising = edge_planes(flow, flow_vectors, 2, 1, 1)
        sinking = edge_planes(flow, flow_vectors, 2, 1, -1)
        target = lax.broadcasted_iota(jnp.int32, (rows, 1), 0)
        planes = jnp.where(
            target == row_index + 1,
            rising.reshape(1, -1),
            jnp.where(target == row_index - 1, sinking.reshape(1, -1), 0.0),
        )
        spread = jnp.broadcast_to(motion.reshape(1, -1), (rows, motion.size))
        everyone = lax.all_to_all(
            jnp.concatenate([spread, planes], 1), "row", split_axis=0, concat_axis=0, tiled=True
        )
        column = in_order(everyone[:, : motion.size].reshape((rows,) + motion.shape), 2)
        below = lax.dynamic_index_in_dim(everyone, jnp.maximum(row_index - 1, 0), 0, False)
        above = lax.dynamic_index_in_dim(everyone, jnp.minimum(row_index + 1, rows - 1), 0, False)
        from_below = jnp.where(row_index == 0, 0.0, below[motion.size :]).reshape(rising.shape)
        from_above = jnp.where(row_index == rows - 1, 0.0, above[motion.size :]).reshape(
            sinking.shape
        )
        mode = "first" if time_step == 0 else "middle"
        scalars, sides = scalar_stage(mode, scalars, halos, column, solid_flag, source)
        flow = displace(flow, flow_vectors, 2, 1, from_below, from_above)
        leaving_y = {1: scalars[3, :, span_y - 1], -1: scalars[4, :, 0]}
        flow, arrived_y = packed_section(flow, leaving_y, 1, 0, send_spanwise, keep_spanwise, True)
        leaving_x = {1: sides[:, :, 0], -1: sides[:, :, 1]}
        if lax.axis_size("gx") == 2:
            flow, arrived_x = swapped_section(flow, leaving_x, send_streamwise, inflow_fill)
        else:
            flow, arrived_x = packed_section(
                flow, leaving_x, 0, 2, send_streamwise, inflow_fill, False
            )
        sides = jnp.stack([arrived_x[1], arrived_x[-1]], 2)
        sides = jnp.pad(sides, ((0, 0), (0, 0), (0, 6), (0, span_x - depth)))
        halos = (sides, arrived_y[1], arrived_y[-1])
    amount = scalar_stage("final", scalars, halos, None, None, None)
    stacked = jnp.stack(flow)
    return (stacked, amount)


def solution(mesh):
    in_specs = (
        P(None, "gy", "row", "gx"),
        P("row", "gy", None, "gx"),
        P("gy", None, "gx"),
        P(),
        P(),
        P(),
    )
    out_specs = (P(None, "gy", "row", "gx"), P("row", "gy", None, "gx"))
    return jax.shard_map(
        on_device, mesh=mesh, in_specs=in_specs, out_specs=out_specs, check_vma=False
    )
```
